32 devices in a mesh: gx: 8 (over z, x), gy: 4 (over y, core).
Axes of the slice: x: 2, y: 2, z: 4, core: 2. Of those that a mesh axis runs over, the one named last changes fastest.
Arguments:
- layer_slowness: float32 [8], replicated, may hold values from 0.5 to 2
- layer_rigidity: float32 [8], replicated, may hold values from 0.5 to 4
- layer_damping: float32 [8], replicated, may hold values from 0.02 to 0.2
- layer_of_level: int32 [32], replicated, may hold values from 0 to 7
- slot_offset: int32 [8192], replicated, may hold values from 0 to 2047
- slot_level: int32 [8192], replicated, may hold values from 0 to 31
- slot_target: int32 [8192], P(('gx', 'gy')), may hold values from 0 to 786431
- live_count: int32 [32], P(('gx', 'gy')), may hold values from 1 to 256, 4096 in all
- moduli: float32 [2, 256, 128, 256], P(None, 'gx', 'gy'), may hold values from 0.02 to 0.06
- field_old: float32 [3, 256, 128, 256], P(None, 'gx', 'gy'), may hold values from -0.3 to 0.3
- field_now: float32 [3, 256, 128, 256], P(None, 'gx', 'gy'), may hold values from -0.3 to 0.3
Outputs:
- final_field: float32 [3, 256, 128, 256], P(None, 'gx', 'gy')
- prior_field: float32 [3, 256, 128, 256], P(None, 'gx', 'gy')
The draws below stay inside these ranges and needn't reach their ends.
Inputs may be any that keep to these rules, and one draw needn't show every extreme that they name: live_count sums to 8192 // 2 over all owners, and some owner uses all 256 slots.
All inputs are finite; a program needn't handle non-finite values. No bound on the sum of `live_count` on one device may be relied on, other than what follows from the above.
Results may differ from the reference program's by a relative error of at most 0.0036.
Values may be sent and summed in bfloat16 or wider, within the bound.
No kernel may reach another device: no remote copies, remote signals or barrier semaphores. Data moves between devices by JAX's collectives and lax.ppermute only.
A program may use at most 128 MiB of HBM per device.

```python
import math
import jax
import jax.numpy as jnp
import numpy as np
from jax import lax

F = 128
NK = 1024
NR = 2048
ND = 32
NL = 8
STEPS = 4
TSTART = 32
Q_DEV = 256
CX = 32
CY = 32
NZ = 256
SLOTS = 8192
NX = 256
NY = 128
N_GX = 8
N_GY = 4


def plant(drawn, rng, least, high):
    place = [jax.random.randint(jax.random.fold_in(rng, axis), (), 0, length) for axis, length in enumerate(drawn.shape)]
    main_axis = drawn.shape.index(max(drawn.shape))
    beside = place[:main_axis] + [(place[main_axis] + 1) % drawn.shape[main_axis]] + place[main_axis + 1:]
    return drawn.at[tuple(place)].set(least).at[tuple(beside)].set(high)


def steps_of(own_key, extent, shards, least, high):
    level = 1.0
    for position, parts in shards:
        draws = jax.random.uniform(jax.random.fold_in(jax.random.fold_in(own_key, 6), position), (parts,), jnp.float32, least / len(shards), high / len(shards))
        level = level * jnp.repeat(jnp.exp(draws), extent[position] // parts).reshape((-1,) + (1,) * (len(extent) - 1 - position))
    return level


def split_up(count, total, bound, lean):
    portions = [(1 << 20) // math.isqrt(rank ** lean) + 1 for rank in range(2, count + 1)]
    rest, holding = total - bound - (count - 1), [1] * (count - 1)
    while rest > 0:
        free = [i for i in range(count - 1) if holding[i] < bound]
        whole, budget = sum([portions[i] for i in free]), rest
        for i in free:
            extra = min(bound - holding[i], max(1, budget * portions[i] // whole), rest)
            holding[i] = holding[i] + extra
            rest = rest - extra
    return np.array([bound] + holding)


def ragged_sizes(rng, count, total, bound, lean):
    if count == 2:
        one = jax.random.randint(rng, (), max(1, total - bound), min(bound, total - 1) + 1)
        return jnp.stack([one, total - one])
    lengths = jnp.asarray(split_up(count, total, bound, lean), jnp.int32)
    couples = (count - 1) // 2
    source_of, taker = lengths[1:1 + 2 * couples:2], lengths[2:2 + 2 * couples:2]
    room = jnp.minimum(source_of - 1, bound - taker)
    moved = jax.random.randint(jax.random.fold_in(rng, 1), (couples,), 0, 1 << 20) % (room + 1)
    lengths = lengths.at[1:1 + 2 * couples:2].set(source_of - moved).at[2:2 + 2 * couples:2].set(taker + moved)
    return lengths[jax.random.permutation(jax.random.fold_in(rng, 2), count)]


def noise(stream_key, dims, scale, most, split=(), held_as=jnp.bfloat16):
    entries = jax.random.normal(stream_key, dims, jnp.float32) * scale
    if len(split) > 0:
        entries = steps_of(stream_key, dims, split, -0.22, 0.18) * entries
    return jnp.clip(entries, min=-most, max=most).astype(held_as)


def setup_inputs(seed: int = 0) -> dict:
    arg_keys = jax.random.split(jax.random.key(seed), 12)
    layer_slowness = jnp.clip(jnp.exp(jax.random.uniform(arg_keys[0], (NL,), jnp.float32, math.log(0.5), math.log(2.0))), 0.5, 2.0)
    layer_rigidity = jnp.clip(jnp.exp(jax.random.uniform(arg_keys[1], (NL,), jnp.float32, math.log(0.5), math.log(4.0))), 0.5, 4.0)
    layer_damping = jnp.clip(jnp.exp(jax.random.uniform(arg_keys[2], (NL,), jnp.float32, math.log(0.02), math.log(0.2))), 0.02, 0.2)
    layer_of_level = plant(jax.random.randint(arg_keys[3], (ND,), 0, NL), jax.random.fold_in(arg_keys[3], 1), 0, NL - 1).astype(jnp.int32)
    slot_offset = plant(jax.random.randint(arg_keys[4], (SLOTS,), 0, NR), jax.random.fold_in(arg_keys[4], 1), 0, NR - 1).astype(jnp.int32)
    slot_level = plant(jax.random.randint(arg_keys[5], (SLOTS,), 0, ND), jax.random.fold_in(arg_keys[5], 1), 0, ND - 1).astype(jnp.int32)
    slot_target = plant(jax.random.randint(arg_keys[6], (SLOTS,), 0, 3 * CX * CY * NZ), jax.random.fold_in(arg_keys[6], 1), 0, (3 * CX * CY * NZ) - 1).astype(jnp.int32)
    live_count = ragged_sizes(arg_keys[7], N_GX * N_GY, SLOTS // 2, Q_DEV, 2).astype(jnp.int32)
    moduli = jnp.clip(0.02 + 0.04 * jax.random.uniform(arg_keys[8], (2, NX, NY, NZ), jnp.float32) ** steps_of(arg_keys[8], (2, NX, NY, NZ), ((1, 8), (2, 4)), -0.2, 0.2), 0.02, 0.06)
    field_old = noise(arg_keys[9], (3, NX, NY, NZ), 0.05, 0.3, ((1, 8), (2, 4)), jnp.float32)
    field_now = noise(arg_keys[10], (3, NX, NY, NZ), 0.05, 0.3, ((1, 8), (2, 4)), jnp.float32)
    return dict(layer_slowness=layer_slowness, layer_rigidity=layer_rigidity, layer_damping=layer_damping, layer_of_level=layer_of_level, slot_offset=slot_offset, slot_level=slot_level, slot_target=slot_target, live_count=live_count, moduli=moduli, field_old=field_old, field_now=field_now)


step_depth = 0.25

def level_table(values, layer_of_level):
    one_hot = (layer_of_level[:, None] == jnp.arange(values.shape[0], dtype=jnp.int32)[None, :]).astype(jnp.float32)
    return lax.optimization_barrier(jnp.sum(one_hot * values[None, :], axis=1))

def wave_kernel(angular, slowness, rigidity, damping, count_k):
    wavenum = (jnp.arange(count_k, dtype=jnp.float32) + 0.5) * (4.0 / count_k)
    spread = angular[None, :, None] * slowness[:, None, None]
    vertical = jnp.sqrt(wavenum[None, None, :] * wavenum[None, None, :] + spread * spread)
    impedance = rigidity[:, None, None] * vertical
    beneath = jnp.concatenate([impedance[1:], impedance[-1:]], axis=0)
    reflect = (impedance - beneath) / (impedance + beneath)
    fading = jnp.exp(-2.0 * step_depth * vertical * damping[:, None, None])
    two_way = 2.0 * step_depth * vertical
    trip_re = fading * jnp.cos(two_way)
    trip_im = -fading * jnp.sin(two_way)

    def upward(state_in, layer_data):
        refl_re, refl_im = state_in
        coefficient, along_re, along_im = layer_data
        upper_re = coefficient + refl_re
        upper_im = refl_im
        lower_re = 1.0 + coefficient * refl_re
        lower_im = coefficient * refl_im
        magnitude = lower_re * lower_re + lower_im * lower_im
        ratio_re = (upper_re * lower_re + upper_im * lower_im) / magnitude
        ratio_im = (upper_im * lower_re - upper_re * lower_im) / magnitude
        fresh_re = along_re * ratio_re - along_im * ratio_im
        fresh_im = along_re * ratio_im + along_im * ratio_re
        return ((fresh_re, fresh_im), (fresh_re, fresh_im))
    bottom = jnp.zeros(vertical.shape[1:], jnp.float32)
    _, (refl_re, refl_im) = lax.scan(upward, (bottom, bottom), (reflect, trip_re, trip_im), reverse=True)
    travel = step_depth * vertical
    phases = jnp.cumsum(travel, axis=0) - travel
    absorbed = travel * damping[:, None, None]
    losses = jnp.cumsum(absorbed, axis=0) - absorbed
    down_size = jnp.exp(-losses)
    down_re = down_size * jnp.cos(phases)
    down_im = -down_size * jnp.sin(phases)
    weight = 1.0 / math.sqrt(count_k)
    kernel_re = weight * (down_re * (1.0 + refl_re) - down_im * refl_im)
    kernel_im = weight * (down_re * refl_im + down_im * (1.0 + refl_re))
    return jnp.transpose(jnp.stack([kernel_re, kernel_im]), (0, 2, 1, 3))

def offset_basis(count_k, count_r):
    modulus = count_k * count_r // 2
    odd_index = 2 * jnp.arange(count_k, dtype=jnp.int32) + 1
    spots = jnp.arange(count_r, dtype=jnp.int32)
    turns = odd_index[:, None] * spots[None, :] % modulus
    return jnp.cos(turns.astype(jnp.float32) * (2.0 * math.pi / modulus)).astype(jnp.bfloat16)

def time_basis(freq_ids, count_f, count_steps, first_time):
    period = 2 * count_f
    times = first_time + jnp.arange(count_steps, dtype=jnp.int32)
    turns = (freq_ids[None, :] + 1) * times[:, None] % period
    angles = turns.astype(jnp.float32) * (2.0 * math.pi / period)
    weight = 1.0 / math.sqrt(count_f)
    return jnp.stack([weight * jnp.cos(angles), -weight * jnp.sin(angles)], axis=1)

def shifted(grid_block, step_x, step_y, step_z):
    width_x = grid_block.shape[0] - 4
    width_y = grid_block.shape[1] - 4
    width_z = grid_block.shape[2] - 4
    return grid_block[2 + step_x:2 + step_x + width_x, 2 + step_y:2 + step_y + width_y, 2 + step_z:2 + step_z + width_z]

def curvature(grid_block, first_axis):
    summed = None
    for offset, factor in [(-2, -1.0), (-1, 16.0), (0, -30.0), (1, 16.0), (2, -1.0)]:
        moves = tuple((offset if index == first_axis else 0 for index in range(3)))
        contrib = factor * shifted(grid_block, moves[0], moves[1], moves[2])
        summed = contrib if summed is None else summed + contrib
    return summed / 12.0

def mixed(grid_block, first_axis, second_axis):
    summed = None
    for sign_a, sign_b, factor in [(1, 1, 1.0), (1, -1, -1.0), (-1, 1, -1.0), (-1, -1, 1.0)]:
        moves = tuple((sign_a if index == first_axis else sign_b if index == second_axis else 0 for index in range(3)))
        contrib = factor * shifted(grid_block, moves[0], moves[1], moves[2])
        summed = contrib if summed is None else summed + contrib
    return summed / 4.0

def elastic(padded, moduli):
    first_lame = moduli[0]
    shear_mod = moduli[1]
    stiffness = first_lame + 2.0 * shear_mod
    coupling = first_lame + shear_mod
    result = []
    for component in range(3):
        update = stiffness * curvature(padded[component], component)
        for partner in range(3):
            if partner != component:
                update = update + shear_mod * curvature(padded[component], partner)
                update = update + coupling * mixed(padded[partner], component, partner)
        result.append(update)
    return jnp.stack(result)

def reference(layer_slowness, layer_rigidity, layer_damping, layer_of_level, slot_offset, slot_level, slot_target, live_count, moduli, field_old, field_now):
    slowness = level_table(layer_slowness, layer_of_level)
    rigidity = level_table(layer_rigidity, layer_of_level)
    damping = level_table(layer_damping, layer_of_level)
    freq_all = jnp.arange(F, dtype=jnp.int32)
    angular = (freq_all + 1).astype(jnp.float32) * (4.0 / F)
    kernel = wave_kernel(angular, slowness, rigidity, damping, NK).astype(jnp.bfloat16)
    cosines = offset_basis(NK, NR).astype(jnp.float32)
    waveforms = time_basis(freq_all, F, STEPS, TSTART)
    lookup = slot_level * NR + slot_offset

    def one_frequency(summed, inputs):
        kernel_f, wave_f = inputs
        spectrum = jnp.dot(kernel_f.astype(jnp.float32).reshape(2 * ND, NK), cosines, precision=lax.Precision.HIGHEST)
        picked = jnp.take(spectrum.reshape(2, ND * NR), lookup, axis=1).astype(jnp.bfloat16)
        picked = lax.optimization_barrier(picked).astype(jnp.float32)
        return (summed + jnp.dot(wave_f, picked, precision=lax.Precision.HIGHEST), None)
    traces, _ = lax.scan(one_frequency, jnp.zeros((STEPS, SLOTS), jnp.float32), (jnp.transpose(kernel, (1, 0, 2, 3)), jnp.transpose(waveforms, (2, 0, 1))))
    slot_ids = jnp.arange(SLOTS, dtype=jnp.int32)
    owner = slot_ids // Q_DEV
    within = slot_ids % Q_DEV
    occupied = (within < live_count[owner]).astype(jnp.float32)
    cells = CX * CY * NZ
    component = slot_target // cells
    local_cell = slot_target % cells
    cell_x = local_cell // (CY * NZ)
    cell_y = local_cell // NZ % CY
    cell_z = local_cell % NZ
    grid_x = owner // N_GY * CX + cell_x
    grid_y = owner % N_GY * CY + cell_y
    target = ((component * NX + grid_x) * NY + grid_y) * NZ + cell_z
    previous, current = (field_old, field_now)
    for instant in range(STEPS):
        padded = jnp.pad(current, ((0, 0), (2, 2), (2, 2), (2, 2)))
        advanced = 2.0 * current - previous + elastic(padded, moduli)
        advanced = advanced.reshape(-1).at[target].add(traces[instant] * occupied).reshape(current.shape)
        previous, current = (current, advanced)
    return (current, previous)
```

```python
import math

import jax
import jax.numpy as jnp
from jax import lax
from jax.sharding import PartitionSpec as P

F = 128
NK = 1024
NR = 2048
ND = 32
STEPS = 4
TSTART = 32


step_depth = 0.25


def padded_2(block, sides, width):
    for axis, dim in sides:
        count = lax.axis_size(axis)
        forward = [(i, i + 1) for i in range(count - 1)]
        backward = [(target, source) for source, target in forward]
        low = lax.ppermute(
            lax.slice_in_dim(block, block.shape[dim] - width, None, axis=dim), axis, forward
        )
        high = lax.ppermute(lax.slice_in_dim(block, 0, width, axis=dim), axis, backward)
        block = jnp.concatenate([low, block, high], axis=dim)
    return block


def level_table(values, layer_of_level):
    one_hot = (
        layer_of_level[:, None] == jnp.arange(values.shape[0], dtype=jnp.int32)[None, :]
    ).astype(jnp.float32)
    return jnp.sum(one_hot * values[None, :], axis=1)


def wave_kernel(angular, slowness, rigidity, damping, count_k):
    wavenum = (jnp.arange(count_k, dtype=jnp.float32) + 0.5) * (4.0 / count_k)
    spread = angular[None, :, None] * slowness[:, None, None]
    vertical = jnp.sqrt(wavenum[None, None, :] * wavenum[None, None, :] + spread * spread)
    impedance = rigidity[:, None, None] * vertical
    beneath = jnp.concatenate([impedance[1:], impedance[-1:]], axis=0)
    reflect = (impedance - beneath) / (impedance + beneath)
    fading = jnp.exp(-2.0 * step_depth * vertical * damping[:, None, None])
    two_way = 2.0 * step_depth * vertical
    trip_re = fading * jnp.cos(two_way)
    trip_im = -fading * jnp.sin(two_way)

    def upward(state_in, layer_data):
        refl_re, refl_im = state_in
        coefficient, along_re, along_im = layer_data
        upper_re = coefficient + refl_re
        lower_re = 1.0 + coefficient * refl_re
        lower_im = coefficient * refl_im
        magnitude = lower_re * lower_re + lower_im * lower_im
        ratio_re = (upper_re * lower_re + refl_im * lower_im) / magnitude
        ratio_im = (refl_im * lower_re - upper_re * lower_im) / magnitude
        fresh_re = along_re * ratio_re - along_im * ratio_im
        fresh_im = along_re * ratio_im + along_im * ratio_re
        return ((fresh_re, fresh_im), (fresh_re, fresh_im))

    bottom = jnp.zeros(vertical.shape[1:], jnp.float32)
    _, (refl_re, refl_im) = lax.scan(
        upward, (bottom, bottom), (reflect, trip_re, trip_im), reverse=True
    )
    travel = step_depth * vertical
    phases = jnp.cumsum(travel, axis=0) - travel
    absorbed = travel * damping[:, None, None]
    losses = jnp.cumsum(absorbed, axis=0) - absorbed
    down_size = jnp.exp(-losses)
    down_re = down_size * jnp.cos(phases)
    down_im = -down_size * jnp.sin(phases)
    weight = 1.0 / math.sqrt(count_k)
    kernel_re = weight * (down_re * (1.0 + refl_re) - down_im * refl_im)
    kernel_im = weight * (down_re * refl_im + down_im * (1.0 + refl_re))
    return jnp.transpose(jnp.stack([kernel_re, kernel_im]), (0, 2, 1, 3))


def offset_basis(count_k, count_r):
    modulus = count_k * count_r // 2
    low_count = 64
    odd_index = 2 * jnp.arange(count_k, dtype=jnp.int32) + 1
    high = jnp.arange(count_r // low_count, dtype=jnp.int32) * low_count
    low = jnp.arange(low_count, dtype=jnp.int32)
    scale = 2.0 * math.pi / modulus
    high_angle = (odd_index[:, None] * high[None, :] % modulus).astype(jnp.float32) * scale
    low_angle = (odd_index[:, None] * low[None, :] % modulus).astype(jnp.float32) * scale
    cos_h, sin_h = jnp.cos(high_angle), jnp.sin(high_angle)
    cos_l, sin_l = jnp.cos(low_angle), jnp.sin(low_angle)
    basis = cos_h[:, :, None] * cos_l[:, None, :] - sin_h[:, :, None] * sin_l[:, None, :]
    basis = basis.reshape(count_k, count_r).astype(jnp.bfloat16)
    return lax.optimization_barrier(basis)


def time_basis(freq_ids, count_f, count_steps, first_time):
    period = 2 * count_f
    times = first_time + jnp.arange(count_steps, dtype=jnp.int32)
    turns = (freq_ids[None, :] + 1) * times[:, None] % period
    angles = turns.astype(jnp.float32) * (2.0 * math.pi / period)
    weight = 1.0 / math.sqrt(count_f)
    return jnp.stack([weight * jnp.cos(angles), -weight * jnp.sin(angles)], axis=1)


def shifted(grid_block, step_x, step_y, step_z):
    width_x = grid_block.shape[0] - 4
    width_y = grid_block.shape[1] - 4
    width_z = grid_block.shape[2] - 4
    return grid_block[
        2 + step_x : 2 + step_x + width_x,
        2 + step_y : 2 + step_y + width_y,
        2 + step_z : 2 + step_z + width_z,
    ]


def curvature(grid_block, first_axis):
    summed = None
    for offset, factor in [(-2, -1.0), (-1, 16.0), (0, -30.0), (1, 16.0), (2, -1.0)]:
        moves = tuple((offset if index == first_axis else 0 for index in range(3)))
        contrib = factor * shifted(grid_block, moves[0], moves[1], moves[2])
        summed = contrib if summed is None else summed + contrib
    return summed / 12.0


def mixed(grid_block, first_axis, second_axis):
    summed = None
    for sign_a, sign_b, factor in [(1, 1, 1.0), (1, -1, -1.0), (-1, 1, -1.0), (-1, -1, 1.0)]:
        moves = tuple(
            (
                sign_a if index == first_axis else sign_b if index == second_axis else 0
                for index in range(3)
            )
        )
        contrib = factor * shifted(grid_block, moves[0], moves[1], moves[2])
        summed = contrib if summed is None else summed + contrib
    return summed / 4.0


def elastic(padded, moduli):
    first_lame = moduli[0]
    shear_mod = moduli[1]
    stiffness = first_lame + 2.0 * shear_mod
    coupling = first_lame + shear_mod
    result = []
    for component in range(3):
        update = stiffness * curvature(padded[component], component)
        for partner in range(3):
            if partner != component:
                update = update + shear_mod * curvature(padded[component], partner)
                update = update + coupling * mixed(padded[partner], component, partner)
        result.append(update)
    return jnp.stack(result)


def shards(
    layer_slowness,
    layer_rigidity,
    layer_damping,
    layer_of_level,
    slot_offset,
    slot_level,
    slot_target,
    live_count,
    moduli,
    field_old,
    field_now,
):
    size_gx = lax.axis_size("gx")
    size_gy = lax.axis_size("gy")
    groups = size_gx * size_gy
    per_device = F // groups
    device = lax.axis_index("gx") * size_gy + lax.axis_index("gy")
    freq_ids = device * per_device + jnp.arange(per_device, dtype=jnp.int32)
    angular = (freq_ids + 1).astype(jnp.float32) * (4.0 / F)
    slowness = level_table(layer_slowness, layer_of_level)
    rigidity = level_table(layer_rigidity, layer_of_level)
    damping = level_table(layer_damping, layer_of_level)
    kernel = wave_kernel(angular, slowness, rigidity, damping, NK).astype(jnp.bfloat16)
    cosines = offset_basis(NK, NR)
    spectrum_table = jnp.dot(
        kernel.reshape(2 * per_device * ND, NK), cosines, preferred_element_type=jnp.float32
    )
    table_rounded = spectrum_table.astype(jnp.bfloat16)
    all_slots = slot_offset.shape[0]
    width = math.gcd(all_slots, 4096)
    count_blocks = all_slots // width
    offset_blocks = slot_offset.reshape(count_blocks, width)
    level_blocks = slot_level.reshape(count_blocks, width)

    def select_block(pair):
        offsets, levels = pair
        offset_hot = (jnp.arange(NR, dtype=jnp.int32)[:, None] == offsets[None, :]).astype(
            jnp.bfloat16
        )
        rows = jnp.dot(table_rounded, offset_hot, preferred_element_type=jnp.float32).reshape(
            2, per_device, ND, width
        )
        level_hot = (jnp.arange(ND, dtype=jnp.int32)[:, None] == levels[None, :]).astype(
            jnp.float32
        )
        return jnp.sum(rows * level_hot[None, None, :, :], axis=2)

    selected = lax.map(select_block, (offset_blocks, level_blocks))
    spectra = (
        jnp.transpose(selected, (1, 2, 0, 3)).reshape(2, per_device, all_slots).astype(jnp.bfloat16)
    )
    slots_dev = slot_target.shape[0]
    occupied = (jnp.arange(slots_dev, dtype=jnp.int32) < live_count[0]).astype(jnp.float32)
    parcel = spectra.reshape(2, per_device, groups, slots_dev)
    arrived = lax.all_to_all(parcel, ("gx", "gy"), split_axis=2, concat_axis=1, tiled=True)
    freq_order = jnp.arange(F, dtype=jnp.int32)
    waveforms = time_basis(freq_order, F, STEPS, TSTART).reshape(STEPS, 2 * F)
    traces = jnp.dot(
        waveforms,
        arrived.reshape(2 * F, slots_dev).astype(jnp.float32),
        precision=lax.Precision.HIGHEST,
    )
    block_x = field_now.shape[1]
    block_y = field_now.shape[2]
    depth = field_now.shape[3]
    columns = slot_target // depth
    layer_z = slot_target % depth
    weighted = traces * occupied[None, :]
    column_hot = (
        jnp.arange(3 * block_x * block_y, dtype=jnp.int32)[:, None] == columns[None, :]
    ).astype(jnp.float32)
    depth_hot = (layer_z[:, None] == jnp.arange(depth, dtype=jnp.int32)[None, :]).astype(
        jnp.float32
    )
    spread_traces = weighted[:, :, None] * depth_hot[None, :, :]
    sources = jnp.einsum("ag,ngz->naz", column_hot, spread_traces, precision=lax.Precision.HIGHEST)
    sources = sources.reshape(STEPS, 3, block_x, block_y, depth)
    previous, current = (field_old, field_now)
    for instant in range(STEPS):
        padded = padded_2(current, (("gx", 1), ("gy", 2)), 2)
        padded = jnp.pad(padded, ((0, 0), (0, 0), (0, 0), (2, 2)))
        advanced = 2.0 * current - previous + elastic(padded, moduli)
        advanced = advanced + sources[instant]
        previous, current = (current, advanced)
    return (current, previous)


def solution(mesh):
    in_specs = (
        P(),
        P(),
        P(),
        P(),
        P(),
        P(),
        P(("gx", "gy")),
        P(("gx", "gy")),
        P(None, "gx", "gy", None),
        P(None, "gx", "gy", None),
        P(None, "gx", "gy", None),
    )
    out_specs = (P(None, "gx", "gy", None), P(None, "gx", "gy", None))
    return jax.shard_map(shards, mesh=mesh, in_specs=in_specs, out_specs=out_specs, check_vma=False)
```

```python
import math

import jax
import jax.numpy as jnp
from jax import lax
from jax.sharding import PartitionSpec as P
from jax.experimental import pallas as pl
from jax.experimental.pallas import tpu as pltpu
import functools

F = 128
NK = 1024
NR = 2048
ND = 32
STEPS = 4
TSTART = 32


step_depth = 0.25


def padded_2(block, sides, width):
    for axis, dim in sides:
        count = lax.axis_size(axis)
        forward = [(i, i + 1) for i in range(count - 1)]
        backward = [(target, source) for source, target in forward]
        low = lax.ppermute(
            lax.slice_in_dim(block, block.shape[dim] - width, None, axis=dim), axis, forward
        )
        high = lax.ppermute(lax.slice_in_dim(block, 0, width, axis=dim), axis, backward)
        block = jnp.concatenate([low, block, high], axis=dim)
    return block


TAPS = ((-2, -1.0), (-1, 16.0), (1, 16.0), (2, -1.0))


def step_kernel(up_ref, prev_ref, mod_ref, src_ref, out_ref, *, bx):
    i = pl.program_id(0)
    depth = out_ref.shape[3]
    lane = lax.broadcasted_iota(jnp.int32, (8, depth), 1)
    masks = {dz: (lane + dz >= 0) & (lane + dz < depth) for dz in (-2, -1, 1, 2)}

    def zs(v, dz):
        if dz == 0:
            return v
        return jnp.where(masks[dz], pltpu.roll(v, (-dz) % depth, 1), 0.0)

    def plane(p, carry):
        xp = i * bx + p + 2
        for g in range(out_ref.shape[2] // 8):
            def load(c, dx, dy):
                return up_ref[c, xp + dx, pl.ds(8 * g + 2 + dy, 8), :]

            lam = mod_ref[0, p, pl.ds(8 * g, 8), :]
            mu = mod_ref[1, p, pl.ds(8 * g, 8), :]
            stiff = lam + 2.0 * mu
            coup = lam + mu
            centers = [load(c, 0, 0) for c in range(3)]

            def curv(c, axis):
                center = centers[c]
                acc = -30.0 * center
                for off, w in TAPS:
                    if axis == 0:
                        t = load(c, off, 0)
                    elif axis == 1:
                        t = load(c, 0, off)
                    else:
                        t = zs(center, off)
                    acc = acc + w * t
                return acc / 12.0

            def mixed(p_c, a, b):
                acc = None
                for sa in (1, -1):
                    for sb in (1, -1):
                        d = [0, 0, 0]
                        d[a] = sa
                        d[b] = sb
                        t = zs(load(p_c, d[0], d[1]), d[2])
                        t = t if sa * sb > 0 else -t
                        acc = t if acc is None else acc + t
                return acc / 4.0

            for c in range(3):
                upd = stiff * curv(c, c)
                for e in range(3):
                    if e != c:
                        upd = upd + mu * curv(c, e)
                        upd = upd + coup * mixed(e, c, e)
                prev = prev_ref[c, p, pl.ds(8 * g, 8), :]
                src = src_ref[c, p, pl.ds(8 * g, 8), :]
                out_ref[c, p, pl.ds(8 * g, 8), :] = (2.0 * centers[c] - prev + upd) + src
        return carry

    lax.fori_loop(0, bx, plane, 0)


def elastic_step(upad, prev, moduli, sources, instant, bx=8):
    _, px, py, depth = upad.shape
    nx, ny = px - 4, py - 4
    kernel = functools.partial(step_kernel, bx=bx)
    block = lambda i: (0, i, 0, 0)
    return pl.pallas_call(
        kernel,
        grid=(nx // bx,),
        in_specs=[
            pl.BlockSpec((3, px, py, depth), lambda i: (0, 0, 0, 0)),
            pl.BlockSpec((3, bx, ny, depth), block),
            pl.BlockSpec((2, bx, ny, depth), block),
            pl.BlockSpec((None, 3, bx, ny, depth), lambda i: (instant, 0, i, 0, 0)),
        ],
        out_specs=pl.BlockSpec((3, bx, ny, depth), block),
        out_shape=jax.ShapeDtypeStruct((3, nx, ny, depth), jnp.float32),
    )(upad, prev, moduli, sources)


def halo_padded(block, width):
    size_x = lax.axis_size("gx")
    size_y = lax.axis_size("gy")
    nx, ny = block.shape[1], block.shape[2]

    def shift(piece, step_x, step_y):
        pairs = []
        for ix in range(size_x):
            for iy in range(size_y):
                jx, jy = ix + step_x, iy + step_y
                if 0 <= jx < size_x and 0 <= jy < size_y:
                    pairs.append((ix * size_y + iy, jx * size_y + jy))
        return lax.ppermute(piece, ("gx", "gy"), pairs)

    lo_x = slice(0, width)
    hi_x = slice(nx - width, nx)
    lo_y = slice(0, width)
    hi_y = slice(ny - width, ny)
    whole = slice(None)
    part = lambda sx, sy: block[:, sx, sy, :]
    left = shift(part(hi_x, whole), 1, 0)
    right = shift(part(lo_x, whole), -1, 0)
    down = shift(part(whole, hi_y), 0, 1)
    up = shift(part(whole, lo_y), 0, -1)
    ll = shift(part(hi_x, hi_y), 1, 1)
    lh = shift(part(hi_x, lo_y), 1, -1)
    hl = shift(part(lo_x, hi_y), -1, 1)
    hh = shift(part(lo_x, lo_y), -1, -1)
    low_row = jnp.concatenate([ll, left, lh], axis=2)
    mid_row = jnp.concatenate([down, block, up], axis=2)
    high_row = jnp.concatenate([hl, right, hh], axis=2)
    return jnp.concatenate([low_row, mid_row, high_row], axis=1)


def level_table(values, layer_of_level):
    one_hot = (
        layer_of_level[:, None] == jnp.arange(values.shape[0], dtype=jnp.int32)[None, :]
    ).astype(jnp.float32)
    return jnp.sum(one_hot * values[None, :], axis=1)


def wave_kernel(angular, slowness, rigidity, damping, count_k):
    wavenum = (jnp.arange(count_k, dtype=jnp.float32) + 0.5) * (4.0 / count_k)
    spread = angular[None, :, None] * slowness[:, None, None]
    vertical = jnp.sqrt(wavenum[None, None, :] * wavenum[None, None, :] + spread * spread)
    impedance = rigidity[:, None, None] * vertical
    beneath = jnp.concatenate([impedance[1:], impedance[-1:]], axis=0)
    reflect = (impedance - beneath) / (impedance + beneath)
    fading = jnp.exp(-2.0 * step_depth * vertical * damping[:, None, None])
    two_way = 2.0 * step_depth * vertical
    trip_re = fading * jnp.cos(two_way)
    trip_im = -fading * jnp.sin(two_way)

    def upward(state_in, layer_data):
        refl_re, refl_im = state_in
        coefficient, along_re, along_im = layer_data
        upper_re = coefficient + refl_re
        lower_re = 1.0 + coefficient * refl_re
        lower_im = coefficient * refl_im
        magnitude = lower_re * lower_re + lower_im * lower_im
        ratio_re = (upper_re * lower_re + refl_im * lower_im) / magnitude
        ratio_im = (refl_im * lower_re - upper_re * lower_im) / magnitude
        fresh_re = along_re * ratio_re - along_im * ratio_im
        fresh_im = along_re * ratio_im + along_im * ratio_re
        return ((fresh_re, fresh_im), (fresh_re, fresh_im))

    bottom = jnp.zeros(vertical.shape[1:], jnp.float32)
    _, (refl_re, refl_im) = lax.scan(
        upward, (bottom, bottom), (reflect, trip_re, trip_im), reverse=True
    )
    travel = step_depth * vertical
    phases = jnp.cumsum(travel, axis=0) - travel
    absorbed = travel * damping[:, None, None]
    losses = jnp.cumsum(absorbed, axis=0) - absorbed
    down_size = jnp.exp(-losses)
    down_re = down_size * jnp.cos(phases)
    down_im = -down_size * jnp.sin(phases)
    weight = 1.0 / math.sqrt(count_k)
    kernel_re = weight * (down_re * (1.0 + refl_re) - down_im * refl_im)
    kernel_im = weight * (down_re * refl_im + down_im * (1.0 + refl_re))
    return jnp.transpose(jnp.stack([kernel_re, kernel_im]), (0, 2, 1, 3))


def offset_basis(count_k, count_r):
    modulus = count_k * count_r // 2
    low_count = 64
    odd_index = 2 * jnp.arange(count_k, dtype=jnp.int32) + 1
    high = jnp.arange(count_r // low_count, dtype=jnp.int32) * low_count
    low = jnp.arange(low_count, dtype=jnp.int32)
    scale = 2.0 * math.pi / modulus
    high_angle = (odd_index[:, None] * high[None, :] % modulus).astype(jnp.float32) * scale
    low_angle = (odd_index[:, None] * low[None, :] % modulus).astype(jnp.float32) * scale
    cos_h, sin_h = jnp.cos(high_angle), jnp.sin(high_angle)
    cos_l, sin_l = jnp.cos(low_angle), jnp.sin(low_angle)
    basis = cos_h[:, :, None] * cos_l[:, None, :] - sin_h[:, :, None] * sin_l[:, None, :]
    basis = basis.reshape(count_k, count_r).astype(jnp.bfloat16)
    return lax.optimization_barrier(basis)


def time_basis(freq_ids, count_f, count_steps, first_time):
    period = 2 * count_f
    times = first_time + jnp.arange(count_steps, dtype=jnp.int32)
    turns = (freq_ids[None, :] + 1) * times[:, None] % period
    angles = turns.astype(jnp.float32) * (2.0 * math.pi / period)
    weight = 1.0 / math.sqrt(count_f)
    return jnp.stack([weight * jnp.cos(angles), -weight * jnp.sin(angles)], axis=1)


def shifted(grid_block, step_x, step_y, step_z):
    width_x = grid_block.shape[0] - 4
    width_y = grid_block.shape[1] - 4
    width_z = grid_block.shape[2] - 4
    return grid_block[
        2 + step_x : 2 + step_x + width_x,
        2 + step_y : 2 + step_y + width_y,
        2 + step_z : 2 + step_z + width_z,
    ]


def curvature(grid_block, first_axis):
    summed = None
    for offset, factor in [(-2, -1.0), (-1, 16.0), (0, -30.0), (1, 16.0), (2, -1.0)]:
        moves = tuple((offset if index == first_axis else 0 for index in range(3)))
        contrib = factor * shifted(grid_block, moves[0], moves[1], moves[2])
        summed = contrib if summed is None else summed + contrib
    return summed / 12.0


def mixed(grid_block, first_axis, second_axis):
    summed = None
    for sign_a, sign_b, factor in [(1, 1, 1.0), (1, -1, -1.0), (-1, 1, -1.0), (-1, -1, 1.0)]:
        moves = tuple(
            (
                sign_a if index == first_axis else sign_b if index == second_axis else 0
                for index in range(3)
            )
        )
        contrib = factor * shifted(grid_block, moves[0], moves[1], moves[2])
        summed = contrib if summed is None else summed + contrib
    return summed / 4.0


def elastic(padded, moduli):
    first_lame = moduli[0]
    shear_mod = moduli[1]
    stiffness = first_lame + 2.0 * shear_mod
    coupling = first_lame + shear_mod
    result = []
    for component in range(3):
        update = stiffness * curvature(padded[component], component)
        for partner in range(3):
            if partner != component:
                update = update + shear_mod * curvature(padded[component], partner)
                update = update + coupling * mixed(padded[partner], component, partner)
        result.append(update)
    return jnp.stack(result)


def shards(
    layer_slowness,
    layer_rigidity,
    layer_damping,
    layer_of_level,
    slot_offset,
    slot_level,
    slot_target,
    live_count,
    moduli,
    field_old,
    field_now,
):
    size_gx = lax.axis_size("gx")
    size_gy = lax.axis_size("gy")
    groups = size_gx * size_gy
    per_device = F // groups
    device = lax.axis_index("gx") * size_gy + lax.axis_index("gy")
    freq_ids = device * per_device + jnp.arange(per_device, dtype=jnp.int32)
    angular = (freq_ids + 1).astype(jnp.float32) * (4.0 / F)
    slowness = level_table(layer_slowness, layer_of_level)
    rigidity = level_table(layer_rigidity, layer_of_level)
    damping = level_table(layer_damping, layer_of_level)
    kernel = wave_kernel(angular, slowness, rigidity, damping, NK).astype(jnp.bfloat16)
    cosines = offset_basis(NK, NR)
    spectrum_table = jnp.dot(
        kernel.reshape(2 * per_device * ND, NK), cosines, preferred_element_type=jnp.float32
    )
    table_rounded = spectrum_table.astype(jnp.bfloat16)
    all_slots = slot_offset.shape[0]
    width = math.gcd(all_slots, 4096)
    count_blocks = all_slots // width
    offset_blocks = slot_offset.reshape(count_blocks, width)
    level_blocks = slot_level.reshape(count_blocks, width)

    def select_block(pair):
        offsets, levels = pair
        offset_hot = (jnp.arange(NR, dtype=jnp.int32)[:, None] == offsets[None, :]).astype(
            jnp.bfloat16
        )
        rows = jnp.dot(table_rounded, offset_hot, preferred_element_type=jnp.float32).reshape(
            2, per_device, ND, width
        )
        level_hot = (jnp.arange(ND, dtype=jnp.int32)[:, None] == levels[None, :]).astype(
            jnp.float32
        )
        return jnp.sum(rows * level_hot[None, None, :, :], axis=2)

    selected = lax.map(select_block, (offset_blocks, level_blocks))
    spectra = (
        jnp.transpose(selected, (1, 2, 0, 3)).reshape(2, per_device, all_slots).astype(jnp.bfloat16)
    )
    slots_dev = slot_target.shape[0]
    occupied = (jnp.arange(slots_dev, dtype=jnp.int32) < live_count[0]).astype(jnp.float32)
    parcel = spectra.reshape(2, per_device, groups, slots_dev)
    arrived = lax.all_to_all(parcel, ("gx", "gy"), split_axis=2, concat_axis=1, tiled=True)
    freq_order = jnp.arange(F, dtype=jnp.int32)
    waveforms = time_basis(freq_order, F, STEPS, TSTART).reshape(STEPS, 2 * F)
    traces = jnp.dot(
        waveforms,
        arrived.reshape(2 * F, slots_dev).astype(jnp.float32),
        precision=lax.Precision.HIGHEST,
    )
    block_x = field_now.shape[1]
    block_y = field_now.shape[2]
    depth = field_now.shape[3]
    columns = slot_target // depth
    layer_z = slot_target % depth
    weighted = traces * occupied[None, :]
    column_hot = (
        jnp.arange(3 * block_x * block_y, dtype=jnp.int32)[:, None] == columns[None, :]
    ).astype(jnp.float32)
    depth_hot = (layer_z[:, None] == jnp.arange(depth, dtype=jnp.int32)[None, :]).astype(
        jnp.float32
    )
    spread_traces = weighted[:, :, None] * depth_hot[None, :, :]
    sources = jnp.einsum("ag,ngz->naz", column_hot, spread_traces, precision=lax.Precision.HIGHEST)
    sources = sources.reshape(STEPS, 3, block_x, block_y, depth)
    previous, current = (field_old, field_now)
    for instant in range(STEPS):
        padded = halo_padded(current, 2)
        advanced = elastic_step(padded, previous, moduli, sources, instant)
        previous, current = (current, advanced)
    return (current, previous)


def solution(mesh):
    in_specs = (
        P(),
        P(),
        P(),
        P(),
        P(),
        P(),
        P(("gx", "gy")),
        P(("gx", "gy")),
        P(None, "gx", "gy", None),
        P(None, "gx", "gy", None),
        P(None, "gx", "gy", None),
    )
    out_specs = (P(None, "gx", "gy", None), P(None, "gx", "gy", None))
    return jax.shard_map(shards, mesh=mesh, in_specs=in_specs, out_specs=out_specs, check_vma=False)
```

```python
import math

import jax
import jax.numpy as jnp
from jax import lax
from jax.sharding import PartitionSpec as P
from jax.experimental import pallas as pl
from jax.experimental.pallas import tpu as pltpu
import functools

F = 128
NK = 1024
NR = 2048
ND = 32
STEPS = 4
TSTART = 32


step_depth = 0.25


def padded_2(block, sides, width):
    for axis, dim in sides:
        count = lax.axis_size(axis)
        forward = [(i, i + 1) for i in range(count - 1)]
        backward = [(target, source) for source, target in forward]
        low = lax.ppermute(
            lax.slice_in_dim(block, block.shape[dim] - width, None, axis=dim), axis, forward
        )
        high = lax.ppermute(lax.slice_in_dim(block, 0, width, axis=dim), axis, backward)
        block = jnp.concatenate([low, block, high], axis=dim)
    return block


TAPS = ((-2, -1.0), (-1, 16.0), (1, 16.0), (2, -1.0))


def step_kernel(up_ref, prev_ref, mod_ref, src_ref, out_ref, *, bx):
    i = pl.program_id(0)
    depth = out_ref.shape[3]
    lane = lax.broadcasted_iota(jnp.int32, (8, depth), 1)
    masks = {dz: (lane + dz >= 0) & (lane + dz < depth) for dz in (-2, -1, 1, 2)}

    def zs(v, dz):
        if dz == 0:
            return v
        return jnp.where(masks[dz], pltpu.roll(v, (-dz) % depth, 1), 0.0)

    def plane(p, carry):
        xp = i * bx + p + 2
        for g in range(out_ref.shape[2] // 8):
            def load(c, dx, dy):
                return up_ref[c, xp + dx, pl.ds(8 * g + 2 + dy, 8), :]

            lam = mod_ref[0, p, pl.ds(8 * g, 8), :]
            mu = mod_ref[1, p, pl.ds(8 * g, 8), :]
            stiff = lam + 2.0 * mu
            coup = lam + mu
            centers = [load(c, 0, 0) for c in range(3)]

            def curv(c, axis):
                center = centers[c]
                acc = -30.0 * center
                for off, w in TAPS:
                    if axis == 0:
                        t = load(c, off, 0)
                    elif axis == 1:
                        t = load(c, 0, off)
                    else:
                        t = zs(center, off)
                    acc = acc + w * t
                return acc / 12.0

            def mixed(p_c, a, b):
                acc = None
                for sa in (1, -1):
                    for sb in (1, -1):
                        d = [0, 0, 0]
                        d[a] = sa
                        d[b] = sb
                        t = zs(load(p_c, d[0], d[1]), d[2])
                        t = t if sa * sb > 0 else -t
                        acc = t if acc is None else acc + t
                return acc / 4.0

            for c in range(3):
                upd = stiff * curv(c, c)
                for e in range(3):
                    if e != c:
                        upd = upd + mu * curv(c, e)
                        upd = upd + coup * mixed(e, c, e)
                prev = prev_ref[c, p, pl.ds(8 * g, 8), :]
                src = src_ref[c, p, pl.ds(8 * g, 8), :]
                out_ref[c, p, pl.ds(8 * g, 8), :] = (2.0 * centers[c] - prev + upd) + src
        return carry

    lax.fori_loop(0, bx, plane, 0)


def elastic_step(upad, prev, moduli, sources, bx=8):
    _, px, py, depth = upad.shape
    nx, ny = px - 4, py - 4
    kernel = functools.partial(step_kernel, bx=bx)
    block = lambda i: (0, i, 0, 0)
    return pl.pallas_call(
        kernel,
        grid=(nx // bx,),
        in_specs=[
            pl.BlockSpec((3, px, py, depth), lambda i: (0, 0, 0, 0)),
            pl.BlockSpec((3, bx, ny, depth), block),
            pl.BlockSpec((2, bx, ny, depth), block),
            pl.BlockSpec((3, bx, ny, depth), block),
        ],
        out_specs=pl.BlockSpec((3, bx, ny, depth), block),
        out_shape=jax.ShapeDtypeStruct((3, nx, ny, depth), jnp.float32),
    )(upad, prev, moduli, sources)


def halo_padded(block, width):
    size_x = lax.axis_size("gx")
    size_y = lax.axis_size("gy")
    nx, ny = block.shape[1], block.shape[2]

    def shift(piece, step_x, step_y):
        pairs = []
        for ix in range(size_x):
            for iy in range(size_y):
                jx, jy = ix + step_x, iy + step_y
                if 0 <= jx < size_x and 0 <= jy < size_y:
                    pairs.append((ix * size_y + iy, jx * size_y + jy))
        return lax.ppermute(piece, ("gx", "gy"), pairs)

    lo_x = slice(0, width)
    hi_x = slice(nx - width, nx)
    lo_y = slice(0, width)
    hi_y = slice(ny - width, ny)
    whole = slice(None)
    part = lambda sx, sy: block[:, sx, sy, :]
    left = shift(part(hi_x, whole), 1, 0)
    right = shift(part(lo_x, whole), -1, 0)
    down = shift(part(whole, hi_y), 0, 1)
    up = shift(part(whole, lo_y), 0, -1)
    ll = shift(part(hi_x, hi_y), 1, 1)
    lh = shift(part(hi_x, lo_y), 1, -1)
    hl = shift(part(lo_x, hi_y), -1, 1)
    hh = shift(part(lo_x, lo_y), -1, -1)
    low_row = jnp.concatenate([ll, left, lh], axis=2)
    mid_row = jnp.concatenate([down, block, up], axis=2)
    high_row = jnp.concatenate([hl, right, hh], axis=2)
    return jnp.concatenate([low_row, mid_row, high_row], axis=1)


def level_table(values, layer_of_level):
    one_hot = (
        layer_of_level[:, None] == jnp.arange(values.shape[0], dtype=jnp.int32)[None, :]
    ).astype(jnp.float32)
    return jnp.sum(one_hot * values[None, :], axis=1)


def wave_kernel(angular, slowness, rigidity, damping, count_k):
    wavenum = (jnp.arange(count_k, dtype=jnp.float32) + 0.5) * (4.0 / count_k)
    spread = angular[None, :, None] * slowness[:, None, None]
    vertical = jnp.sqrt(wavenum[None, None, :] * wavenum[None, None, :] + spread * spread)
    impedance = rigidity[:, None, None] * vertical
    beneath = jnp.concatenate([impedance[1:], impedance[-1:]], axis=0)
    reflect = (impedance - beneath) / (impedance + beneath)
    fading = jnp.exp(-2.0 * step_depth * vertical * damping[:, None, None])
    two_way = 2.0 * step_depth * vertical
    trip_re = fading * jnp.cos(two_way)
    trip_im = -fading * jnp.sin(two_way)

    def upward(state_in, layer_data):
        refl_re, refl_im = state_in
        coefficient, along_re, along_im = layer_data
        upper_re = coefficient + refl_re
        lower_re = 1.0 + coefficient * refl_re
        lower_im = coefficient * refl_im
        magnitude = lower_re * lower_re + lower_im * lower_im
        ratio_re = (upper_re * lower_re + refl_im * lower_im) / magnitude
        ratio_im = (refl_im * lower_re - upper_re * lower_im) / magnitude
        fresh_re = along_re * ratio_re - along_im * ratio_im
        fresh_im = along_re * ratio_im + along_im * ratio_re
        return ((fresh_re, fresh_im), (fresh_re, fresh_im))

    bottom = jnp.zeros(vertical.shape[1:], jnp.float32)
    _, (refl_re, refl_im) = lax.scan(
        upward, (bottom, bottom), (reflect, trip_re, trip_im), reverse=True
    )
    travel = step_depth * vertical
    phases = jnp.cumsum(travel, axis=0) - travel
    absorbed = travel * damping[:, None, None]
    losses = jnp.cumsum(absorbed, axis=0) - absorbed
    down_size = jnp.exp(-losses)
    down_re = down_size * jnp.cos(phases)
    down_im = -down_size * jnp.sin(phases)
    weight = 1.0 / math.sqrt(count_k)
    kernel_re = weight * (down_re * (1.0 + refl_re) - down_im * refl_im)
    kernel_im = weight * (down_re * refl_im + down_im * (1.0 + refl_re))
    return jnp.transpose(jnp.stack([kernel_re, kernel_im]), (0, 2, 1, 3))


def offset_basis(count_k, count_r):
    modulus = count_k * count_r // 2
    low_count = 64
    odd_index = 2 * jnp.arange(count_k, dtype=jnp.int32) + 1
    high = jnp.arange(count_r // low_count, dtype=jnp.int32) * low_count
    low = jnp.arange(low_count, dtype=jnp.int32)
    scale = 2.0 * math.pi / modulus
    high_angle = (odd_index[:, None] * high[None, :] % modulus).astype(jnp.float32) * scale
    low_angle = (odd_index[:, None] * low[None, :] % modulus).astype(jnp.float32) * scale
    cos_h, sin_h = jnp.cos(high_angle), jnp.sin(high_angle)
    cos_l, sin_l = jnp.cos(low_angle), jnp.sin(low_angle)
    basis = cos_h[:, :, None] * cos_l[:, None, :] - sin_h[:, :, None] * sin_l[:, None, :]
    basis = basis.reshape(count_k, count_r).astype(jnp.bfloat16)
    return lax.optimization_barrier(basis)


def time_basis(freq_ids, count_f, count_steps, first_time):
    period = 2 * count_f
    times = first_time + jnp.arange(count_steps, dtype=jnp.int32)
    turns = (freq_ids[None, :] + 1) * times[:, None] % period
    angles = turns.astype(jnp.float32) * (2.0 * math.pi / period)
    weight = 1.0 / math.sqrt(count_f)
    return jnp.stack([weight * jnp.cos(angles), -weight * jnp.sin(angles)], axis=1)


def shifted(grid_block, step_x, step_y, step_z):
    width_x = grid_block.shape[0] - 4
    width_y = grid_block.shape[1] - 4
    width_z = grid_block.shape[2] - 4
    return grid_block[
        2 + step_x : 2 + step_x + width_x,
        2 + step_y : 2 + step_y + width_y,
        2 + step_z : 2 + step_z + width_z,
    ]


def curvature(grid_block, first_axis):
    summed = None
    for offset, factor in [(-2, -1.0), (-1, 16.0), (0, -30.0), (1, 16.0), (2, -1.0)]:
        moves = tuple((offset if index == first_axis else 0 for index in range(3)))
        contrib = factor * shifted(grid_block, moves[0], moves[1], moves[2])
        summed = contrib if summed is None else summed + contrib
    return summed / 12.0


def mixed(grid_block, first_axis, second_axis):
    summed = None
    for sign_a, sign_b, factor in [(1, 1, 1.0), (1, -1, -1.0), (-1, 1, -1.0), (-1, -1, 1.0)]:
        moves = tuple(
            (
                sign_a if index == first_axis else sign_b if index == second_axis else 0
                for index in range(3)
            )
        )
        contrib = factor * shifted(grid_block, moves[0], moves[1], moves[2])
        summed = contrib if summed is None else summed + contrib
    return summed / 4.0


def elastic(padded, moduli):
    first_lame = moduli[0]
    shear_mod = moduli[1]
    stiffness = first_lame + 2.0 * shear_mod
    coupling = first_lame + shear_mod
    result = []
    for component in range(3):
        update = stiffness * curvature(padded[component], component)
        for partner in range(3):
            if partner != component:
                update = update + shear_mod * curvature(padded[component], partner)
                update = update + coupling * mixed(padded[partner], component, partner)
        result.append(update)
    return jnp.stack(result)


def shards(
    layer_slowness,
    layer_rigidity,
    layer_damping,
    layer_of_level,
    slot_offset,
    slot_level,
    slot_target,
    live_count,
    moduli,
    field_old,
    field_now,
):
    size_gx = lax.axis_size("gx")
    size_gy = lax.axis_size("gy")
    groups = size_gx * size_gy
    per_device = F // groups
    device = lax.axis_index("gx") * size_gy + lax.axis_index("gy")
    freq_ids = device * per_device + jnp.arange(per_device, dtype=jnp.int32)
    angular = (freq_ids + 1).astype(jnp.float32) * (4.0 / F)
    slowness = level_table(layer_slowness, layer_of_level)
    rigidity = level_table(layer_rigidity, layer_of_level)
    damping = level_table(layer_damping, layer_of_level)
    kernel = wave_kernel(angular, slowness, rigidity, damping, NK).astype(jnp.bfloat16)
    cosines = offset_basis(NK, NR)
    spectrum_table = jnp.dot(
        kernel.reshape(2 * per_device * ND, NK), cosines, preferred_element_type=jnp.float32
    )
    table_rounded = spectrum_table.astype(jnp.bfloat16)
    all_slots = slot_offset.shape[0]
    width = math.gcd(all_slots, 4096)
    count_blocks = all_slots // width
    offset_blocks = slot_offset.reshape(count_blocks, width)
    level_blocks = slot_level.reshape(count_blocks, width)

    def select_block(pair):
        offsets, levels = pair
        offset_hot = (jnp.arange(NR, dtype=jnp.int32)[:, None] == offsets[None, :]).astype(
            jnp.bfloat16
        )
        rows = jnp.dot(table_rounded, offset_hot, preferred_element_type=jnp.float32).reshape(
            2, per_device, ND, width
        )
        level_hot = (jnp.arange(ND, dtype=jnp.int32)[:, None] == levels[None, :]).astype(
            jnp.float32
        )
        return jnp.sum(rows * level_hot[None, None, :, :], axis=2)

    selected = lax.map(select_block, (offset_blocks, level_blocks))
    spectra = (
        jnp.transpose(selected, (1, 2, 0, 3)).reshape(2, per_device, all_slots).astype(jnp.bfloat16)
    )
    slots_dev = slot_target.shape[0]
    occupied = (jnp.arange(slots_dev, dtype=jnp.int32) < live_count[0]).astype(jnp.float32)
    parcel = spectra.reshape(2, per_device, groups, slots_dev)
    arrived = lax.all_to_all(parcel, ("gx", "gy"), split_axis=2, concat_axis=1, tiled=True)
    freq_order = jnp.arange(F, dtype=jnp.int32)
    waveforms = time_basis(freq_order, F, STEPS, TSTART).reshape(STEPS, 2 * F)
    traces = jnp.dot(
        waveforms,
        arrived.reshape(2 * F, slots_dev).astype(jnp.float32),
        precision=lax.Precision.HIGHEST,
    )
    block_x = field_now.shape[1]
    block_y = field_now.shape[2]
    depth = field_now.shape[3]
    columns = slot_target // depth
    layer_z = slot_target % depth
    weighted = traces * occupied[None, :]
    column_hot = (
        jnp.arange(3 * block_x * block_y, dtype=jnp.int32)[:, None] == columns[None, :]
    ).astype(jnp.float32)
    depth_hot = (layer_z[:, None] == jnp.arange(depth, dtype=jnp.int32)[None, :]).astype(
        jnp.float32
    )
    previous, current = (field_old, field_now)
    for instant in range(STEPS):
        spread = weighted[instant][:, None] * depth_hot
        source = jnp.dot(column_hot, spread, precision=lax.Precision.HIGHEST)
        source = source.reshape(3, block_x, block_y, depth)
        padded = padded_2(current, (("gx", 1), ("gy", 2)), 2)
        advanced = elastic_step(padded, previous, moduli, source)
        previous, current = (current, advanced)
    return (current, previous)


def solution(mesh):
    in_specs = (
        P(),
        P(),
        P(),
        P(),
        P(),
        P(),
        P(("gx", "gy")),
        P(("gx", "gy")),
        P(None, "gx", "gy", None),
        P(None, "gx", "gy", None),
        P(None, "gx", "gy", None),
    )
    out_specs = (P(None, "gx", "gy", None), P(None, "gx", "gy", None))
    return jax.shard_map(shards, mesh=mesh, in_specs=in_specs, out_specs=out_specs, check_vma=False)
```

```python
import math

import jax
import jax.numpy as jnp
from jax import lax
from jax.sharding import PartitionSpec as P
from jax.experimental import pallas as pl
from jax.experimental.pallas import tpu as pltpu
import functools

F = 128
NK = 1024
NR = 2048
ND = 32
STEPS = 4
TSTART = 32


step_depth = 0.25


def padded_2(block, sides, width):
    for axis, dim in sides:
        count = lax.axis_size(axis)
        forward = [(i, i + 1) for i in range(count - 1)]
        backward = [(target, source) for source, target in forward]
        low = lax.ppermute(
            lax.slice_in_dim(block, block.shape[dim] - width, None, axis=dim), axis, forward
        )
        high = lax.ppermute(lax.slice_in_dim(block, 0, width, axis=dim), axis, backward)
        block = jnp.concatenate([low, block, high], axis=dim)
    return block


YPAD = 8


def step_kernel(up_ref, prev_ref, mod_ref, src_ref, out_ref, *, bx):
    i = pl.program_id(0)
    depth = out_ref.shape[3]
    lane = lax.broadcasted_iota(jnp.int32, (8, depth), 1)
    masks = {dz: (lane + dz >= 0) & (lane + dz < depth) for dz in (-2, -1, 1, 2)}

    def zs(v, dz):
        if dz == 0:
            return v
        return jnp.where(masks[dz], pltpu.roll(v, (-dz) % depth, 1), 0.0)

    def plane(p, carry):
        xp = i * bx + p + 2
        for g in range(out_ref.shape[2] // 8):
            def load(c, dx, dy):
                return up_ref[c, xp + dx, pl.ds(8 * g + YPAD + dy, 8), :]

            lam = mod_ref[0, p, pl.ds(8 * g, 8), :]
            mu = mod_ref[1, p, pl.ds(8 * g, 8), :]
            stiff = lam + 2.0 * mu
            coup = lam + mu
            centers = [load(c, 0, 0) for c in range(3)]

            def curv(c, axis):
                center = centers[c]
                near = None
                far = None
                for off in (-1, 1, -2, 2):
                    if axis == 0:
                        t = load(c, off, 0)
                    elif axis == 1:
                        t = load(c, 0, off)
                    else:
                        t = zs(center, off)
                    if abs(off) == 1:
                        near = t if near is None else near + t
                    else:
                        far = t if far is None else far + t
                return 16.0 * near - far - 30.0 * center

            def mixed(p_c, a, b):
                acc = None
                for sa in (1, -1):
                    for sb in (1, -1):
                        d = [0, 0, 0]
                        d[a] = sa
                        d[b] = sb
                        t = zs(load(p_c, d[0], d[1]), d[2])
                        if acc is None:
                            acc = t
                        elif sa * sb > 0:
                            acc = acc + t
                        else:
                            acc = acc - t
                return acc

            for c in range(3):
                others = [e for e in range(3) if e != c]
                second = stiff * curv(c, c) + mu * (curv(c, others[0]) + curv(c, others[1]))
                cross = mixed(others[0], c, others[0]) + mixed(others[1], c, others[1])
                upd = second * (1.0 / 12.0) + coup * (cross * 0.25)
                prev = prev_ref[c, p, pl.ds(8 * g, 8), :]
                src = src_ref[c, p, pl.ds(8 * g, 8), :]
                out_ref[c, p, pl.ds(8 * g, 8), :] = (2.0 * centers[c] - prev + upd) + src
        return carry

    lax.fori_loop(0, bx, plane, 0)


def elastic_step(upad, prev, moduli, sources, bx=8):
    _, px, py, depth = upad.shape
    nx, ny = px - 4, py - 2 * YPAD
    kernel = functools.partial(step_kernel, bx=bx)
    block = lambda i: (0, i, 0, 0)
    return pl.pallas_call(
        kernel,
        grid=(nx // bx,),
        in_specs=[
            pl.BlockSpec((3, px, py, depth), lambda i: (0, 0, 0, 0)),
            pl.BlockSpec((3, bx, ny, depth), block),
            pl.BlockSpec((2, bx, ny, depth), block),
            pl.BlockSpec((3, bx, ny, depth), block),
        ],
        out_specs=pl.BlockSpec((3, bx, ny, depth), block),
        out_shape=jax.ShapeDtypeStruct((3, nx, ny, depth), jnp.float32),
    )(upad, prev, moduli, sources)


def level_table(values, layer_of_level):
    one_hot = (
        layer_of_level[:, None] == jnp.arange(values.shape[0], dtype=jnp.int32)[None, :]
    ).astype(jnp.float32)
    return jnp.sum(one_hot * values[None, :], axis=1)


def wave_kernel(angular, slowness, rigidity, damping, count_k):
    wavenum = (jnp.arange(count_k, dtype=jnp.float32) + 0.5) * (4.0 / count_k)
    spread = angular[None, :, None] * slowness[:, None, None]
    vertical = jnp.sqrt(wavenum[None, None, :] * wavenum[None, None, :] + spread * spread)
    impedance = rigidity[:, None, None] * vertical
    beneath = jnp.concatenate([impedance[1:], impedance[-1:]], axis=0)
    reflect = (impedance - beneath) / (impedance + beneath)
    fading = jnp.exp(-2.0 * step_depth * vertical * damping[:, None, None])
    two_way = 2.0 * step_depth * vertical
    trip_re = fading * jnp.cos(two_way)
    trip_im = -fading * jnp.sin(two_way)

    def upward(state_in, layer_data):
        refl_re, refl_im = state_in
        coefficient, along_re, along_im = layer_data
        upper_re = coefficient + refl_re
        lower_re = 1.0 + coefficient * refl_re
        lower_im = coefficient * refl_im
        magnitude = lower_re * lower_re + lower_im * lower_im
        ratio_re = (upper_re * lower_re + refl_im * lower_im) / magnitude
        ratio_im = (refl_im * lower_re - upper_re * lower_im) / magnitude
        fresh_re = along_re * ratio_re - along_im * ratio_im
        fresh_im = along_re * ratio_im + along_im * ratio_re
        return ((fresh_re, fresh_im), (fresh_re, fresh_im))

    bottom = jnp.zeros(vertical.shape[1:], jnp.float32)
    _, (refl_re, refl_im) = lax.scan(
        upward, (bottom, bottom), (reflect, trip_re, trip_im), reverse=True
    )
    travel = step_depth * vertical
    phases = jnp.cumsum(travel, axis=0) - travel
    absorbed = travel * damping[:, None, None]
    losses = jnp.cumsum(absorbed, axis=0) - absorbed
    down_size = jnp.exp(-losses)
    down_re = down_size * jnp.cos(phases)
    down_im = -down_size * jnp.sin(phases)
    weight = 1.0 / math.sqrt(count_k)
    kernel_re = weight * (down_re * (1.0 + refl_re) - down_im * refl_im)
    kernel_im = weight * (down_re * refl_im + down_im * (1.0 + refl_re))
    return jnp.transpose(jnp.stack([kernel_re, kernel_im]), (0, 2, 1, 3))


def offset_basis(count_k, count_r):
    modulus = count_k * count_r // 2
    low_count = 64
    odd_index = 2 * jnp.arange(count_k, dtype=jnp.int32) + 1
    high = jnp.arange(count_r // low_count, dtype=jnp.int32) * low_count
    low = jnp.arange(low_count, dtype=jnp.int32)
    scale = 2.0 * math.pi / modulus
    high_angle = (odd_index[:, None] * high[None, :] % modulus).astype(jnp.float32) * scale
    low_angle = (odd_index[:, None] * low[None, :] % modulus).astype(jnp.float32) * scale
    cos_h, sin_h = jnp.cos(high_angle), jnp.sin(high_angle)
    cos_l, sin_l = jnp.cos(low_angle), jnp.sin(low_angle)
    basis = cos_h[:, :, None] * cos_l[:, None, :] - sin_h[:, :, None] * sin_l[:, None, :]
    basis = basis.reshape(count_k, count_r).astype(jnp.bfloat16)
    return lax.optimization_barrier(basis)


def time_basis(freq_ids, count_f, count_steps, first_time):
    period = 2 * count_f
    times = first_time + jnp.arange(count_steps, dtype=jnp.int32)
    turns = (freq_ids[None, :] + 1) * times[:, None] % period
    angles = turns.astype(jnp.float32) * (2.0 * math.pi / period)
    weight = 1.0 / math.sqrt(count_f)
    return jnp.stack([weight * jnp.cos(angles), -weight * jnp.sin(angles)], axis=1)


def shifted(grid_block, step_x, step_y, step_z):
    width_x = grid_block.shape[0] - 4
    width_y = grid_block.shape[1] - 4
    width_z = grid_block.shape[2] - 4
    return grid_block[
        2 + step_x : 2 + step_x + width_x,
        2 + step_y : 2 + step_y + width_y,
        2 + step_z : 2 + step_z + width_z,
    ]


def curvature(grid_block, first_axis):
    summed = None
    for offset, factor in [(-2, -1.0), (-1, 16.0), (0, -30.0), (1, 16.0), (2, -1.0)]:
        moves = tuple((offset if index == first_axis else 0 for index in range(3)))
        contrib = factor * shifted(grid_block, moves[0], moves[1], moves[2])
        summed = contrib if summed is None else summed + contrib
    return summed / 12.0


def mixed(grid_block, first_axis, second_axis):
    summed = None
    for sign_a, sign_b, factor in [(1, 1, 1.0), (1, -1, -1.0), (-1, 1, -1.0), (-1, -1, 1.0)]:
        moves = tuple(
            (
                sign_a if index == first_axis else sign_b if index == second_axis else 0
                for index in range(3)
            )
        )
        contrib = factor * shifted(grid_block, moves[0], moves[1], moves[2])
        summed = contrib if summed is None else summed + contrib
    return summed / 4.0


def elastic(padded, moduli):
    first_lame = moduli[0]
    shear_mod = moduli[1]
    stiffness = first_lame + 2.0 * shear_mod
    coupling = first_lame + shear_mod
    result = []
    for component in range(3):
        update = stiffness * curvature(padded[component], component)
        for partner in range(3):
            if partner != component:
                update = update + shear_mod * curvature(padded[component], partner)
                update = update + coupling * mixed(padded[partner], component, partner)
        result.append(update)
    return jnp.stack(result)


def shards(
    layer_slowness,
    layer_rigidity,
    layer_damping,
    layer_of_level,
    slot_offset,
    slot_level,
    slot_target,
    live_count,
    moduli,
    field_old,
    field_now,
):
    size_gx = lax.axis_size("gx")
    size_gy = lax.axis_size("gy")
    groups = size_gx * size_gy
    per_device = F // groups
    device = lax.axis_index("gx") * size_gy + lax.axis_index("gy")
    freq_ids = device * per_device + jnp.arange(per_device, dtype=jnp.int32)
    angular = (freq_ids + 1).astype(jnp.float32) * (4.0 / F)
    slowness = level_table(layer_slowness, layer_of_level)
    rigidity = level_table(layer_rigidity, layer_of_level)
    damping = level_table(layer_damping, layer_of_level)
    kernel = wave_kernel(angular, slowness, rigidity, damping, NK).astype(jnp.bfloat16)
    cosines = offset_basis(NK, NR)
    spectrum_table = jnp.dot(
        kernel.reshape(2 * per_device * ND, NK), cosines, preferred_element_type=jnp.float32
    )
    table_rounded = spectrum_table.astype(jnp.bfloat16)
    all_slots = slot_offset.shape[0]
    width = math.gcd(all_slots, 4096)
    count_blocks = all_slots // width
    offset_blocks = slot_offset.reshape(count_blocks, width)
    level_blocks = slot_level.reshape(count_blocks, width)

    def select_block(pair):
        offsets, levels = pair
        offset_hot = (jnp.arange(NR, dtype=jnp.int32)[:, None] == offsets[None, :]).astype(
            jnp.bfloat16
        )
        rows = jnp.dot(table_rounded, offset_hot, preferred_element_type=jnp.float32).reshape(
            2, per_device, ND, width
        )
        level_hot = (jnp.arange(ND, dtype=jnp.int32)[:, None] == levels[None, :]).astype(
            jnp.float32
        )
        return jnp.sum(rows * level_hot[None, None, :, :], axis=2)

    selected = lax.map(select_block, (offset_blocks, level_blocks))
    spectra = (
        jnp.transpose(selected, (1, 2, 0, 3)).reshape(2, per_device, all_slots).astype(jnp.bfloat16)
    )
    slots_dev = slot_target.shape[0]
    occupied = (jnp.arange(slots_dev, dtype=jnp.int32) < live_count[0]).astype(jnp.float32)
    parcel = spectra.reshape(2, per_device, groups, slots_dev)
    arrived = lax.all_to_all(parcel, ("gx", "gy"), split_axis=2, concat_axis=1, tiled=True)
    freq_order = jnp.arange(F, dtype=jnp.int32)
    waveforms = time_basis(freq_order, F, STEPS, TSTART).reshape(STEPS, 2 * F)
    traces = jnp.dot(
        waveforms,
        arrived.reshape(2 * F, slots_dev).astype(jnp.float32),
        precision=lax.Precision.HIGHEST,
    )
    block_x = field_now.shape[1]
    block_y = field_now.shape[2]
    depth = field_now.shape[3]
    columns = slot_target // depth
    layer_z = slot_target % depth
    weighted = traces * occupied[None, :]
    column_hot = (
        jnp.arange(3 * block_x * block_y, dtype=jnp.int32)[:, None] == columns[None, :]
    ).astype(jnp.float32)
    depth_hot = (layer_z[:, None] == jnp.arange(depth, dtype=jnp.int32)[None, :]).astype(
        jnp.float32
    )
    previous, current = (field_old, field_now)
    for instant in range(STEPS):
        spread = weighted[instant][:, None] * depth_hot
        source = jnp.dot(column_hot, spread, precision=lax.Precision.HIGHEST)
        source = source.reshape(3, block_x, block_y, depth)
        padded = padded_2(current, (("gx", 1), ("gy", 2)), 2)
        padded = jnp.pad(padded, ((0, 0), (0, 0), (YPAD - 2, YPAD - 2), (0, 0)))
        advanced = elastic_step(padded, previous, moduli, source)
        previous, current = (current, advanced)
    return (current, previous)


def solution(mesh):
    in_specs = (
        P(),
        P(),
        P(),
        P(),
        P(),
        P(),
        P(("gx", "gy")),
        P(("gx", "gy")),
        P(None, "gx", "gy", None),
        P(None, "gx", "gy", None),
        P(None, "gx", "gy", None),
    )
    out_specs = (P(None, "gx", "gy", None), P(None, "gx", "gy", None))
    return jax.shard_map(shards, mesh=mesh, in_specs=in_specs, out_specs=out_specs, check_vma=False)
```

```python
import math

import jax
import jax.numpy as jnp
from jax import lax
from jax.sharding import PartitionSpec as P
from jax.experimental import pallas as pl
from jax.experimental.pallas import tpu as pltpu
import functools

F = 128
NK = 1024
NR = 2048
ND = 32
STEPS = 4
TSTART = 32


step_depth = 0.25


def padded_2(block, sides, width):
    for axis, dim in sides:
        count = lax.axis_size(axis)
        forward = [(i, i + 1) for i in range(count - 1)]
        backward = [(target, source) for source, target in forward]
        low = lax.ppermute(
            lax.slice_in_dim(block, block.shape[dim] - width, None, axis=dim), axis, forward
        )
        high = lax.ppermute(lax.slice_in_dim(block, 0, width, axis=dim), axis, backward)
        block = jnp.concatenate([low, block, high], axis=dim)
    return block


YPAD = 8


def step_kernel(up_ref, prev_ref, mod_ref, src_ref, *rest, bx, first, stride):
    out_ref = rest[-1]
    i = first + pl.program_id(0) * stride
    depth = out_ref.shape[3]
    lane = lax.broadcasted_iota(jnp.int32, (8, depth), 1)
    masks = {dz: (lane + dz >= 0) & (lane + dz < depth) for dz in (-2, -1, 1, 2)}

    def zs(v, dz):
        if dz == 0:
            return v
        return jnp.where(masks[dz], pltpu.roll(v, (-dz) % depth, 1), 0.0)

    def plane(p, carry):
        xp = i * bx + p + 2
        for g in range(out_ref.shape[2] // 8):
            def load(c, dx, dy):
                return up_ref[c, xp + dx, pl.ds(8 * g + YPAD + dy, 8), :]

            lam = mod_ref[0, p, pl.ds(8 * g, 8), :]
            mu = mod_ref[1, p, pl.ds(8 * g, 8), :]
            stiff = lam + 2.0 * mu
            coup = lam + mu
            centers = [load(c, 0, 0) for c in range(3)]

            def curv(c, axis):
                center = centers[c]
                near = None
                far = None
                for off in (-1, 1, -2, 2):
                    if axis == 0:
                        t = load(c, off, 0)
                    elif axis == 1:
                        t = load(c, 0, off)
                    else:
                        t = zs(center, off)
                    if abs(off) == 1:
                        near = t if near is None else near + t
                    else:
                        far = t if far is None else far + t
                return 16.0 * near - far - 30.0 * center

            def mixed(p_c, a, b):
                acc = None
                for sa in (1, -1):
                    for sb in (1, -1):
                        d = [0, 0, 0]
                        d[a] = sa
                        d[b] = sb
                        t = zs(load(p_c, d[0], d[1]), d[2])
                        if acc is None:
                            acc = t
                        elif sa * sb > 0:
                            acc = acc + t
                        else:
                            acc = acc - t
                return acc

            for c in range(3):
                others = [e for e in range(3) if e != c]
                second = stiff * curv(c, c) + mu * (curv(c, others[0]) + curv(c, others[1]))
                cross = mixed(others[0], c, others[0]) + mixed(others[1], c, others[1])
                upd = second * (1.0 / 12.0) + coup * (cross * 0.25)
                prev = prev_ref[c, p, pl.ds(8 * g, 8), :]
                src = src_ref[c, p, pl.ds(8 * g, 8), :]
                out_ref[c, p, pl.ds(8 * g, 8), :] = (2.0 * centers[c] - prev + upd) + src
        return carry

    lax.fori_loop(0, bx, plane, 0)


def elastic_part(upad, prev, moduli, sources, bx, first, stride, count, into=None):
    _, px, py, depth = upad.shape
    nx, ny = px - 4, py - 2 * YPAD
    kernel = functools.partial(step_kernel, bx=bx, first=first, stride=stride)
    block = lambda i: (0, first + i * stride, 0, 0)
    in_specs = [
        pl.BlockSpec((3, px, py, depth), lambda i: (0, 0, 0, 0)),
        pl.BlockSpec((3, bx, ny, depth), block),
        pl.BlockSpec((2, bx, ny, depth), block),
        pl.BlockSpec((3, bx, ny, depth), block),
    ]
    operands = [upad, prev, moduli, sources]
    aliases = {}
    if into is not None:
        in_specs.append(pl.BlockSpec(memory_space=pl.ANY))
        operands.append(into)
        aliases = {4: 0}
    return pl.pallas_call(
        kernel,
        grid=(count,),
        in_specs=in_specs,
        out_specs=pl.BlockSpec((3, bx, ny, depth), block),
        out_shape=jax.ShapeDtypeStruct((3, nx, ny, depth), jnp.float32),
        input_output_aliases=aliases,
    )(*operands)


def elastic_step(upad, prev, moduli, sources, bx=4):
    nx = upad.shape[1] - 4
    blocks = nx // bx
    edge = elastic_part(upad, prev, moduli, sources, bx, 0, blocks - 1, 2)
    whole = elastic_part(upad, prev, moduli, sources, bx, 1, 1, blocks - 2, into=edge)
    return edge, whole


def exchange(edge, whole, width):
    size_x = lax.axis_size("gx")
    size_y = lax.axis_size("gy")
    nx = whole.shape[1]
    forward_x = [(i, i + 1) for i in range(size_x - 1)]
    backward_x = [(t, s) for s, t in forward_x]
    low = lax.ppermute(edge[:, nx - width:], "gx", forward_x)
    high = lax.ppermute(edge[:, :width], "gx", backward_x)
    block = jnp.concatenate([low, whole, high], axis=1)
    ny = block.shape[2]
    forward_y = [(i, i + 1) for i in range(size_y - 1)]
    backward_y = [(t, s) for s, t in forward_y]
    low = lax.ppermute(block[:, :, ny - width:], "gy", forward_y)
    high = lax.ppermute(block[:, :, :width], "gy", backward_y)
    pad = jnp.zeros(block.shape[:2] + (YPAD - width,) + block.shape[3:], block.dtype)
    return jnp.concatenate([pad, low, block, high, pad], axis=2)


def level_table(values, layer_of_level):
    one_hot = (
        layer_of_level[:, None] == jnp.arange(values.shape[0], dtype=jnp.int32)[None, :]
    ).astype(jnp.float32)
    return jnp.sum(one_hot * values[None, :], axis=1)


def wave_kernel(angular, slowness, rigidity, damping, count_k):
    wavenum = (jnp.arange(count_k, dtype=jnp.float32) + 0.5) * (4.0 / count_k)
    spread = angular[None, :, None] * slowness[:, None, None]
    vertical = jnp.sqrt(wavenum[None, None, :] * wavenum[None, None, :] + spread * spread)
    impedance = rigidity[:, None, None] * vertical
    beneath = jnp.concatenate([impedance[1:], impedance[-1:]], axis=0)
    reflect = (impedance - beneath) / (impedance + beneath)
    fading = jnp.exp(-2.0 * step_depth * vertical * damping[:, None, None])
    two_way = 2.0 * step_depth * vertical
    trip_re = fading * jnp.cos(two_way)
    trip_im = -fading * jnp.sin(two_way)

    def upward(state_in, layer_data):
        refl_re, refl_im = state_in
        coefficient, along_re, along_im = layer_data
        upper_re = coefficient + refl_re
        lower_re = 1.0 + coefficient * refl_re
        lower_im = coefficient * refl_im
        magnitude = lower_re * lower_re + lower_im * lower_im
        ratio_re = (upper_re * lower_re + refl_im * lower_im) / magnitude
        ratio_im = (refl_im * lower_re - upper_re * lower_im) / magnitude
        fresh_re = along_re * ratio_re - along_im * ratio_im
        fresh_im = along_re * ratio_im + along_im * ratio_re
        return ((fresh_re, fresh_im), (fresh_re, fresh_im))

    bottom = jnp.zeros(vertical.shape[1:], jnp.float32)
    _, (refl_re, refl_im) = lax.scan(
        upward, (bottom, bottom), (reflect, trip_re, trip_im), reverse=True
    )
    travel = step_depth * vertical
    phases = jnp.cumsum(travel, axis=0) - travel
    absorbed = travel * damping[:, None, None]
    losses = jnp.cumsum(absorbed, axis=0) - absorbed
    down_size = jnp.exp(-losses)
    down_re = down_size * jnp.cos(phases)
    down_im = -down_size * jnp.sin(phases)
    weight = 1.0 / math.sqrt(count_k)
    kernel_re = weight * (down_re * (1.0 + refl_re) - down_im * refl_im)
    kernel_im = weight * (down_re * refl_im + down_im * (1.0 + refl_re))
    return jnp.transpose(jnp.stack([kernel_re, kernel_im]), (0, 2, 1, 3))


def offset_basis(count_k, count_r):
    modulus = count_k * count_r // 2
    low_count = 64
    odd_index = 2 * jnp.arange(count_k, dtype=jnp.int32) + 1
    high = jnp.arange(count_r // low_count, dtype=jnp.int32) * low_count
    low = jnp.arange(low_count, dtype=jnp.int32)
    scale = 2.0 * math.pi / modulus
    high_angle = (odd_index[:, None] * high[None, :] % modulus).astype(jnp.float32) * scale
    low_angle = (odd_index[:, None] * low[None, :] % modulus).astype(jnp.float32) * scale
    cos_h, sin_h = jnp.cos(high_angle), jnp.sin(high_angle)
    cos_l, sin_l = jnp.cos(low_angle), jnp.sin(low_angle)
    basis = cos_h[:, :, None] * cos_l[:, None, :] - sin_h[:, :, None] * sin_l[:, None, :]
    basis = basis.reshape(count_k, count_r).astype(jnp.bfloat16)
    return lax.optimization_barrier(basis)


def time_basis(freq_ids, count_f, count_steps, first_time):
    period = 2 * count_f
    times = first_time + jnp.arange(count_steps, dtype=jnp.int32)
    turns = (freq_ids[None, :] + 1) * times[:, None] % period
    angles = turns.astype(jnp.float32) * (2.0 * math.pi / period)
    weight = 1.0 / math.sqrt(count_f)
    return jnp.stack([weight * jnp.cos(angles), -weight * jnp.sin(angles)], axis=1)


def shifted(grid_block, step_x, step_y, step_z):
    width_x = grid_block.shape[0] - 4
    width_y = grid_block.shape[1] - 4
    width_z = grid_block.shape[2] - 4
    return grid_block[
        2 + step_x : 2 + step_x + width_x,
        2 + step_y : 2 + step_y + width_y,
        2 + step_z : 2 + step_z + width_z,
    ]


def curvature(grid_block, first_axis):
    summed = None
    for offset, factor in [(-2, -1.0), (-1, 16.0), (0, -30.0), (1, 16.0), (2, -1.0)]:
        moves = tuple((offset if index == first_axis else 0 for index in range(3)))
        contrib = factor * shifted(grid_block, moves[0], moves[1], moves[2])
        summed = contrib if summed is None else summed + contrib
    return summed / 12.0


def mixed(grid_block, first_axis, second_axis):
    summed = None
    for sign_a, sign_b, factor in [(1, 1, 1.0), (1, -1, -1.0), (-1, 1, -1.0), (-1, -1, 1.0)]:
        moves = tuple(
            (
                sign_a if index == first_axis else sign_b if index == second_axis else 0
                for index in range(3)
            )
        )
        contrib = factor * shifted(grid_block, moves[0], moves[1], moves[2])
        summed = contrib if summed is None else summed + contrib
    return summed / 4.0


def elastic(padded, moduli):
    first_lame = moduli[0]
    shear_mod = moduli[1]
    stiffness = first_lame + 2.0 * shear_mod
    coupling = first_lame + shear_mod
    result = []
    for component in range(3):
        update = stiffness * curvature(padded[component], component)
        for partner in range(3):
            if partner != component:
                update = update + shear_mod * curvature(padded[component], partner)
                update = update + coupling * mixed(padded[partner], component, partner)
        result.append(update)
    return jnp.stack(result)


def shards(
    layer_slowness,
    layer_rigidity,
    layer_damping,
    layer_of_level,
    slot_offset,
    slot_level,
    slot_target,
    live_count,
    moduli,
    field_old,
    field_now,
):
    size_gx = lax.axis_size("gx")
    size_gy = lax.axis_size("gy")
    groups = size_gx * size_gy
    per_device = F // groups
    device = lax.axis_index("gx") * size_gy + lax.axis_index("gy")
    freq_ids = device * per_device + jnp.arange(per_device, dtype=jnp.int32)
    angular = (freq_ids + 1).astype(jnp.float32) * (4.0 / F)
    slowness = level_table(layer_slowness, layer_of_level)
    rigidity = level_table(layer_rigidity, layer_of_level)
    damping = level_table(layer_damping, layer_of_level)
    kernel = wave_kernel(angular, slowness, rigidity, damping, NK).astype(jnp.bfloat16)
    cosines = offset_basis(NK, NR)
    spectrum_table = jnp.dot(
        kernel.reshape(2 * per_device * ND, NK), cosines, preferred_element_type=jnp.float32
    )
    table_rounded = spectrum_table.astype(jnp.bfloat16)
    all_slots = slot_offset.shape[0]
    width = math.gcd(all_slots, 4096)
    count_blocks = all_slots // width
    offset_blocks = slot_offset.reshape(count_blocks, width)
    level_blocks = slot_level.reshape(count_blocks, width)

    def select_block(pair):
        offsets, levels = pair
        offset_hot = (jnp.arange(NR, dtype=jnp.int32)[:, None] == offsets[None, :]).astype(
            jnp.bfloat16
        )
        rows = jnp.dot(table_rounded, offset_hot, preferred_element_type=jnp.float32).reshape(
            2, per_device, ND, width
        )
        level_hot = (jnp.arange(ND, dtype=jnp.int32)[:, None] == levels[None, :]).astype(
            jnp.float32
        )
        return jnp.sum(rows * level_hot[None, None, :, :], axis=2)

    selected = lax.map(select_block, (offset_blocks, level_blocks))
    spectra = (
        jnp.transpose(selected, (1, 2, 0, 3)).reshape(2, per_device, all_slots).astype(jnp.bfloat16)
    )
    slots_dev = slot_target.shape[0]
    occupied = (jnp.arange(slots_dev, dtype=jnp.int32) < live_count[0]).astype(jnp.float32)
    parcel = spectra.reshape(2, per_device, groups, slots_dev)
    arrived = lax.all_to_all(parcel, ("gx", "gy"), split_axis=2, concat_axis=1, tiled=True)
    freq_order = jnp.arange(F, dtype=jnp.int32)
    waveforms = time_basis(freq_order, F, STEPS, TSTART).reshape(STEPS, 2 * F)
    traces = jnp.dot(
        waveforms,
        arrived.reshape(2 * F, slots_dev).astype(jnp.float32),
        precision=lax.Precision.HIGHEST,
    )
    block_x = field_now.shape[1]
    block_y = field_now.shape[2]
    depth = field_now.shape[3]
    columns = slot_target // depth
    layer_z = slot_target % depth
    weighted = traces * occupied[None, :]
    column_hot = (
        jnp.arange(3 * block_x * block_y, dtype=jnp.int32)[:, None] == columns[None, :]
    ).astype(jnp.float32)
    depth_hot = (layer_z[:, None] == jnp.arange(depth, dtype=jnp.int32)[None, :]).astype(
        jnp.float32
    )
    previous, current = (field_old, field_now)
    edge = field_now
    for instant in range(STEPS):
        spread = weighted[instant][:, None] * depth_hot
        source = jnp.dot(column_hot, spread, precision=lax.Precision.HIGHEST)
        source = source.reshape(3, block_x, block_y, depth)
        padded = exchange(edge, current, 2)
        edge, advanced = elastic_step(padded, previous, moduli, source)
        previous, current = (current, advanced)
    return (current, previous)


def solution(mesh):
    in_specs = (
        P(),
        P(),
        P(),
        P(),
        P(),
        P(),
        P(("gx", "gy")),
        P(("gx", "gy")),
        P(None, "gx", "gy", None),
        P(None, "gx", "gy", None),
        P(None, "gx", "gy", None),
    )
    out_specs = (P(None, "gx", "gy", None), P(None, "gx", "gy", None))
    return jax.shard_map(shards, mesh=mesh, in_specs=in_specs, out_specs=out_specs, check_vma=False)
```

```python
import math

import jax
import jax.numpy as jnp
from jax import lax
from jax.sharding import PartitionSpec as P
from jax.experimental import pallas as pl
from jax.experimental.pallas import tpu as pltpu
import functools

F = 128
NK = 1024
NR = 2048
ND = 32
STEPS = 4
TSTART = 32


step_depth = 0.25


def padded_2(block, sides, width):
    for axis, dim in sides:
        count = lax.axis_size(axis)
        forward = [(i, i + 1) for i in range(count - 1)]
        backward = [(target, source) for source, target in forward]
        low = lax.ppermute(
            lax.slice_in_dim(block, block.shape[dim] - width, None, axis=dim), axis, forward
        )
        high = lax.ppermute(lax.slice_in_dim(block, 0, width, axis=dim), axis, backward)
        block = jnp.concatenate([low, block, high], axis=dim)
    return block


YPAD = 8


def step_kernel(up_ref, prev_ref, mod_ref, src_ref, out_ref, *, bx):
    i = pl.program_id(0)
    depth = out_ref.shape[3]
    lane = lax.broadcasted_iota(jnp.int32, (8, depth), 1)
    masks = {dz: (lane + dz >= 0) & (lane + dz < depth) for dz in (-2, -1, 1, 2)}

    def zs(v, dz):
        if dz == 0:
            return v
        return jnp.where(masks[dz], pltpu.roll(v, (-dz) % depth, 1), 0.0)

    def plane(p, carry):
        xp = i * bx + p + 2
        for g in range(out_ref.shape[2] // 8):
            def load(c, dx, dy):
                return up_ref[c, xp + dx, pl.ds(8 * g + YPAD + dy, 8), :]

            lam = mod_ref[0, p, pl.ds(8 * g, 8), :]
            mu = mod_ref[1, p, pl.ds(8 * g, 8), :]
            stiff = lam + 2.0 * mu
            coup = lam + mu
            centers = [load(c, 0, 0) for c in range(3)]

            def curv(c, axis):
                center = centers[c]
                near = None
                far = None
                for off in (-1, 1, -2, 2):
                    if axis == 0:
                        t = load(c, off, 0)
                    elif axis == 1:
                        t = load(c, 0, off)
                    else:
                        t = zs(center, off)
                    if abs(off) == 1:
                        near = t if near is None else near + t
                    else:
                        far = t if far is None else far + t
                return 16.0 * near - far - 30.0 * center

            def mixed(p_c, a, b):
                acc = None
                for sa in (1, -1):
                    for sb in (1, -1):
                        d = [0, 0, 0]
                        d[a] = sa
                        d[b] = sb
                        t = zs(load(p_c, d[0], d[1]), d[2])
                        if acc is None:
                            acc = t
                        elif sa * sb > 0:
                            acc = acc + t
                        else:
                            acc = acc - t
                return acc

            for c in range(3):
                others = [e for e in range(3) if e != c]
                second = stiff * curv(c, c) + mu * (curv(c, others[0]) + curv(c, others[1]))
                cross = mixed(others[0], c, others[0]) + mixed(others[1], c, others[1])
                upd = second * (1.0 / 12.0) + coup * (cross * 0.25)
                prev = prev_ref[c, p, pl.ds(8 * g, 8), :]
                src = src_ref[c, p, pl.ds(8 * g, 8), :]
                out_ref[c, p, pl.ds(8 * g, 8), :] = (2.0 * centers[c] - prev + upd) + src
        return carry

    lax.fori_loop(0, bx, plane, 0)


def elastic_step(upad, prev, moduli, sources, bx=8):
    _, px, py, depth = upad.shape
    nx, ny = px - 4, py - 2 * YPAD
    kernel = functools.partial(step_kernel, bx=bx)
    block = lambda i: (0, i, 0, 0)
    return pl.pallas_call(
        kernel,
        grid=(nx // bx,),
        in_specs=[
            pl.BlockSpec((3, px, py, depth), lambda i: (0, 0, 0, 0)),
            pl.BlockSpec((3, bx, ny, depth), block),
            pl.BlockSpec((2, bx, ny, depth), block),
            pl.BlockSpec((3, bx, ny, depth), block),
        ],
        out_specs=pl.BlockSpec((3, bx, ny, depth), block),
        out_shape=jax.ShapeDtypeStruct((3, nx, ny, depth), jnp.float32),
    )(upad, prev, moduli, sources)


def level_table(values, layer_of_level):
    one_hot = (
        layer_of_level[:, None] == jnp.arange(values.shape[0], dtype=jnp.int32)[None, :]
    ).astype(jnp.float32)
    return jnp.sum(one_hot * values[None, :], axis=1)


def wave_kernel(angular, slowness, rigidity, damping, count_k):
    wavenum = (jnp.arange(count_k, dtype=jnp.float32) + 0.5) * (4.0 / count_k)
    spread = angular[None, :, None] * slowness[:, None, None]
    vertical = jnp.sqrt(wavenum[None, None, :] * wavenum[None, None, :] + spread * spread)
    impedance = rigidity[:, None, None] * vertical
    beneath = jnp.concatenate([impedance[1:], impedance[-1:]], axis=0)
    reflect = (impedance - beneath) / (impedance + beneath)
    fading = jnp.exp(-2.0 * step_depth * vertical * damping[:, None, None])
    two_way = 2.0 * step_depth * vertical
    trip_re = fading * jnp.cos(two_way)
    trip_im = -fading * jnp.sin(two_way)

    def upward(state_in, layer_data):
        refl_re, refl_im = state_in
        coefficient, along_re, along_im = layer_data
        upper_re = coefficient + refl_re
        lower_re = 1.0 + coefficient * refl_re
        lower_im = coefficient * refl_im
        magnitude = lower_re * lower_re + lower_im * lower_im
        ratio_re = (upper_re * lower_re + refl_im * lower_im) / magnitude
        ratio_im = (refl_im * lower_re - upper_re * lower_im) / magnitude
        fresh_re = along_re * ratio_re - along_im * ratio_im
        fresh_im = along_re * ratio_im + along_im * ratio_re
        return ((fresh_re, fresh_im), (fresh_re, fresh_im))

    bottom = jnp.zeros(vertical.shape[1:], jnp.float32)
    _, (refl_re, refl_im) = lax.scan(
        upward, (bottom, bottom), (reflect, trip_re, trip_im), reverse=True
    )
    travel = step_depth * vertical
    phases = jnp.cumsum(travel, axis=0) - travel
    absorbed = travel * damping[:, None, None]
    losses = jnp.cumsum(absorbed, axis=0) - absorbed
    down_size = jnp.exp(-losses)
    down_re = down_size * jnp.cos(phases)
    down_im = -down_size * jnp.sin(phases)
    weight = 1.0 / math.sqrt(count_k)
    kernel_re = weight * (down_re * (1.0 + refl_re) - down_im * refl_im)
    kernel_im = weight * (down_re * refl_im + down_im * (1.0 + refl_re))
    return jnp.transpose(jnp.stack([kernel_re, kernel_im]), (0, 2, 1, 3))


def offset_basis(count_k, count_r):
    modulus = count_k * count_r // 2
    low_count = 64
    odd_index = 2 * jnp.arange(count_k, dtype=jnp.int32) + 1
    high = jnp.arange(count_r // low_count, dtype=jnp.int32) * low_count
    low = jnp.arange(low_count, dtype=jnp.int32)
    scale = 2.0 * math.pi / modulus
    high_angle = (odd_index[:, None] * high[None, :] % modulus).astype(jnp.float32) * scale
    low_angle = (odd_index[:, None] * low[None, :] % modulus).astype(jnp.float32) * scale
    cos_h, sin_h = jnp.cos(high_angle), jnp.sin(high_angle)
    cos_l, sin_l = jnp.cos(low_angle), jnp.sin(low_angle)
    basis = cos_h[:, :, None] * cos_l[:, None, :] - sin_h[:, :, None] * sin_l[:, None, :]
    basis = basis.reshape(count_k, count_r).astype(jnp.bfloat16)
    return lax.optimization_barrier(basis)


def time_basis(freq_ids, count_f, count_steps, first_time):
    period = 2 * count_f
    times = first_time + jnp.arange(count_steps, dtype=jnp.int32)
    turns = (freq_ids[None, :] + 1) * times[:, None] % period
    angles = turns.astype(jnp.float32) * (2.0 * math.pi / period)
    weight = 1.0 / math.sqrt(count_f)
    return jnp.stack([weight * jnp.cos(angles), -weight * jnp.sin(angles)], axis=1)


def shifted(grid_block, step_x, step_y, step_z):
    width_x = grid_block.shape[0] - 4
    width_y = grid_block.shape[1] - 4
    width_z = grid_block.shape[2] - 4
    return grid_block[
        2 + step_x : 2 + step_x + width_x,
        2 + step_y : 2 + step_y + width_y,
        2 + step_z : 2 + step_z + width_z,
    ]


def curvature(grid_block, first_axis):
    summed = None
    for offset, factor in [(-2, -1.0), (-1, 16.0), (0, -30.0), (1, 16.0), (2, -1.0)]:
        moves = tuple((offset if index == first_axis else 0 for index in range(3)))
        contrib = factor * shifted(grid_block, moves[0], moves[1], moves[2])
        summed = contrib if summed is None else summed + contrib
    return summed / 12.0


def mixed(grid_block, first_axis, second_axis):
    summed = None
    for sign_a, sign_b, factor in [(1, 1, 1.0), (1, -1, -1.0), (-1, 1, -1.0), (-1, -1, 1.0)]:
        moves = tuple(
            (
                sign_a if index == first_axis else sign_b if index == second_axis else 0
                for index in range(3)
            )
        )
        contrib = factor * shifted(grid_block, moves[0], moves[1], moves[2])
        summed = contrib if summed is None else summed + contrib
    return summed / 4.0


def elastic(padded, moduli):
    first_lame = moduli[0]
    shear_mod = moduli[1]
    stiffness = first_lame + 2.0 * shear_mod
    coupling = first_lame + shear_mod
    result = []
    for component in range(3):
        update = stiffness * curvature(padded[component], component)
        for partner in range(3):
            if partner != component:
                update = update + shear_mod * curvature(padded[component], partner)
                update = update + coupling * mixed(padded[partner], component, partner)
        result.append(update)
    return jnp.stack(result)


def shards(
    layer_slowness,
    layer_rigidity,
    layer_damping,
    layer_of_level,
    slot_offset,
    slot_level,
    slot_target,
    live_count,
    moduli,
    field_old,
    field_now,
):
    size_gx = lax.axis_size("gx")
    size_gy = lax.axis_size("gy")
    groups = size_gx * size_gy
    per_device = F // groups
    device = lax.axis_index("gx") * size_gy + lax.axis_index("gy")
    freq_ids = device * per_device + jnp.arange(per_device, dtype=jnp.int32)
    angular = (freq_ids + 1).astype(jnp.float32) * (4.0 / F)
    slowness = level_table(layer_slowness, layer_of_level)
    rigidity = level_table(layer_rigidity, layer_of_level)
    damping = level_table(layer_damping, layer_of_level)
    kernel = wave_kernel(angular, slowness, rigidity, damping, NK).astype(jnp.bfloat16)
    cosines = offset_basis(NK, NR)
    spectrum_table = jnp.dot(
        kernel.reshape(2 * per_device * ND, NK), cosines, preferred_element_type=jnp.float32
    )
    table_rounded = spectrum_table.astype(jnp.bfloat16)
    first_padded = padded_2(field_now, (("gx", 1),), 2)
    first_padded, table_rounded = lax.optimization_barrier((first_padded, table_rounded))
    all_slots = slot_offset.shape[0]
    width = math.gcd(all_slots, 4096)
    count_blocks = all_slots // width
    offset_blocks = slot_offset.reshape(count_blocks, width)
    level_blocks = slot_level.reshape(count_blocks, width)

    def select_block(pair):
        offsets, levels = pair
        offset_hot = (jnp.arange(NR, dtype=jnp.int32)[:, None] == offsets[None, :]).astype(
            jnp.bfloat16
        )
        rows = jnp.dot(table_rounded, offset_hot, preferred_element_type=jnp.float32).reshape(
            2, per_device, ND, width
        )
        level_hot = (jnp.arange(ND, dtype=jnp.int32)[:, None] == levels[None, :]).astype(
            jnp.float32
        )
        return jnp.sum(rows * level_hot[None, None, :, :], axis=2)

    selected = lax.map(select_block, (offset_blocks, level_blocks))
    spectra = (
        jnp.transpose(selected, (1, 2, 0, 3)).reshape(2, per_device, all_slots).astype(jnp.bfloat16)
    )
    slots_dev = slot_target.shape[0]
    occupied = (jnp.arange(slots_dev, dtype=jnp.int32) < live_count[0]).astype(jnp.float32)
    first_padded = padded_2(first_padded, (("gy", 2),), 2)
    first_padded, spectra = lax.optimization_barrier((first_padded, spectra))
    parcel = spectra.reshape(2, per_device, groups, slots_dev)
    arrived = lax.all_to_all(parcel, ("gx", "gy"), split_axis=2, concat_axis=1, tiled=True)
    freq_order = jnp.arange(F, dtype=jnp.int32)
    waveforms = time_basis(freq_order, F, STEPS, TSTART).reshape(STEPS, 2 * F)
    traces = jnp.dot(
        waveforms,
        arrived.reshape(2 * F, slots_dev).astype(jnp.float32),
        precision=lax.Precision.HIGHEST,
    )
    block_x = field_now.shape[1]
    block_y = field_now.shape[2]
    depth = field_now.shape[3]
    columns = slot_target // depth
    layer_z = slot_target % depth
    weighted = traces * occupied[None, :]
    column_hot = (
        jnp.arange(3 * block_x * block_y, dtype=jnp.int32)[:, None] == columns[None, :]
    ).astype(jnp.float32)
    depth_hot = (layer_z[:, None] == jnp.arange(depth, dtype=jnp.int32)[None, :]).astype(
        jnp.float32
    )
    previous, current = (field_old, field_now)
    for instant in range(STEPS):
        spread = weighted[instant][:, None] * depth_hot
        source = jnp.dot(column_hot, spread, precision=lax.Precision.HIGHEST)
        source = source.reshape(3, block_x, block_y, depth)
        padded = first_padded if instant == 0 else padded_2(current, (("gx", 1), ("gy", 2)), 2)
        padded = jnp.pad(padded, ((0, 0), (0, 0), (YPAD - 2, YPAD - 2), (0, 0)))
        advanced = elastic_step(padded, previous, moduli, source)
        previous, current = (current, advanced)
    return (current, previous)


def solution(mesh):
    in_specs = (
        P(),
        P(),
        P(),
        P(),
        P(),
        P(),
        P(("gx", "gy")),
        P(("gx", "gy")),
        P(None, "gx", "gy", None),
        P(None, "gx", "gy", None),
        P(None, "gx", "gy", None),
    )
    out_specs = (P(None, "gx", "gy", None), P(None, "gx", "gy", None))
    return jax.shard_map(shards, mesh=mesh, in_specs=in_specs, out_specs=out_specs, check_vma=False)
```

```python
import math

import jax
import jax.numpy as jnp
from jax import lax
from jax.sharding import PartitionSpec as P
from jax.experimental import pallas as pl
from jax.experimental.pallas import tpu as pltpu
import functools

F = 128
NK = 1024
NR = 2048
ND = 32
STEPS = 4
TSTART = 32


step_depth = 0.25


def padded_2(block, sides, width):
    for axis, dim in sides:
        count = lax.axis_size(axis)
        forward = [(i, i + 1) for i in range(count - 1)]
        backward = [(target, source) for source, target in forward]
        low = lax.ppermute(
            lax.slice_in_dim(block, block.shape[dim] - width, None, axis=dim), axis, forward
        )
        high = lax.ppermute(lax.slice_in_dim(block, 0, width, axis=dim), axis, backward)
        block = jnp.concatenate([low, block, high], axis=dim)
    return block


YPAD = 8


def step_kernel(u_ref, xlo_ref, xhi_ref, ylo_ref, yhi_ref, prev_ref, mod_ref, src_ref, out_ref, up_ref, *, bx):
    i = pl.program_id(0)
    nx, ny = u_ref.shape[1], u_ref.shape[2]

    @pl.when(i == 0)
    def _():
        for c in range(3):
            def fill(x, carry):
                up_ref[c, x + 2, pl.ds(YPAD, ny), :] = u_ref[c, x]
                return carry

            lax.fori_loop(0, nx, fill, 0)
        up_ref[:, 0:2, pl.ds(YPAD, ny), :] = xlo_ref[...]
        up_ref[:, nx + 2:nx + 4, pl.ds(YPAD, ny), :] = xhi_ref[...]
        up_ref[:, :, pl.ds(YPAD - 2, 2), :] = ylo_ref[...]
        up_ref[:, :, pl.ds(YPAD + ny, 2), :] = yhi_ref[...]

    depth = out_ref.shape[3]
    lane = lax.broadcasted_iota(jnp.int32, (8, depth), 1)
    masks = {dz: (lane + dz >= 0) & (lane + dz < depth) for dz in (-2, -1, 1, 2)}

    def zs(v, dz):
        if dz == 0:
            return v
        return jnp.where(masks[dz], pltpu.roll(v, (-dz) % depth, 1), 0.0)

    def plane(p, carry):
        xp = i * bx + p + 2
        for g in range(out_ref.shape[2] // 8):
            def load(c, dx, dy):
                return up_ref[c, xp + dx, pl.ds(8 * g + YPAD + dy, 8), :]

            lam = mod_ref[0, p, pl.ds(8 * g, 8), :]
            mu = mod_ref[1, p, pl.ds(8 * g, 8), :]
            stiff = lam + 2.0 * mu
            coup = lam + mu
            centers = [load(c, 0, 0) for c in range(3)]

            def curv(c, axis):
                center = centers[c]
                near = None
                far = None
                for off in (-1, 1, -2, 2):
                    if axis == 0:
                        t = load(c, off, 0)
                    elif axis == 1:
                        t = load(c, 0, off)
                    else:
                        t = zs(center, off)
                    if abs(off) == 1:
                        near = t if near is None else near + t
                    else:
                        far = t if far is None else far + t
                return 16.0 * near - far - 30.0 * center

            def mixed(p_c, a, b):
                acc = None
                for sa in (1, -1):
                    for sb in (1, -1):
                        d = [0, 0, 0]
                        d[a] = sa
                        d[b] = sb
                        t = zs(load(p_c, d[0], d[1]), d[2])
                        if acc is None:
                            acc = t
                        elif sa * sb > 0:
                            acc = acc + t
                        else:
                            acc = acc - t
                return acc

            for c in range(3):
                others = [e for e in range(3) if e != c]
                second = stiff * curv(c, c) + mu * (curv(c, others[0]) + curv(c, others[1]))
                cross = mixed(others[0], c, others[0]) + mixed(others[1], c, others[1])
                upd = second * (1.0 / 12.0) + coup * (cross * 0.25)
                prev = prev_ref[c, p, pl.ds(8 * g, 8), :]
                src = src_ref[c, p, pl.ds(8 * g, 8), :]
                out_ref[c, p, pl.ds(8 * g, 8), :] = (2.0 * centers[c] - prev + upd) + src
        return carry

    lax.fori_loop(0, bx, plane, 0)


def elastic_step(u, xlo, xhi, ylo, yhi, prev, moduli, sources, bx=8):
    _, nx, ny, depth = u.shape
    kernel = functools.partial(step_kernel, bx=bx)
    block = lambda i: (0, i, 0, 0)
    whole = lambda i: (0, 0, 0, 0)
    return pl.pallas_call(
        kernel,
        grid=(nx // bx,),
        in_specs=[
            pl.BlockSpec(u.shape, whole),
            pl.BlockSpec(xlo.shape, whole),
            pl.BlockSpec(xhi.shape, whole),
            pl.BlockSpec(ylo.shape, whole),
            pl.BlockSpec(yhi.shape, whole),
            pl.BlockSpec((3, bx, ny, depth), block),
            pl.BlockSpec((2, bx, ny, depth), block),
            pl.BlockSpec((3, bx, ny, depth), block),
        ],
        out_specs=pl.BlockSpec((3, bx, ny, depth), block),
        out_shape=jax.ShapeDtypeStruct((3, nx, ny, depth), jnp.float32),
        scratch_shapes=[pltpu.VMEM((3, nx + 4, ny + 2 * YPAD, depth), jnp.float32)],
        compiler_params=pltpu.CompilerParams(dimension_semantics=("arbitrary",)),
    )(u, xlo, xhi, ylo, yhi, prev, moduli, sources)


def halos(block, width):
    size_x = lax.axis_size("gx")
    size_y = lax.axis_size("gy")
    nx, ny = block.shape[1], block.shape[2]
    forward_x = [(i, i + 1) for i in range(size_x - 1)]
    backward_x = [(t, s) for s, t in forward_x]
    xlo = lax.ppermute(block[:, nx - width:], "gx", forward_x)
    xhi = lax.ppermute(block[:, :width], "gx", backward_x)
    forward_y = [(i, i + 1) for i in range(size_y - 1)]
    backward_y = [(t, s) for s, t in forward_y]
    rows = lambda sl: jnp.concatenate([xlo[:, :, sl], block[:, :, sl], xhi[:, :, sl]], axis=1)
    ylo = lax.ppermute(rows(slice(ny - width, ny)), "gy", forward_y)
    yhi = lax.ppermute(rows(slice(0, width)), "gy", backward_y)
    return xlo, xhi, ylo, yhi


def level_table(values, layer_of_level):
    one_hot = (
        layer_of_level[:, None] == jnp.arange(values.shape[0], dtype=jnp.int32)[None, :]
    ).astype(jnp.float32)
    return jnp.sum(one_hot * values[None, :], axis=1)


def wave_kernel(angular, slowness, rigidity, damping, count_k):
    wavenum = (jnp.arange(count_k, dtype=jnp.float32) + 0.5) * (4.0 / count_k)
    spread = angular[None, :, None] * slowness[:, None, None]
    vertical = jnp.sqrt(wavenum[None, None, :] * wavenum[None, None, :] + spread * spread)
    impedance = rigidity[:, None, None] * vertical
    beneath = jnp.concatenate([impedance[1:], impedance[-1:]], axis=0)
    reflect = (impedance - beneath) / (impedance + beneath)
    fading = jnp.exp(-2.0 * step_depth * vertical * damping[:, None, None])
    two_way = 2.0 * step_depth * vertical
    trip_re = fading * jnp.cos(two_way)
    trip_im = -fading * jnp.sin(two_way)

    def upward(state_in, layer_data):
        refl_re, refl_im = state_in
        coefficient, along_re, along_im = layer_data
        upper_re = coefficient + refl_re
        lower_re = 1.0 + coefficient * refl_re
        lower_im = coefficient * refl_im
        magnitude = lower_re * lower_re + lower_im * lower_im
        ratio_re = (upper_re * lower_re + refl_im * lower_im) / magnitude
        ratio_im = (refl_im * lower_re - upper_re * lower_im) / magnitude
        fresh_re = along_re * ratio_re - along_im * ratio_im
        fresh_im = along_re * ratio_im + along_im * ratio_re
        return ((fresh_re, fresh_im), (fresh_re, fresh_im))

    bottom = jnp.zeros(vertical.shape[1:], jnp.float32)
    _, (refl_re, refl_im) = lax.scan(
        upward, (bottom, bottom), (reflect, trip_re, trip_im), reverse=True
    )
    travel = step_depth * vertical
    phases = jnp.cumsum(travel, axis=0) - travel
    absorbed = travel * damping[:, None, None]
    losses = jnp.cumsum(absorbed, axis=0) - absorbed
    down_size = jnp.exp(-losses)
    down_re = down_size * jnp.cos(phases)
    down_im = -down_size * jnp.sin(phases)
    weight = 1.0 / math.sqrt(count_k)
    kernel_re = weight * (down_re * (1.0 + refl_re) - down_im * refl_im)
    kernel_im = weight * (down_re * refl_im + down_im * (1.0 + refl_re))
    return jnp.transpose(jnp.stack([kernel_re, kernel_im]), (0, 2, 1, 3))


def offset_basis(count_k, count_r):
    modulus = count_k * count_r // 2
    low_count = 64
    odd_index = 2 * jnp.arange(count_k, dtype=jnp.int32) + 1
    high = jnp.arange(count_r // low_count, dtype=jnp.int32) * low_count
    low = jnp.arange(low_count, dtype=jnp.int32)
    scale = 2.0 * math.pi / modulus
    high_angle = (odd_index[:, None] * high[None, :] % modulus).astype(jnp.float32) * scale
    low_angle = (odd_index[:, None] * low[None, :] % modulus).astype(jnp.float32) * scale
    cos_h, sin_h = jnp.cos(high_angle), jnp.sin(high_angle)
    cos_l, sin_l = jnp.cos(low_angle), jnp.sin(low_angle)
    basis = cos_h[:, :, None] * cos_l[:, None, :] - sin_h[:, :, None] * sin_l[:, None, :]
    basis = basis.reshape(count_k, count_r).astype(jnp.bfloat16)
    return lax.optimization_barrier(basis)


def time_basis(freq_ids, count_f, count_steps, first_time):
    period = 2 * count_f
    times = first_time + jnp.arange(count_steps, dtype=jnp.int32)
    turns = (freq_ids[None, :] + 1) * times[:, None] % period
    angles = turns.astype(jnp.float32) * (2.0 * math.pi / period)
    weight = 1.0 / math.sqrt(count_f)
    return jnp.stack([weight * jnp.cos(angles), -weight * jnp.sin(angles)], axis=1)


def shifted(grid_block, step_x, step_y, step_z):
    width_x = grid_block.shape[0] - 4
    width_y = grid_block.shape[1] - 4
    width_z = grid_block.shape[2] - 4
    return grid_block[
        2 + step_x : 2 + step_x + width_x,
        2 + step_y : 2 + step_y + width_y,
        2 + step_z : 2 + step_z + width_z,
    ]


def curvature(grid_block, first_axis):
    summed = None
    for offset, factor in [(-2, -1.0), (-1, 16.0), (0, -30.0), (1, 16.0), (2, -1.0)]:
        moves = tuple((offset if index == first_axis else 0 for index in range(3)))
        contrib = factor * shifted(grid_block, moves[0], moves[1], moves[2])
        summed = contrib if summed is None else summed + contrib
    return summed / 12.0


def mixed(grid_block, first_axis, second_axis):
    summed = None
    for sign_a, sign_b, factor in [(1, 1, 1.0), (1, -1, -1.0), (-1, 1, -1.0), (-1, -1, 1.0)]:
        moves = tuple(
            (
                sign_a if index == first_axis else sign_b if index == second_axis else 0
                for index in range(3)
            )
        )
        contrib = factor * shifted(grid_block, moves[0], moves[1], moves[2])
        summed = contrib if summed is None else summed + contrib
    return summed / 4.0


def elastic(padded, moduli):
    first_lame = moduli[0]
    shear_mod = moduli[1]
    stiffness = first_lame + 2.0 * shear_mod
    coupling = first_lame + shear_mod
    result = []
    for component in range(3):
        update = stiffness * curvature(padded[component], component)
        for partner in range(3):
            if partner != component:
                update = update + shear_mod * curvature(padded[component], partner)
                update = update + coupling * mixed(padded[partner], component, partner)
        result.append(update)
    return jnp.stack(result)


def shards(
    layer_slowness,
    layer_rigidity,
    layer_damping,
    layer_of_level,
    slot_offset,
    slot_level,
    slot_target,
    live_count,
    moduli,
    field_old,
    field_now,
):
    size_gx = lax.axis_size("gx")
    size_gy = lax.axis_size("gy")
    groups = size_gx * size_gy
    per_device = F // groups
    device = lax.axis_index("gx") * size_gy + lax.axis_index("gy")
    freq_ids = device * per_device + jnp.arange(per_device, dtype=jnp.int32)
    angular = (freq_ids + 1).astype(jnp.float32) * (4.0 / F)
    slowness = level_table(layer_slowness, layer_of_level)
    rigidity = level_table(layer_rigidity, layer_of_level)
    damping = level_table(layer_damping, layer_of_level)
    kernel = wave_kernel(angular, slowness, rigidity, damping, NK).astype(jnp.bfloat16)
    cosines = offset_basis(NK, NR)
    spectrum_table = jnp.dot(
        kernel.reshape(2 * per_device * ND, NK), cosines, preferred_element_type=jnp.float32
    )
    table_rounded = spectrum_table.astype(jnp.bfloat16)
    all_slots = slot_offset.shape[0]
    width = math.gcd(all_slots, 4096)
    count_blocks = all_slots // width
    offset_blocks = slot_offset.reshape(count_blocks, width)
    level_blocks = slot_level.reshape(count_blocks, width)

    def select_block(pair):
        offsets, levels = pair
        offset_hot = (jnp.arange(NR, dtype=jnp.int32)[:, None] == offsets[None, :]).astype(
            jnp.bfloat16
        )
        rows = jnp.dot(table_rounded, offset_hot, preferred_element_type=jnp.float32).reshape(
            2, per_device, ND, width
        )
        level_hot = (jnp.arange(ND, dtype=jnp.int32)[:, None] == levels[None, :]).astype(
            jnp.float32
        )
        return jnp.sum(rows * level_hot[None, None, :, :], axis=2)

    selected = lax.map(select_block, (offset_blocks, level_blocks))
    spectra = (
        jnp.transpose(selected, (1, 2, 0, 3)).reshape(2, per_device, all_slots).astype(jnp.bfloat16)
    )
    slots_dev = slot_target.shape[0]
    occupied = (jnp.arange(slots_dev, dtype=jnp.int32) < live_count[0]).astype(jnp.float32)
    parcel = spectra.reshape(2, per_device, groups, slots_dev)
    arrived = lax.all_to_all(parcel, ("gx", "gy"), split_axis=2, concat_axis=1, tiled=True)
    freq_order = jnp.arange(F, dtype=jnp.int32)
    waveforms = time_basis(freq_order, F, STEPS, TSTART).reshape(STEPS, 2 * F)
    traces = jnp.dot(
        waveforms,
        arrived.reshape(2 * F, slots_dev).astype(jnp.float32),
        precision=lax.Precision.HIGHEST,
    )
    block_x = field_now.shape[1]
    block_y = field_now.shape[2]
    depth = field_now.shape[3]
    columns = slot_target // depth
    layer_z = slot_target % depth
    weighted = traces * occupied[None, :]
    column_hot = (
        jnp.arange(3 * block_x * block_y, dtype=jnp.int32)[:, None] == columns[None, :]
    ).astype(jnp.float32)
    depth_hot = (layer_z[:, None] == jnp.arange(depth, dtype=jnp.int32)[None, :]).astype(
        jnp.float32
    )
    previous, current = (field_old, field_now)
    for instant in range(STEPS):
        spread = weighted[instant][:, None] * depth_hot
        source = jnp.dot(column_hot, spread, precision=lax.Precision.HIGHEST)
        source = source.reshape(3, block_x, block_y, depth)
        xlo, xhi, ylo, yhi = halos(current, 2)
        advanced = elastic_step(current, xlo, xhi, ylo, yhi, previous, moduli, source)
        previous, current = (current, advanced)
    return (current, previous)


def solution(mesh):
    in_specs = (
        P(),
        P(),
        P(),
        P(),
        P(),
        P(),
        P(("gx", "gy")),
        P(("gx", "gy")),
        P(None, "gx", "gy", None),
        P(None, "gx", "gy", None),
        P(None, "gx", "gy", None),
    )
    out_specs = (P(None, "gx", "gy", None), P(None, "gx", "gy", None))
    return jax.shard_map(shards, mesh=mesh, in_specs=in_specs, out_specs=out_specs, check_vma=False)
```

```python
import math

import jax
import jax.numpy as jnp
from jax import lax
from jax.sharding import PartitionSpec as P
from jax.experimental import pallas as pl
from jax.experimental.pallas import tpu as pltpu
import functools

F = 128
NK = 1024
NR = 2048
ND = 32
STEPS = 4
TSTART = 32


step_depth = 0.25


def padded_2(block, sides, width):
    for axis, dim in sides:
        count = lax.axis_size(axis)
        forward = [(i, i + 1) for i in range(count - 1)]
        backward = [(target, source) for source, target in forward]
        low = lax.ppermute(
            lax.slice_in_dim(block, block.shape[dim] - width, None, axis=dim), axis, forward
        )
        high = lax.ppermute(lax.slice_in_dim(block, 0, width, axis=dim), axis, backward)
        block = jnp.concatenate([low, block, high], axis=dim)
    return block


YPAD = 8


def step_kernel(u_ref, xlo_ref, xhi_ref, ylo_ref, yhi_ref, prev_ref, mod_ref, src_ref, out_ref, up_ref, *, bx):
    i = pl.program_id(0)
    nx, ny = u_ref.shape[1], u_ref.shape[2]

    @pl.when(i == 0)
    def _():
        for c in range(3):
            def fill(x, carry):
                up_ref[c, x + 2, pl.ds(YPAD, ny), :] = u_ref[c, x]
                return carry

            lax.fori_loop(0, nx, fill, 0)
        up_ref[:, 0:2, pl.ds(YPAD, ny), :] = xlo_ref[...]
        up_ref[:, nx + 2:nx + 4, pl.ds(YPAD, ny), :] = xhi_ref[...]
        up_ref[:, :, pl.ds(YPAD - 2, 2), :] = ylo_ref[...]
        up_ref[:, :, pl.ds(YPAD + ny, 2), :] = yhi_ref[...]

    depth = out_ref.shape[3]
    lane = lax.broadcasted_iota(jnp.int32, (8, depth), 1)
    masks = {dz: (lane + dz >= 0) & (lane + dz < depth) for dz in (-2, -1, 1, 2)}

    def zs(v, dz):
        if dz == 0:
            return v
        return jnp.where(masks[dz], pltpu.roll(v, (-dz) % depth, 1), 0.0)

    def plane(p, carry):
        xp = i * bx + p + 2
        for g in range(out_ref.shape[2] // 8):
            def load(c, dx, dy):
                return up_ref[c, xp + dx, pl.ds(8 * g + YPAD + dy, 8), :]

            lam = mod_ref[0, p, pl.ds(8 * g, 8), :]
            mu = mod_ref[1, p, pl.ds(8 * g, 8), :]
            stiff = lam + 2.0 * mu
            coup = lam + mu
            centers = [load(c, 0, 0) for c in range(3)]

            def curv(c, axis):
                center = centers[c]
                near = None
                far = None
                for off in (-1, 1, -2, 2):
                    if axis == 0:
                        t = load(c, off, 0)
                    elif axis == 1:
                        t = load(c, 0, off)
                    else:
                        t = zs(center, off)
                    if abs(off) == 1:
                        near = t if near is None else near + t
                    else:
                        far = t if far is None else far + t
                return 16.0 * near - far - 30.0 * center

            def mixed(p_c, a, b):
                if 2 in (a, b):
                    n = a + b - 2
                    d = [0, 0]
                    d[n] = 1
                    step = load(p_c, d[0], d[1])
                    d[n] = -1
                    diff = step - load(p_c, d[0], d[1])
                    return zs(diff, 1) - zs(diff, -1)
                acc = None
                for sa in (1, -1):
                    for sb in (1, -1):
                        d = [0, 0, 0]
                        d[a] = sa
                        d[b] = sb
                        t = zs(load(p_c, d[0], d[1]), d[2])
                        if acc is None:
                            acc = t
                        elif sa * sb > 0:
                            acc = acc + t
                        else:
                            acc = acc - t
                return acc

            for c in range(3):
                others = [e for e in range(3) if e != c]
                second = stiff * curv(c, c) + mu * (curv(c, others[0]) + curv(c, others[1]))
                cross = mixed(others[0], c, others[0]) + mixed(others[1], c, others[1])
                upd = second * (1.0 / 12.0) + coup * (cross * 0.25)
                prev = prev_ref[c, p, pl.ds(8 * g, 8), :]
                src = src_ref[c, p, pl.ds(8 * g, 8), :]
                out_ref[c, p, pl.ds(8 * g, 8), :] = (2.0 * centers[c] - prev + upd) + src
        return carry

    lax.fori_loop(0, bx, plane, 0)


def elastic_step(u, xlo, xhi, ylo, yhi, prev, moduli, sources, bx=8):
    _, nx, ny, depth = u.shape
    kernel = functools.partial(step_kernel, bx=bx)
    block = lambda i: (0, i, 0, 0)
    whole = lambda i: (0, 0, 0, 0)
    return pl.pallas_call(
        kernel,
        grid=(nx // bx,),
        in_specs=[
            pl.BlockSpec(u.shape, whole),
            pl.BlockSpec(xlo.shape, whole),
            pl.BlockSpec(xhi.shape, whole),
            pl.BlockSpec(ylo.shape, whole),
            pl.BlockSpec(yhi.shape, whole),
            pl.BlockSpec((3, bx, ny, depth), block),
            pl.BlockSpec((2, bx, ny, depth), block),
            pl.BlockSpec((3, bx, ny, depth), block),
        ],
        out_specs=pl.BlockSpec((3, bx, ny, depth), block),
        out_shape=jax.ShapeDtypeStruct((3, nx, ny, depth), jnp.float32),
        scratch_shapes=[pltpu.VMEM((3, nx + 4, ny + 2 * YPAD, depth), jnp.float32)],
        compiler_params=pltpu.CompilerParams(dimension_semantics=("arbitrary",)),
    )(u, xlo, xhi, ylo, yhi, prev, moduli, sources)


def halos(block, width):
    size_x = lax.axis_size("gx")
    size_y = lax.axis_size("gy")
    nx, ny = block.shape[1], block.shape[2]
    forward_x = [(i, i + 1) for i in range(size_x - 1)]
    backward_x = [(t, s) for s, t in forward_x]
    xlo = lax.ppermute(block[:, nx - width:], "gx", forward_x)
    xhi = lax.ppermute(block[:, :width], "gx", backward_x)
    forward_y = [(i, i + 1) for i in range(size_y - 1)]
    backward_y = [(t, s) for s, t in forward_y]
    rows = lambda sl: jnp.concatenate([xlo[:, :, sl], block[:, :, sl], xhi[:, :, sl]], axis=1)
    ylo = lax.ppermute(rows(slice(ny - width, ny)), "gy", forward_y)
    yhi = lax.ppermute(rows(slice(0, width)), "gy", backward_y)
    return xlo, xhi, ylo, yhi


def level_table(values, layer_of_level):
    one_hot = (
        layer_of_level[:, None] == jnp.arange(values.shape[0], dtype=jnp.int32)[None, :]
    ).astype(jnp.float32)
    return jnp.sum(one_hot * values[None, :], axis=1)


def wave_kernel(angular, slowness, rigidity, damping, count_k):
    wavenum = (jnp.arange(count_k, dtype=jnp.float32) + 0.5) * (4.0 / count_k)
    spread = angular[None, :, None] * slowness[:, None, None]
    vertical = jnp.sqrt(wavenum[None, None, :] * wavenum[None, None, :] + spread * spread)
    impedance = rigidity[:, None, None] * vertical
    beneath = jnp.concatenate([impedance[1:], impedance[-1:]], axis=0)
    reflect = (impedance - beneath) / (impedance + beneath)
    fading = jnp.exp(-2.0 * step_depth * vertical * damping[:, None, None])
    two_way = 2.0 * step_depth * vertical
    trip_re = fading * jnp.cos(two_way)
    trip_im = -fading * jnp.sin(two_way)

    def upward(state_in, layer_data):
        refl_re, refl_im = state_in
        coefficient, along_re, along_im = layer_data
        upper_re = coefficient + refl_re
        lower_re = 1.0 + coefficient * refl_re
        lower_im = coefficient * refl_im
        magnitude = lower_re * lower_re + lower_im * lower_im
        ratio_re = (upper_re * lower_re + refl_im * lower_im) / magnitude
        ratio_im = (refl_im * lower_re - upper_re * lower_im) / magnitude
        fresh_re = along_re * ratio_re - along_im * ratio_im
        fresh_im = along_re * ratio_im + along_im * ratio_re
        return ((fresh_re, fresh_im), (fresh_re, fresh_im))

    bottom = jnp.zeros(vertical.shape[1:], jnp.float32)
    _, (refl_re, refl_im) = lax.scan(
        upward, (bottom, bottom), (reflect, trip_re, trip_im), reverse=True
    )
    travel = step_depth * vertical
    phases = jnp.cumsum(travel, axis=0) - travel
    absorbed = travel * damping[:, None, None]
    losses = jnp.cumsum(absorbed, axis=0) - absorbed
    down_size = jnp.exp(-losses)
    down_re = down_size * jnp.cos(phases)
    down_im = -down_size * jnp.sin(phases)
    weight = 1.0 / math.sqrt(count_k)
    kernel_re = weight * (down_re * (1.0 + refl_re) - down_im * refl_im)
    kernel_im = weight * (down_re * refl_im + down_im * (1.0 + refl_re))
    return jnp.transpose(jnp.stack([kernel_re, kernel_im]), (0, 2, 1, 3))


def offset_basis(count_k, count_r):
    modulus = count_k * count_r // 2
    low_count = 64
    odd_index = 2 * jnp.arange(count_k, dtype=jnp.int32) + 1
    high = jnp.arange(count_r // low_count, dtype=jnp.int32) * low_count
    low = jnp.arange(low_count, dtype=jnp.int32)
    scale = 2.0 * math.pi / modulus
    high_angle = (odd_index[:, None] * high[None, :] % modulus).astype(jnp.float32) * scale
    low_angle = (odd_index[:, None] * low[None, :] % modulus).astype(jnp.float32) * scale
    cos_h, sin_h = jnp.cos(high_angle), jnp.sin(high_angle)
    cos_l, sin_l = jnp.cos(low_angle), jnp.sin(low_angle)
    basis = cos_h[:, :, None] * cos_l[:, None, :] - sin_h[:, :, None] * sin_l[:, None, :]
    basis = basis.reshape(count_k, count_r).astype(jnp.bfloat16)
    return lax.optimization_barrier(basis)


def time_basis(freq_ids, count_f, count_steps, first_time):
    period = 2 * count_f
    times = first_time + jnp.arange(count_steps, dtype=jnp.int32)
    turns = (freq_ids[None, :] + 1) * times[:, None] % period
    angles = turns.astype(jnp.float32) * (2.0 * math.pi / period)
    weight = 1.0 / math.sqrt(count_f)
    return jnp.stack([weight * jnp.cos(angles), -weight * jnp.sin(angles)], axis=1)


def shifted(grid_block, step_x, step_y, step_z):
    width_x = grid_block.shape[0] - 4
    width_y = grid_block.shape[1] - 4
    width_z = grid_block.shape[2] - 4
    return grid_block[
        2 + step_x : 2 + step_x + width_x,
        2 + step_y : 2 + step_y + width_y,
        2 + step_z : 2 + step_z + width_z,
    ]


def curvature(grid_block, first_axis):
    summed = None
    for offset, factor in [(-2, -1.0), (-1, 16.0), (0, -30.0), (1, 16.0), (2, -1.0)]:
        moves = tuple((offset if index == first_axis else 0 for index in range(3)))
        contrib = factor * shifted(grid_block, moves[0], moves[1], moves[2])
        summed = contrib if summed is None else summed + contrib
    return summed / 12.0


def mixed(grid_block, first_axis, second_axis):
    summed = None
    for sign_a, sign_b, factor in [(1, 1, 1.0), (1, -1, -1.0), (-1, 1, -1.0), (-1, -1, 1.0)]:
        moves = tuple(
            (
                sign_a if index == first_axis else sign_b if index == second_axis else 0
                for index in range(3)
            )
        )
        contrib = factor * shifted(grid_block, moves[0], moves[1], moves[2])
        summed = contrib if summed is None else summed + contrib
    return summed / 4.0


def elastic(padded, moduli):
    first_lame = moduli[0]
    shear_mod = moduli[1]
    stiffness = first_lame + 2.0 * shear_mod
    coupling = first_lame + shear_mod
    result = []
    for component in range(3):
        update = stiffness * curvature(padded[component], component)
        for partner in range(3):
            if partner != component:
                update = update + shear_mod * curvature(padded[component], partner)
                update = update + coupling * mixed(padded[partner], component, partner)
        result.append(update)
    return jnp.stack(result)


def shards(
    layer_slowness,
    layer_rigidity,
    layer_damping,
    layer_of_level,
    slot_offset,
    slot_level,
    slot_target,
    live_count,
    moduli,
    field_old,
    field_now,
):
    size_gx = lax.axis_size("gx")
    size_gy = lax.axis_size("gy")
    groups = size_gx * size_gy
    per_device = F // groups
    device = lax.axis_index("gx") * size_gy + lax.axis_index("gy")
    freq_ids = device * per_device + jnp.arange(per_device, dtype=jnp.int32)
    angular = (freq_ids + 1).astype(jnp.float32) * (4.0 / F)
    slowness = level_table(layer_slowness, layer_of_level)
    rigidity = level_table(layer_rigidity, layer_of_level)
    damping = level_table(layer_damping, layer_of_level)
    kernel = wave_kernel(angular, slowness, rigidity, damping, NK).astype(jnp.bfloat16)
    cosines = offset_basis(NK, NR)
    spectrum_table = jnp.dot(
        kernel.reshape(2 * per_device * ND, NK), cosines, preferred_element_type=jnp.float32
    )
    table_rounded = spectrum_table.astype(jnp.bfloat16)
    all_slots = slot_offset.shape[0]
    width = math.gcd(all_slots, 4096)
    count_blocks = all_slots // width
    offset_blocks = slot_offset.reshape(count_blocks, width)
    level_blocks = slot_level.reshape(count_blocks, width)

    def select_block(pair):
        offsets, levels = pair
        offset_hot = (jnp.arange(NR, dtype=jnp.int32)[:, None] == offsets[None, :]).astype(
            jnp.bfloat16
        )
        rows = jnp.dot(table_rounded, offset_hot, preferred_element_type=jnp.float32).reshape(
            2, per_device, ND, width
        )
        level_hot = (jnp.arange(ND, dtype=jnp.int32)[:, None] == levels[None, :]).astype(
            jnp.float32
        )
        return jnp.sum(rows * level_hot[None, None, :, :], axis=2)

    selected = lax.map(select_block, (offset_blocks, level_blocks))
    spectra = (
        jnp.transpose(selected, (1, 2, 0, 3)).reshape(2, per_device, all_slots).astype(jnp.bfloat16)
    )
    slots_dev = slot_target.shape[0]
    occupied = (jnp.arange(slots_dev, dtype=jnp.int32) < live_count[0]).astype(jnp.float32)
    parcel = spectra.reshape(2, per_device, groups, slots_dev)
    arrived = lax.all_to_all(parcel, ("gx", "gy"), split_axis=2, concat_axis=1, tiled=True)
    freq_order = jnp.arange(F, dtype=jnp.int32)
    waveforms = time_basis(freq_order, F, STEPS, TSTART).reshape(STEPS, 2 * F)
    traces = jnp.dot(
        waveforms,
        arrived.reshape(2 * F, slots_dev).astype(jnp.float32),
        precision=lax.Precision.HIGHEST,
    )
    block_x = field_now.shape[1]
    block_y = field_now.shape[2]
    depth = field_now.shape[3]
    columns = slot_target // depth
    layer_z = slot_target % depth
    weighted = traces * occupied[None, :]
    column_hot = (
        jnp.arange(3 * block_x * block_y, dtype=jnp.int32)[:, None] == columns[None, :]
    ).astype(jnp.float32)
    depth_hot = (layer_z[:, None] == jnp.arange(depth, dtype=jnp.int32)[None, :]).astype(
        jnp.float32
    )
    previous, current = (field_old, field_now)
    for instant in range(STEPS):
        spread = weighted[instant][:, None] * depth_hot
        source = jnp.dot(column_hot, spread, precision=lax.Precision.HIGHEST)
        source = source.reshape(3, block_x, block_y, depth)
        xlo, xhi, ylo, yhi = halos(current, 2)
        advanced = elastic_step(current, xlo, xhi, ylo, yhi, previous, moduli, source)
        previous, current = (current, advanced)
    return (current, previous)


def solution(mesh):
    in_specs = (
        P(),
        P(),
        P(),
        P(),
        P(),
        P(),
        P(("gx", "gy")),
        P(("gx", "gy")),
        P(None, "gx", "gy", None),
        P(None, "gx", "gy", None),
        P(None, "gx", "gy", None),
    )
    out_specs = (P(None, "gx", "gy", None), P(None, "gx", "gy", None))
    return jax.shard_map(shards, mesh=mesh, in_specs=in_specs, out_specs=out_specs, check_vma=False)
```

```python
import math

import jax
import jax.numpy as jnp
from jax import lax
from jax.sharding import PartitionSpec as P
from jax.experimental import pallas as pl
from jax.experimental.pallas import tpu as pltpu
import functools

F = 128
NK = 1024
NR = 2048
ND = 32
STEPS = 4
TSTART = 32


step_depth = 0.25


def padded_2(block, sides, width):
    for axis, dim in sides:
        count = lax.axis_size(axis)
        forward = [(i, i + 1) for i in range(count - 1)]
        backward = [(target, source) for source, target in forward]
        low = lax.ppermute(
            lax.slice_in_dim(block, block.shape[dim] - width, None, axis=dim), axis, forward
        )
        high = lax.ppermute(lax.slice_in_dim(block, 0, width, axis=dim), axis, backward)
        block = jnp.concatenate([low, block, high], axis=dim)
    return block


YPAD = 8


def step_kernel(u_ref, xlo_ref, xhi_ref, ylo_ref, yhi_ref, prev_ref, mod_ref, src_ref, out_ref, up_ref, *, bx):
    i = pl.program_id(0)
    nx, ny = u_ref.shape[1], u_ref.shape[2]

    @pl.when(i == 0)
    def _():
        for c in range(3):
            def fill(x, carry):
                up_ref[c, x + 2, pl.ds(YPAD, ny), :] = u_ref[c, x]
                return carry

            lax.fori_loop(0, nx, fill, 0)
        up_ref[:, 0:2, pl.ds(YPAD, ny), :] = xlo_ref[...]
        up_ref[:, nx + 2:nx + 4, pl.ds(YPAD, ny), :] = xhi_ref[...]
        up_ref[:, :, pl.ds(YPAD - 2, 2), :] = ylo_ref[...]
        up_ref[:, :, pl.ds(YPAD + ny, 2), :] = yhi_ref[...]

    depth = out_ref.shape[3]
    lane = lax.broadcasted_iota(jnp.int32, (8, depth), 1)
    masks = {dz: (lane + dz >= 0) & (lane + dz < depth) for dz in (-2, -1, 1, 2)}

    def zs(v, dz):
        if dz == 0:
            return v
        return jnp.where(masks[dz], pltpu.roll(v, (-dz) % depth, 1), 0.0)

    def plane(p, carry):
        xp = i * bx + p + 2
        for g in range(out_ref.shape[2] // 8):
            def load(c, dx, dy):
                return up_ref[c, xp + dx, pl.ds(8 * g + YPAD + dy, 8), :]

            lam = mod_ref[0, p, pl.ds(8 * g, 8), :]
            mu = mod_ref[1, p, pl.ds(8 * g, 8), :]
            stiff = lam + 2.0 * mu
            coup = lam + mu
            centers = [load(c, 0, 0) for c in range(3)]

            def curv(c, axis):
                center = centers[c]
                near = None
                far = None
                for off in (-1, 1, -2, 2):
                    if axis == 0:
                        t = load(c, off, 0)
                    elif axis == 1:
                        t = load(c, 0, off)
                    else:
                        t = zs(center, off)
                    if abs(off) == 1:
                        near = t if near is None else near + t
                    else:
                        far = t if far is None else far + t
                return 16.0 * near - far - 30.0 * center

            def mixed(p_c, a, b):
                if 2 in (a, b):
                    n = a + b - 2
                    d = [0, 0]
                    d[n] = 1
                    step = load(p_c, d[0], d[1])
                    d[n] = -1
                    diff = step - load(p_c, d[0], d[1])
                    return zs(diff, 1) - zs(diff, -1)
                acc = None
                for sa in (1, -1):
                    for sb in (1, -1):
                        d = [0, 0, 0]
                        d[a] = sa
                        d[b] = sb
                        t = zs(load(p_c, d[0], d[1]), d[2])
                        if acc is None:
                            acc = t
                        elif sa * sb > 0:
                            acc = acc + t
                        else:
                            acc = acc - t
                return acc

            for c in range(3):
                others = [e for e in range(3) if e != c]
                second = stiff * curv(c, c) + mu * (curv(c, others[0]) + curv(c, others[1]))
                cross = mixed(others[0], c, others[0]) + mixed(others[1], c, others[1])
                upd = second * (1.0 / 12.0) + coup * (cross * 0.25)
                prev = prev_ref[c, p, pl.ds(8 * g, 8), :]
                src = src_ref[c, p, pl.ds(8 * g, 8), :]
                out_ref[c, p, pl.ds(8 * g, 8), :] = (2.0 * centers[c] - prev + upd) + src
        return carry

    lax.fori_loop(0, bx, plane, 0)


def elastic_step(u, xlo, xhi, ylo, yhi, prev, moduli, sources, bx=8):
    _, nx, ny, depth = u.shape
    kernel = functools.partial(step_kernel, bx=bx)
    block = lambda i: (0, i, 0, 0)
    whole = lambda i: (0, 0, 0, 0)
    return pl.pallas_call(
        kernel,
        grid=(nx // bx,),
        in_specs=[
            pl.BlockSpec(u.shape, whole),
            pl.BlockSpec(xlo.shape, whole),
            pl.BlockSpec(xhi.shape, whole),
            pl.BlockSpec(ylo.shape, whole),
            pl.BlockSpec(yhi.shape, whole),
            pl.BlockSpec((3, bx, ny, depth), block),
            pl.BlockSpec((2, bx, ny, depth), block),
            pl.BlockSpec((3, bx, ny, depth), block),
        ],
        out_specs=pl.BlockSpec((3, bx, ny, depth), block),
        out_shape=jax.ShapeDtypeStruct((3, nx, ny, depth), jnp.float32),
        scratch_shapes=[pltpu.VMEM((3, nx + 4, ny + 2 * YPAD, depth), jnp.float32)],
        compiler_params=pltpu.CompilerParams(dimension_semantics=("arbitrary",)),
    )(u, xlo, xhi, ylo, yhi, prev, moduli, sources)


def halos(block, width):
    size_x = lax.axis_size("gx")
    size_y = lax.axis_size("gy")
    nx, ny = block.shape[1], block.shape[2]

    def send(piece, axis, pairs):
        return lax.ppermute(piece.astype(jnp.bfloat16), axis, pairs).astype(jnp.float32)

    forward_x = [(i, i + 1) for i in range(size_x - 1)]
    backward_x = [(t, s) for s, t in forward_x]
    xlo = send(block[:, nx - width:], "gx", forward_x)
    xhi = send(block[:, :width], "gx", backward_x)
    forward_y = [(i, i + 1) for i in range(size_y - 1)]
    backward_y = [(t, s) for s, t in forward_y]
    rows = lambda sl: jnp.concatenate([xlo[:, :, sl], block[:, :, sl], xhi[:, :, sl]], axis=1)
    ylo = send(rows(slice(ny - width, ny)), "gy", forward_y)
    yhi = send(rows(slice(0, width)), "gy", backward_y)
    return xlo, xhi, ylo, yhi


def level_table(values, layer_of_level):
    one_hot = (
        layer_of_level[:, None] == jnp.arange(values.shape[0], dtype=jnp.int32)[None, :]
    ).astype(jnp.float32)
    return jnp.sum(one_hot * values[None, :], axis=1)


def wave_kernel(angular, slowness, rigidity, damping, count_k):
    wavenum = (jnp.arange(count_k, dtype=jnp.float32) + 0.5) * (4.0 / count_k)
    spread = angular[None, :, None] * slowness[:, None, None]
    vertical = jnp.sqrt(wavenum[None, None, :] * wavenum[None, None, :] + spread * spread)
    impedance = rigidity[:, None, None] * vertical
    beneath = jnp.concatenate([impedance[1:], impedance[-1:]], axis=0)
    reflect = (impedance - beneath) / (impedance + beneath)
    fading = jnp.exp(-2.0 * step_depth * vertical * damping[:, None, None])
    two_way = 2.0 * step_depth * vertical
    trip_re = fading * jnp.cos(two_way)
    trip_im = -fading * jnp.sin(two_way)

    def upward(state_in, layer_data):
        refl_re, refl_im = state_in
        coefficient, along_re, along_im = layer_data
        upper_re = coefficient + refl_re
        lower_re = 1.0 + coefficient * refl_re
        lower_im = coefficient * refl_im
        magnitude = lower_re * lower_re + lower_im * lower_im
        ratio_re = (upper_re * lower_re + refl_im * lower_im) / magnitude
        ratio_im = (refl_im * lower_re - upper_re * lower_im) / magnitude
        fresh_re = along_re * ratio_re - along_im * ratio_im
        fresh_im = along_re * ratio_im + along_im * ratio_re
        return ((fresh_re, fresh_im), (fresh_re, fresh_im))

    bottom = jnp.zeros(vertical.shape[1:], jnp.float32)
    _, (refl_re, refl_im) = lax.scan(
        upward, (bottom, bottom), (reflect, trip_re, trip_im), reverse=True
    )
    travel = step_depth * vertical
    phases = jnp.cumsum(travel, axis=0) - travel
    absorbed = travel * damping[:, None, None]
    losses = jnp.cumsum(absorbed, axis=0) - absorbed
    down_size = jnp.exp(-losses)
    down_re = down_size * jnp.cos(phases)
    down_im = -down_size * jnp.sin(phases)
    weight = 1.0 / math.sqrt(count_k)
    kernel_re = weight * (down_re * (1.0 + refl_re) - down_im * refl_im)
    kernel_im = weight * (down_re * refl_im + down_im * (1.0 + refl_re))
    return jnp.transpose(jnp.stack([kernel_re, kernel_im]), (0, 2, 1, 3))


def offset_basis(count_k, count_r):
    modulus = count_k * count_r // 2
    low_count = 64
    odd_index = 2 * jnp.arange(count_k, dtype=jnp.int32) + 1
    high = jnp.arange(count_r // low_count, dtype=jnp.int32) * low_count
    low = jnp.arange(low_count, dtype=jnp.int32)
    scale = 2.0 * math.pi / modulus
    high_angle = (odd_index[:, None] * high[None, :] % modulus).astype(jnp.float32) * scale
    low_angle = (odd_index[:, None] * low[None, :] % modulus).astype(jnp.float32) * scale
    cos_h, sin_h = jnp.cos(high_angle), jnp.sin(high_angle)
    cos_l, sin_l = jnp.cos(low_angle), jnp.sin(low_angle)
    basis = cos_h[:, :, None] * cos_l[:, None, :] - sin_h[:, :, None] * sin_l[:, None, :]
    basis = basis.reshape(count_k, count_r).astype(jnp.bfloat16)
    return lax.optimization_barrier(basis)


def time_basis(freq_ids, count_f, count_steps, first_time):
    period = 2 * count_f
    times = first_time + jnp.arange(count_steps, dtype=jnp.int32)
    turns = (freq_ids[None, :] + 1) * times[:, None] % period
    angles = turns.astype(jnp.float32) * (2.0 * math.pi / period)
    weight = 1.0 / math.sqrt(count_f)
    return jnp.stack([weight * jnp.cos(angles), -weight * jnp.sin(angles)], axis=1)


def shifted(grid_block, step_x, step_y, step_z):
    width_x = grid_block.shape[0] - 4
    width_y = grid_block.shape[1] - 4
    width_z = grid_block.shape[2] - 4
    return grid_block[
        2 + step_x : 2 + step_x + width_x,
        2 + step_y : 2 + step_y + width_y,
        2 + step_z : 2 + step_z + width_z,
    ]


def curvature(grid_block, first_axis):
    summed = None
    for offset, factor in [(-2, -1.0), (-1, 16.0), (0, -30.0), (1, 16.0), (2, -1.0)]:
        moves = tuple((offset if index == first_axis else 0 for index in range(3)))
        contrib = factor * shifted(grid_block, moves[0], moves[1], moves[2])
        summed = contrib if summed is None else summed + contrib
    return summed / 12.0


def mixed(grid_block, first_axis, second_axis):
    summed = None
    for sign_a, sign_b, factor in [(1, 1, 1.0), (1, -1, -1.0), (-1, 1, -1.0), (-1, -1, 1.0)]:
        moves = tuple(
            (
                sign_a if index == first_axis else sign_b if index == second_axis else 0
                for index in range(3)
            )
        )
        contrib = factor * shifted(grid_block, moves[0], moves[1], moves[2])
        summed = contrib if summed is None else summed + contrib
    return summed / 4.0


def elastic(padded, moduli):
    first_lame = moduli[0]
    shear_mod = moduli[1]
    stiffness = first_lame + 2.0 * shear_mod
    coupling = first_lame + shear_mod
    result = []
    for component in range(3):
        update = stiffness * curvature(padded[component], component)
        for partner in range(3):
            if partner != component:
                update = update + shear_mod * curvature(padded[component], partner)
                update = update + coupling * mixed(padded[partner], component, partner)
        result.append(update)
    return jnp.stack(result)


def shards(
    layer_slowness,
    layer_rigidity,
    layer_damping,
    layer_of_level,
    slot_offset,
    slot_level,
    slot_target,
    live_count,
    moduli,
    field_old,
    field_now,
):
    size_gx = lax.axis_size("gx")
    size_gy = lax.axis_size("gy")
    groups = size_gx * size_gy
    per_device = F // groups
    device = lax.axis_index("gx") * size_gy + lax.axis_index("gy")
    freq_ids = device * per_device + jnp.arange(per_device, dtype=jnp.int32)
    angular = (freq_ids + 1).astype(jnp.float32) * (4.0 / F)
    slowness = level_table(layer_slowness, layer_of_level)
    rigidity = level_table(layer_rigidity, layer_of_level)
    damping = level_table(layer_damping, layer_of_level)
    kernel = wave_kernel(angular, slowness, rigidity, damping, NK).astype(jnp.bfloat16)
    cosines = offset_basis(NK, NR)
    spectrum_table = jnp.dot(
        kernel.reshape(2 * per_device * ND, NK), cosines, preferred_element_type=jnp.float32
    )
    table_rounded = spectrum_table.astype(jnp.bfloat16)
    all_slots = slot_offset.shape[0]
    width = math.gcd(all_slots, 4096)
    count_blocks = all_slots // width
    offset_blocks = slot_offset.reshape(count_blocks, width)
    level_blocks = slot_level.reshape(count_blocks, width)

    def select_block(pair):
        offsets, levels = pair
        offset_hot = (jnp.arange(NR, dtype=jnp.int32)[:, None] == offsets[None, :]).astype(
            jnp.bfloat16
        )
        rows = jnp.dot(table_rounded, offset_hot, preferred_element_type=jnp.float32).reshape(
            2, per_device, ND, width
        )
        level_hot = (jnp.arange(ND, dtype=jnp.int32)[:, None] == levels[None, :]).astype(
            jnp.float32
        )
        return jnp.sum(rows * level_hot[None, None, :, :], axis=2)

    selected = lax.map(select_block, (offset_blocks, level_blocks))
    spectra = (
        jnp.transpose(selected, (1, 2, 0, 3)).reshape(2, per_device, all_slots).astype(jnp.bfloat16)
    )
    slots_dev = slot_target.shape[0]
    occupied = (jnp.arange(slots_dev, dtype=jnp.int32) < live_count[0]).astype(jnp.float32)
    parcel = spectra.reshape(2, per_device, groups, slots_dev)
    arrived = lax.all_to_all(parcel, ("gx", "gy"), split_axis=2, concat_axis=1, tiled=True)
    freq_order = jnp.arange(F, dtype=jnp.int32)
    waveforms = time_basis(freq_order, F, STEPS, TSTART).reshape(STEPS, 2 * F)
    traces = jnp.dot(
        waveforms,
        arrived.reshape(2 * F, slots_dev).astype(jnp.float32),
        precision=lax.Precision.HIGHEST,
    )
    block_x = field_now.shape[1]
    block_y = field_now.shape[2]
    depth = field_now.shape[3]
    columns = slot_target // depth
    layer_z = slot_target % depth
    weighted = traces * occupied[None, :]
    column_hot = (
        jnp.arange(3 * block_x * block_y, dtype=jnp.int32)[:, None] == columns[None, :]
    ).astype(jnp.float32)
    depth_hot = (layer_z[:, None] == jnp.arange(depth, dtype=jnp.int32)[None, :]).astype(
        jnp.float32
    )
    previous, current = (field_old, field_now)
    for instant in range(STEPS):
        spread = weighted[instant][:, None] * depth_hot
        source = jnp.dot(column_hot, spread, precision=lax.Precision.HIGHEST)
        source = source.reshape(3, block_x, block_y, depth)
        xlo, xhi, ylo, yhi = halos(current, 2)
        advanced = elastic_step(current, xlo, xhi, ylo, yhi, previous, moduli, source)
        previous, current = (current, advanced)
    return (current, previous)


def solution(mesh):
    in_specs = (
        P(),
        P(),
        P(),
        P(),
        P(),
        P(),
        P(("gx", "gy")),
        P(("gx", "gy")),
        P(None, "gx", "gy", None),
        P(None, "gx", "gy", None),
        P(None, "gx", "gy", None),
    )
    out_specs = (P(None, "gx", "gy", None), P(None, "gx", "gy", None))
    return jax.shard_map(shards, mesh=mesh, in_specs=in_specs, out_specs=out_specs, check_vma=False)
```

```python
import math

import jax
import jax.numpy as jnp
from jax import lax
from jax.sharding import PartitionSpec as P
from jax.experimental import pallas as pl
from jax.experimental.pallas import tpu as pltpu
import functools

F = 128
NK = 1024
NR = 2048
ND = 32
STEPS = 4
TSTART = 32


step_depth = 0.25


def padded_2(block, sides, width):
    for axis, dim in sides:
        count = lax.axis_size(axis)
        forward = [(i, i + 1) for i in range(count - 1)]
        backward = [(target, source) for source, target in forward]
        low = lax.ppermute(
            lax.slice_in_dim(block, block.shape[dim] - width, None, axis=dim), axis, forward
        )
        high = lax.ppermute(lax.slice_in_dim(block, 0, width, axis=dim), axis, backward)
        block = jnp.concatenate([low, block, high], axis=dim)
    return block


YPAD = 8


def step_kernel(u_ref, xlo_ref, xhi_ref, ylo_ref, yhi_ref, prev_ref, mod_ref, src_ref, out_ref,
                fxlo_ref, fxhi_ref, rylo_ref, ryhi_ref, up_ref, *, bx):
    i = pl.program_id(0)
    nx, ny = u_ref.shape[1], u_ref.shape[2]

    @pl.when(i == 0)
    def _():
        for c in range(3):
            def fill(x, carry):
                up_ref[c, x + 2, pl.ds(YPAD, ny), :] = u_ref[c, x]
                return carry

            lax.fori_loop(0, nx, fill, 0)
        up_ref[:, 0:2, pl.ds(YPAD, ny), :] = xlo_ref[...]
        up_ref[:, nx + 2:nx + 4, pl.ds(YPAD, ny), :] = xhi_ref[...]
        up_ref[:, :, pl.ds(YPAD - 2, 2), :] = ylo_ref[...]
        up_ref[:, :, pl.ds(YPAD + ny, 2), :] = yhi_ref[...]

    depth = out_ref.shape[3]
    lane = lax.broadcasted_iota(jnp.int32, (8, depth), 1)
    masks = {dz: (lane + dz >= 0) & (lane + dz < depth) for dz in (-2, -1, 1, 2)}

    def zs(v, dz):
        if dz == 0:
            return v
        return jnp.where(masks[dz], pltpu.roll(v, (-dz) % depth, 1), 0.0)

    groups = out_ref.shape[2] // 8

    def plane(p, carry):
        xg = i * bx + p
        xp = xg + 2
        for g in range(groups):
            def load(c, dx, dy):
                return up_ref[c, xp + dx, pl.ds(8 * g + YPAD + dy, 8), :]

            lam = mod_ref[0, p, pl.ds(8 * g, 8), :]
            mu = mod_ref[1, p, pl.ds(8 * g, 8), :]
            stiff = lam + 2.0 * mu
            coup = lam + mu
            centers = [load(c, 0, 0) for c in range(3)]

            def curv(c, axis):
                center = centers[c]
                near = None
                far = None
                for off in (-1, 1, -2, 2):
                    if axis == 0:
                        t = load(c, off, 0)
                    elif axis == 1:
                        t = load(c, 0, off)
                    else:
                        t = zs(center, off)
                    if abs(off) == 1:
                        near = t if near is None else near + t
                    else:
                        far = t if far is None else far + t
                return 16.0 * near - far - 30.0 * center

            def mixed(p_c, a, b):
                if 2 in (a, b):
                    n = a + b - 2
                    d = [0, 0]
                    d[n] = 1
                    step = load(p_c, d[0], d[1])
                    d[n] = -1
                    diff = step - load(p_c, d[0], d[1])
                    return zs(diff, 1) - zs(diff, -1)
                acc = None
                for sa in (1, -1):
                    for sb in (1, -1):
                        d = [0, 0, 0]
                        d[a] = sa
                        d[b] = sb
                        t = zs(load(p_c, d[0], d[1]), d[2])
                        if acc is None:
                            acc = t
                        elif sa * sb > 0:
                            acc = acc + t
                        else:
                            acc = acc - t
                return acc

            for c in range(3):
                others = [e for e in range(3) if e != c]
                second = stiff * curv(c, c) + mu * (curv(c, others[0]) + curv(c, others[1]))
                cross = mixed(others[0], c, others[0]) + mixed(others[1], c, others[1])
                upd = second * (1.0 / 12.0) + coup * (cross * 0.25)
                prev = prev_ref[c, p, pl.ds(8 * g, 8), :]
                src = src_ref[c, p, pl.ds(8 * g, 8), :]
                fresh = (2.0 * centers[c] - prev + upd) + src
                out_ref[c, p, pl.ds(8 * g, 8), :] = fresh
                if g == 0:
                    rylo_ref[c, xg] = fresh[0:2]
                if g == groups - 1:
                    ryhi_ref[c, xg] = fresh[6:8]

                @pl.when(xg < 2)
                def _():
                    fxlo_ref[c, jnp.minimum(xg, 1), pl.ds(8 * g, 8), :] = fresh

                @pl.when(xg >= nx - 2)
                def _():
                    fxhi_ref[c, jnp.maximum(xg - (nx - 2), 0), pl.ds(8 * g, 8), :] = fresh
        return carry

    lax.fori_loop(0, bx, plane, 0)


def elastic_step(u, xlo, xhi, ylo, yhi, prev, moduli, sources, bx=8):
    _, nx, ny, depth = u.shape
    kernel = functools.partial(step_kernel, bx=bx)
    block = lambda i: (0, i, 0, 0)
    whole = lambda i: (0, 0, 0, 0)
    return pl.pallas_call(
        kernel,
        grid=(nx // bx,),
        in_specs=[
            pl.BlockSpec(u.shape, whole),
            pl.BlockSpec(xlo.shape, whole),
            pl.BlockSpec(xhi.shape, whole),
            pl.BlockSpec(ylo.shape, whole),
            pl.BlockSpec(yhi.shape, whole),
            pl.BlockSpec((3, bx, ny, depth), block),
            pl.BlockSpec((2, bx, ny, depth), block),
            pl.BlockSpec((3, bx, ny, depth), block),
        ],
        out_specs=[
            pl.BlockSpec((3, bx, ny, depth), block),
            pl.BlockSpec((3, 2, ny, depth), whole),
            pl.BlockSpec((3, 2, ny, depth), whole),
            pl.BlockSpec((3, nx, 2, depth), whole),
            pl.BlockSpec((3, nx, 2, depth), whole),
        ],
        out_shape=[
            jax.ShapeDtypeStruct((3, nx, ny, depth), jnp.float32),
            jax.ShapeDtypeStruct((3, 2, ny, depth), jnp.float32),
            jax.ShapeDtypeStruct((3, 2, ny, depth), jnp.float32),
            jax.ShapeDtypeStruct((3, nx, 2, depth), jnp.float32),
            jax.ShapeDtypeStruct((3, nx, 2, depth), jnp.float32),
        ],
        scratch_shapes=[pltpu.VMEM((3, nx + 4, ny + 2 * YPAD, depth), jnp.float32)],
        compiler_params=pltpu.CompilerParams(dimension_semantics=("arbitrary",)),
    )(u, xlo, xhi, ylo, yhi, prev, moduli, sources)


def faces_of(block, width):
    nx, ny = block.shape[1], block.shape[2]
    return (block[:, :width], block[:, nx - width:], block[:, :, :width], block[:, :, ny - width:])


def halos(faces, width):
    size_x = lax.axis_size("gx")
    size_y = lax.axis_size("gy")
    face_xlo, face_xhi, row_lo, row_hi = faces
    ny = face_xlo.shape[2]
    forward_x = [(i, i + 1) for i in range(size_x - 1)]
    backward_x = [(t, s) for s, t in forward_x]
    xlo = lax.ppermute(face_xhi, "gx", forward_x)
    xhi = lax.ppermute(face_xlo, "gx", backward_x)
    forward_y = [(i, i + 1) for i in range(size_y - 1)]
    backward_y = [(t, s) for s, t in forward_y]
    rows = lambda sl, mid: jnp.concatenate([xlo[:, :, sl], mid, xhi[:, :, sl]], axis=1)
    ylo = lax.ppermute(rows(slice(ny - width, ny), row_hi), "gy", forward_y)
    yhi = lax.ppermute(rows(slice(0, width), row_lo), "gy", backward_y)
    return xlo, xhi, ylo, yhi


def level_table(values, layer_of_level):
    one_hot = (
        layer_of_level[:, None] == jnp.arange(values.shape[0], dtype=jnp.int32)[None, :]
    ).astype(jnp.float32)
    return jnp.sum(one_hot * values[None, :], axis=1)


def wave_kernel(angular, slowness, rigidity, damping, count_k):
    wavenum = (jnp.arange(count_k, dtype=jnp.float32) + 0.5) * (4.0 / count_k)
    spread = angular[None, :, None] * slowness[:, None, None]
    vertical = jnp.sqrt(wavenum[None, None, :] * wavenum[None, None, :] + spread * spread)
    impedance = rigidity[:, None, None] * vertical
    beneath = jnp.concatenate([impedance[1:], impedance[-1:]], axis=0)
    reflect = (impedance - beneath) / (impedance + beneath)
    fading = jnp.exp(-2.0 * step_depth * vertical * damping[:, None, None])
    two_way = 2.0 * step_depth * vertical
    trip_re = fading * jnp.cos(two_way)
    trip_im = -fading * jnp.sin(two_way)

    def upward(state_in, layer_data):
        refl_re, refl_im = state_in
        coefficient, along_re, along_im = layer_data
        upper_re = coefficient + refl_re
        lower_re = 1.0 + coefficient * refl_re
        lower_im = coefficient * refl_im
        magnitude = lower_re * lower_re + lower_im * lower_im
        ratio_re = (upper_re * lower_re + refl_im * lower_im) / magnitude
        ratio_im = (refl_im * lower_re - upper_re * lower_im) / magnitude
        fresh_re = along_re * ratio_re - along_im * ratio_im
        fresh_im = along_re * ratio_im + along_im * ratio_re
        return ((fresh_re, fresh_im), (fresh_re, fresh_im))

    bottom = jnp.zeros(vertical.shape[1:], jnp.float32)
    _, (refl_re, refl_im) = lax.scan(
        upward, (bottom, bottom), (reflect, trip_re, trip_im), reverse=True
    )
    travel = step_depth * vertical
    phases = jnp.cumsum(travel, axis=0) - travel
    absorbed = travel * damping[:, None, None]
    losses = jnp.cumsum(absorbed, axis=0) - absorbed
    down_size = jnp.exp(-losses)
    down_re = down_size * jnp.cos(phases)
    down_im = -down_size * jnp.sin(phases)
    weight = 1.0 / math.sqrt(count_k)
    kernel_re = weight * (down_re * (1.0 + refl_re) - down_im * refl_im)
    kernel_im = weight * (down_re * refl_im + down_im * (1.0 + refl_re))
    return jnp.transpose(jnp.stack([kernel_re, kernel_im]), (0, 2, 1, 3))


def offset_basis(count_k, count_r):
    modulus = count_k * count_r // 2
    low_count = 64
    odd_index = 2 * jnp.arange(count_k, dtype=jnp.int32) + 1
    high = jnp.arange(count_r // low_count, dtype=jnp.int32) * low_count
    low = jnp.arange(low_count, dtype=jnp.int32)
    scale = 2.0 * math.pi / modulus
    high_angle = (odd_index[:, None] * high[None, :] % modulus).astype(jnp.float32) * scale
    low_angle = (odd_index[:, None] * low[None, :] % modulus).astype(jnp.float32) * scale
    cos_h, sin_h = jnp.cos(high_angle), jnp.sin(high_angle)
    cos_l, sin_l = jnp.cos(low_angle), jnp.sin(low_angle)
    basis = cos_h[:, :, None] * cos_l[:, None, :] - sin_h[:, :, None] * sin_l[:, None, :]
    basis = basis.reshape(count_k, count_r).astype(jnp.bfloat16)
    return lax.optimization_barrier(basis)


def time_basis(freq_ids, count_f, count_steps, first_time):
    period = 2 * count_f
    times = first_time + jnp.arange(count_steps, dtype=jnp.int32)
    turns = (freq_ids[None, :] + 1) * times[:, None] % period
    angles = turns.astype(jnp.float32) * (2.0 * math.pi / period)
    weight = 1.0 / math.sqrt(count_f)
    return jnp.stack([weight * jnp.cos(angles), -weight * jnp.sin(angles)], axis=1)


def shifted(grid_block, step_x, step_y, step_z):
    width_x = grid_block.shape[0] - 4
    width_y = grid_block.shape[1] - 4
    width_z = grid_block.shape[2] - 4
    return grid_block[
        2 + step_x : 2 + step_x + width_x,
        2 + step_y : 2 + step_y + width_y,
        2 + step_z : 2 + step_z + width_z,
    ]


def curvature(grid_block, first_axis):
    summed = None
    for offset, factor in [(-2, -1.0), (-1, 16.0), (0, -30.0), (1, 16.0), (2, -1.0)]:
        moves = tuple((offset if index == first_axis else 0 for index in range(3)))
        contrib = factor * shifted(grid_block, moves[0], moves[1], moves[2])
        summed = contrib if summed is None else summed + contrib
    return summed / 12.0


def mixed(grid_block, first_axis, second_axis):
    summed = None
    for sign_a, sign_b, factor in [(1, 1, 1.0), (1, -1, -1.0), (-1, 1, -1.0), (-1, -1, 1.0)]:
        moves = tuple(
            (
                sign_a if index == first_axis else sign_b if index == second_axis else 0
                for index in range(3)
            )
        )
        contrib = factor * shifted(grid_block, moves[0], moves[1], moves[2])
        summed = contrib if summed is None else summed + contrib
    return summed / 4.0


def elastic(padded, moduli):
    first_lame = moduli[0]
    shear_mod = moduli[1]
    stiffness = first_lame + 2.0 * shear_mod
    coupling = first_lame + shear_mod
    result = []
    for component in range(3):
        update = stiffness * curvature(padded[component], component)
        for partner in range(3):
            if partner != component:
                update = update + shear_mod * curvature(padded[component], partner)
                update = update + coupling * mixed(padded[partner], component, partner)
        result.append(update)
    return jnp.stack(result)


def shards(
    layer_slowness,
    layer_rigidity,
    layer_damping,
    layer_of_level,
    slot_offset,
    slot_level,
    slot_target,
    live_count,
    moduli,
    field_old,
    field_now,
):
    size_gx = lax.axis_size("gx")
    size_gy = lax.axis_size("gy")
    groups = size_gx * size_gy
    per_device = F // groups
    device = lax.axis_index("gx") * size_gy + lax.axis_index("gy")
    freq_ids = device * per_device + jnp.arange(per_device, dtype=jnp.int32)
    angular = (freq_ids + 1).astype(jnp.float32) * (4.0 / F)
    slowness = level_table(layer_slowness, layer_of_level)
    rigidity = level_table(layer_rigidity, layer_of_level)
    damping = level_table(layer_damping, layer_of_level)
    kernel = wave_kernel(angular, slowness, rigidity, damping, NK).astype(jnp.bfloat16)
    cosines = offset_basis(NK, NR)
    spectrum_table = jnp.dot(
        kernel.reshape(2 * per_device * ND, NK), cosines, preferred_element_type=jnp.float32
    )
    table_rounded = spectrum_table.astype(jnp.bfloat16)
    all_slots = slot_offset.shape[0]
    width = math.gcd(all_slots, 4096)
    count_blocks = all_slots // width
    offset_blocks = slot_offset.reshape(count_blocks, width)
    level_blocks = slot_level.reshape(count_blocks, width)

    def select_block(pair):
        offsets, levels = pair
        offset_hot = (jnp.arange(NR, dtype=jnp.int32)[:, None] == offsets[None, :]).astype(
            jnp.bfloat16
        )
        rows = jnp.dot(table_rounded, offset_hot, preferred_element_type=jnp.float32).reshape(
            2, per_device, ND, width
        )
        level_hot = (jnp.arange(ND, dtype=jnp.int32)[:, None] == levels[None, :]).astype(
            jnp.float32
        )
        return jnp.sum(rows * level_hot[None, None, :, :], axis=2)

    selected = lax.map(select_block, (offset_blocks, level_blocks))
    spectra = (
        jnp.transpose(selected, (1, 2, 0, 3)).reshape(2, per_device, all_slots).astype(jnp.bfloat16)
    )
    slots_dev = slot_target.shape[0]
    occupied = (jnp.arange(slots_dev, dtype=jnp.int32) < live_count[0]).astype(jnp.float32)
    parcel = spectra.reshape(2, per_device, groups, slots_dev)
    arrived = lax.all_to_all(parcel, ("gx", "gy"), split_axis=2, concat_axis=1, tiled=True)
    freq_order = jnp.arange(F, dtype=jnp.int32)
    waveforms = time_basis(freq_order, F, STEPS, TSTART).reshape(STEPS, 2 * F)
    traces = jnp.dot(
        waveforms,
        arrived.reshape(2 * F, slots_dev).astype(jnp.float32),
        precision=lax.Precision.HIGHEST,
    )
    block_x = field_now.shape[1]
    block_y = field_now.shape[2]
    depth = field_now.shape[3]
    columns = slot_target // depth
    layer_z = slot_target % depth
    weighted = traces * occupied[None, :]
    column_hot = (
        jnp.arange(3 * block_x * block_y, dtype=jnp.int32)[:, None] == columns[None, :]
    ).astype(jnp.float32)
    depth_hot = (layer_z[:, None] == jnp.arange(depth, dtype=jnp.int32)[None, :]).astype(
        jnp.float32
    )
    previous, current = (field_old, field_now)
    faces = faces_of(field_now, 2)
    for instant in range(STEPS):
        spread = weighted[instant][:, None] * depth_hot
        source = jnp.dot(column_hot, spread, precision=lax.Precision.HIGHEST)
        source = source.reshape(3, block_x, block_y, depth)
        xlo, xhi, ylo, yhi = halos(faces, 2)
        advanced, *faces = elastic_step(current, xlo, xhi, ylo, yhi, previous, moduli, source)
        previous, current = (current, advanced)
    return (current, previous)


def solution(mesh):
    in_specs = (
        P(),
        P(),
        P(),
        P(),
        P(),
        P(),
        P(("gx", "gy")),
        P(("gx", "gy")),
        P(None, "gx", "gy", None),
        P(None, "gx", "gy", None),
        P(None, "gx", "gy", None),
    )
    out_specs = (P(None, "gx", "gy", None), P(None, "gx", "gy", None))
    return jax.shard_map(shards, mesh=mesh, in_specs=in_specs, out_specs=out_specs, check_vma=False)
```

```python
import math

import jax
import jax.numpy as jnp
from jax import lax
from jax.sharding import PartitionSpec as P
from jax.experimental import pallas as pl
from jax.experimental.pallas import tpu as pltpu
import functools

F = 128
NK = 1024
NR = 2048
ND = 32
STEPS = 4
TSTART = 32


step_depth = 0.25


def padded_2(block, sides, width):
    for axis, dim in sides:
        count = lax.axis_size(axis)
        forward = [(i, i + 1) for i in range(count - 1)]
        backward = [(target, source) for source, target in forward]
        low = lax.ppermute(
            lax.slice_in_dim(block, block.shape[dim] - width, None, axis=dim), axis, forward
        )
        high = lax.ppermute(lax.slice_in_dim(block, 0, width, axis=dim), axis, backward)
        block = jnp.concatenate([low, block, high], axis=dim)
    return block


YPAD = 8


def step_kernel(u_ref, xlo_ref, xhi_ref, ylo_ref, yhi_ref, prev_ref, mod_ref, src_ref, out_ref,
                fxlo_ref, fxhi_ref, rylo_ref, ryhi_ref, up_ref, *, bx):
    i = pl.program_id(0)
    nx, ny = u_ref.shape[1], u_ref.shape[2]

    @pl.when(i == 0)
    def _():
        for c in range(3):
            def fill(x, carry):
                up_ref[c, x + 2, pl.ds(YPAD, ny), :] = u_ref[c, x]
                return carry

            lax.fori_loop(0, nx, fill, 0)
        up_ref[:, 0:2, pl.ds(YPAD, ny), :] = xlo_ref[...]
        up_ref[:, nx + 2:nx + 4, pl.ds(YPAD, ny), :] = xhi_ref[...]
        up_ref[:, :, pl.ds(YPAD - 2, 2), :] = ylo_ref[...]
        up_ref[:, :, pl.ds(YPAD + ny, 2), :] = yhi_ref[...]

    depth = out_ref.shape[3]
    lane = lax.broadcasted_iota(jnp.int32, (8, depth), 1)
    masks = {dz: (lane + dz >= 0) & (lane + dz < depth) for dz in (-2, -1, 1, 2)}

    def zs(v, dz):
        if dz == 0:
            return v
        return jnp.where(masks[dz], pltpu.roll(v, (-dz) % depth, 1), 0.0)

    groups = out_ref.shape[2] // 8

    def plane(p, carry):
        xp = i * bx + p + 2
        for g in range(groups):
            def load(c, dx, dy):
                return up_ref[c, xp + dx, pl.ds(8 * g + YPAD + dy, 8), :]

            lam = mod_ref[0, p, pl.ds(8 * g, 8), :]
            mu = mod_ref[1, p, pl.ds(8 * g, 8), :]
            stiff = lam + 2.0 * mu
            coup = lam + mu
            centers = [load(c, 0, 0) for c in range(3)]

            def curv(c, axis):
                center = centers[c]
                near = None
                far = None
                for off in (-1, 1, -2, 2):
                    if axis == 0:
                        t = load(c, off, 0)
                    elif axis == 1:
                        t = load(c, 0, off)
                    else:
                        t = zs(center, off)
                    if abs(off) == 1:
                        near = t if near is None else near + t
                    else:
                        far = t if far is None else far + t
                return 16.0 * near - far - 30.0 * center

            def mixed(p_c, a, b):
                if 2 in (a, b):
                    n = a + b - 2
                    d = [0, 0]
                    d[n] = 1
                    step = load(p_c, d[0], d[1])
                    d[n] = -1
                    diff = step - load(p_c, d[0], d[1])
                    return zs(diff, 1) - zs(diff, -1)
                acc = None
                for sa in (1, -1):
                    for sb in (1, -1):
                        d = [0, 0, 0]
                        d[a] = sa
                        d[b] = sb
                        t = zs(load(p_c, d[0], d[1]), d[2])
                        if acc is None:
                            acc = t
                        elif sa * sb > 0:
                            acc = acc + t
                        else:
                            acc = acc - t
                return acc

            for c in range(3):
                others = [e for e in range(3) if e != c]
                second = stiff * curv(c, c) + mu * (curv(c, others[0]) + curv(c, others[1]))
                cross = mixed(others[0], c, others[0]) + mixed(others[1], c, others[1])
                upd = second * (1.0 / 12.0) + coup * (cross * 0.25)
                prev = prev_ref[c, p, pl.ds(8 * g, 8), :]
                src = src_ref[c, p, pl.ds(8 * g, 8), :]
                out_ref[c, p, pl.ds(8 * g, 8), :] = (2.0 * centers[c] - prev + upd) + src
        return carry

    lax.fori_loop(0, bx, plane, 0)
    ny = out_ref.shape[2]
    rylo_ref[:, pl.ds(i * bx, bx)] = out_ref[:, :, 0:2, :]
    ryhi_ref[:, pl.ds(i * bx, bx)] = out_ref[:, :, ny - 2:ny, :]

    @pl.when(i == 0)
    def _():
        fxlo_ref[...] = out_ref[:, 0:2]

    @pl.when(i == pl.num_programs(0) - 1)
    def _():
        fxhi_ref[...] = out_ref[:, bx - 2:bx]


def elastic_step(u, xlo, xhi, ylo, yhi, prev, moduli, sources, bx=8):
    _, nx, ny, depth = u.shape
    kernel = functools.partial(step_kernel, bx=bx)
    block = lambda i: (0, i, 0, 0)
    whole = lambda i: (0, 0, 0, 0)
    return pl.pallas_call(
        kernel,
        grid=(nx // bx,),
        in_specs=[
            pl.BlockSpec(u.shape, whole),
            pl.BlockSpec(xlo.shape, whole),
            pl.BlockSpec(xhi.shape, whole),
            pl.BlockSpec(ylo.shape, whole),
            pl.BlockSpec(yhi.shape, whole),
            pl.BlockSpec((3, bx, ny, depth), block),
            pl.BlockSpec((2, bx, ny, depth), block),
            pl.BlockSpec((3, bx, ny, depth), block),
        ],
        out_specs=[
            pl.BlockSpec((3, bx, ny, depth), block),
            pl.BlockSpec((3, 2, ny, depth), whole),
            pl.BlockSpec((3, 2, ny, depth), whole),
            pl.BlockSpec((3, nx, 2, depth), whole),
            pl.BlockSpec((3, nx, 2, depth), whole),
        ],
        out_shape=[
            jax.ShapeDtypeStruct((3, nx, ny, depth), jnp.float32),
            jax.ShapeDtypeStruct((3, 2, ny, depth), jnp.float32),
            jax.ShapeDtypeStruct((3, 2, ny, depth), jnp.float32),
            jax.ShapeDtypeStruct((3, nx, 2, depth), jnp.float32),
            jax.ShapeDtypeStruct((3, nx, 2, depth), jnp.float32),
        ],
        scratch_shapes=[pltpu.VMEM((3, nx + 4, ny + 2 * YPAD, depth), jnp.float32)],
        compiler_params=pltpu.CompilerParams(dimension_semantics=("arbitrary",)),
    )(u, xlo, xhi, ylo, yhi, prev, moduli, sources)


def faces_of(block, width):
    nx, ny = block.shape[1], block.shape[2]
    return (block[:, :width], block[:, nx - width:], block[:, :, :width], block[:, :, ny - width:])


def halos(faces, width):
    size_x = lax.axis_size("gx")
    size_y = lax.axis_size("gy")
    face_xlo, face_xhi, row_lo, row_hi = faces
    ny = face_xlo.shape[2]
    forward_x = [(i, i + 1) for i in range(size_x - 1)]
    backward_x = [(t, s) for s, t in forward_x]
    xlo = lax.ppermute(face_xhi, "gx", forward_x)
    xhi = lax.ppermute(face_xlo, "gx", backward_x)
    forward_y = [(i, i + 1) for i in range(size_y - 1)]
    backward_y = [(t, s) for s, t in forward_y]
    rows = lambda sl, mid: jnp.concatenate([xlo[:, :, sl], mid, xhi[:, :, sl]], axis=1)
    ylo = lax.ppermute(rows(slice(ny - width, ny), row_hi), "gy", forward_y)
    yhi = lax.ppermute(rows(slice(0, width), row_lo), "gy", backward_y)
    return xlo, xhi, ylo, yhi


def level_table(values, layer_of_level):
    one_hot = (
        layer_of_level[:, None] == jnp.arange(values.shape[0], dtype=jnp.int32)[None, :]
    ).astype(jnp.float32)
    return jnp.sum(one_hot * values[None, :], axis=1)


def wave_kernel(angular, slowness, rigidity, damping, count_k):
    wavenum = (jnp.arange(count_k, dtype=jnp.float32) + 0.5) * (4.0 / count_k)
    spread = angular[None, :, None] * slowness[:, None, None]
    vertical = jnp.sqrt(wavenum[None, None, :] * wavenum[None, None, :] + spread * spread)
    impedance = rigidity[:, None, None] * vertical
    beneath = jnp.concatenate([impedance[1:], impedance[-1:]], axis=0)
    reflect = (impedance - beneath) / (impedance + beneath)
    fading = jnp.exp(-2.0 * step_depth * vertical * damping[:, None, None])
    two_way = 2.0 * step_depth * vertical
    trip_re = fading * jnp.cos(two_way)
    trip_im = -fading * jnp.sin(two_way)

    def upward(state_in, layer_data):
        refl_re, refl_im = state_in
        coefficient, along_re, along_im = layer_data
        upper_re = coefficient + refl_re
        lower_re = 1.0 + coefficient * refl_re
        lower_im = coefficient * refl_im
        magnitude = lower_re * lower_re + lower_im * lower_im
        ratio_re = (upper_re * lower_re + refl_im * lower_im) / magnitude
        ratio_im = (refl_im * lower_re - upper_re * lower_im) / magnitude
        fresh_re = along_re * ratio_re - along_im * ratio_im
        fresh_im = along_re * ratio_im + along_im * ratio_re
        return ((fresh_re, fresh_im), (fresh_re, fresh_im))

    bottom = jnp.zeros(vertical.shape[1:], jnp.float32)
    _, (refl_re, refl_im) = lax.scan(
        upward, (bottom, bottom), (reflect, trip_re, trip_im), reverse=True
    )
    travel = step_depth * vertical
    phases = jnp.cumsum(travel, axis=0) - travel
    absorbed = travel * damping[:, None, None]
    losses = jnp.cumsum(absorbed, axis=0) - absorbed
    down_size = jnp.exp(-losses)
    down_re = down_size * jnp.cos(phases)
    down_im = -down_size * jnp.sin(phases)
    weight = 1.0 / math.sqrt(count_k)
    kernel_re = weight * (down_re * (1.0 + refl_re) - down_im * refl_im)
    kernel_im = weight * (down_re * refl_im + down_im * (1.0 + refl_re))
    return jnp.transpose(jnp.stack([kernel_re, kernel_im]), (0, 2, 1, 3))


def offset_basis(count_k, count_r):
    modulus = count_k * count_r // 2
    low_count = 64
    odd_index = 2 * jnp.arange(count_k, dtype=jnp.int32) + 1
    high = jnp.arange(count_r // low_count, dtype=jnp.int32) * low_count
    low = jnp.arange(low_count, dtype=jnp.int32)
    scale = 2.0 * math.pi / modulus
    high_angle = (odd_index[:, None] * high[None, :] % modulus).astype(jnp.float32) * scale
    low_angle = (odd_index[:, None] * low[None, :] % modulus).astype(jnp.float32) * scale
    cos_h, sin_h = jnp.cos(high_angle), jnp.sin(high_angle)
    cos_l, sin_l = jnp.cos(low_angle), jnp.sin(low_angle)
    basis = cos_h[:, :, None] * cos_l[:, None, :] - sin_h[:, :, None] * sin_l[:, None, :]
    basis = basis.reshape(count_k, count_r).astype(jnp.bfloat16)
    return lax.optimization_barrier(basis)


def time_basis(freq_ids, count_f, count_steps, first_time):
    period = 2 * count_f
    times = first_time + jnp.arange(count_steps, dtype=jnp.int32)
    turns = (freq_ids[None, :] + 1) * times[:, None] % period
    angles = turns.astype(jnp.float32) * (2.0 * math.pi / period)
    weight = 1.0 / math.sqrt(count_f)
    return jnp.stack([weight * jnp.cos(angles), -weight * jnp.sin(angles)], axis=1)


def shifted(grid_block, step_x, step_y, step_z):
    width_x = grid_block.shape[0] - 4
    width_y = grid_block.shape[1] - 4
    width_z = grid_block.shape[2] - 4
    return grid_block[
        2 + step_x : 2 + step_x + width_x,
        2 + step_y : 2 + step_y + width_y,
        2 + step_z : 2 + step_z + width_z,
    ]


def curvature(grid_block, first_axis):
    summed = None
    for offset, factor in [(-2, -1.0), (-1, 16.0), (0, -30.0), (1, 16.0), (2, -1.0)]:
        moves = tuple((offset if index == first_axis else 0 for index in range(3)))
        contrib = factor * shifted(grid_block, moves[0], moves[1], moves[2])
        summed = contrib if summed is None else summed + contrib
    return summed / 12.0


def mixed(grid_block, first_axis, second_axis):
    summed = None
    for sign_a, sign_b, factor in [(1, 1, 1.0), (1, -1, -1.0), (-1, 1, -1.0), (-1, -1, 1.0)]:
        moves = tuple(
            (
                sign_a if index == first_axis else sign_b if index == second_axis else 0
                for index in range(3)
            )
        )
        contrib = factor * shifted(grid_block, moves[0], moves[1], moves[2])
        summed = contrib if summed is None else summed + contrib
    return summed / 4.0


def elastic(padded, moduli):
    first_lame = moduli[0]
    shear_mod = moduli[1]
    stiffness = first_lame + 2.0 * shear_mod
    coupling = first_lame + shear_mod
    result = []
    for component in range(3):
        update = stiffness * curvature(padded[component], component)
        for partner in range(3):
            if partner != component:
                update = update + shear_mod * curvature(padded[component], partner)
                update = update + coupling * mixed(padded[partner], component, partner)
        result.append(update)
    return jnp.stack(result)


def shards(
    layer_slowness,
    layer_rigidity,
    layer_damping,
    layer_of_level,
    slot_offset,
    slot_level,
    slot_target,
    live_count,
    moduli,
    field_old,
    field_now,
):
    size_gx = lax.axis_size("gx")
    size_gy = lax.axis_size("gy")
    groups = size_gx * size_gy
    per_device = F // groups
    device = lax.axis_index("gx") * size_gy + lax.axis_index("gy")
    freq_ids = device * per_device + jnp.arange(per_device, dtype=jnp.int32)
    angular = (freq_ids + 1).astype(jnp.float32) * (4.0 / F)
    slowness = level_table(layer_slowness, layer_of_level)
    rigidity = level_table(layer_rigidity, layer_of_level)
    damping = level_table(layer_damping, layer_of_level)
    kernel = wave_kernel(angular, slowness, rigidity, damping, NK).astype(jnp.bfloat16)
    cosines = offset_basis(NK, NR)
    spectrum_table = jnp.dot(
        kernel.reshape(2 * per_device * ND, NK), cosines, preferred_element_type=jnp.float32
    )
    table_rounded = spectrum_table.astype(jnp.bfloat16)
    all_slots = slot_offset.shape[0]
    width = math.gcd(all_slots, 4096)
    count_blocks = all_slots // width
    offset_blocks = slot_offset.reshape(count_blocks, width)
    level_blocks = slot_level.reshape(count_blocks, width)

    def select_block(pair):
        offsets, levels = pair
        offset_hot = (jnp.arange(NR, dtype=jnp.int32)[:, None] == offsets[None, :]).astype(
            jnp.bfloat16
        )
        rows = jnp.dot(table_rounded, offset_hot, preferred_element_type=jnp.float32).reshape(
            2, per_device, ND, width
        )
        level_hot = (jnp.arange(ND, dtype=jnp.int32)[:, None] == levels[None, :]).astype(
            jnp.float32
        )
        return jnp.sum(rows * level_hot[None, None, :, :], axis=2)

    selected = lax.map(select_block, (offset_blocks, level_blocks))
    spectra = (
        jnp.transpose(selected, (1, 2, 0, 3)).reshape(2, per_device, all_slots).astype(jnp.bfloat16)
    )
    slots_dev = slot_target.shape[0]
    occupied = (jnp.arange(slots_dev, dtype=jnp.int32) < live_count[0]).astype(jnp.float32)
    parcel = spectra.reshape(2, per_device, groups, slots_dev)
    arrived = lax.all_to_all(parcel, ("gx", "gy"), split_axis=2, concat_axis=1, tiled=True)
    freq_order = jnp.arange(F, dtype=jnp.int32)
    waveforms = time_basis(freq_order, F, STEPS, TSTART).reshape(STEPS, 2 * F)
    traces = jnp.dot(
        waveforms,
        arrived.reshape(2 * F, slots_dev).astype(jnp.float32),
        precision=lax.Precision.HIGHEST,
    )
    block_x = field_now.shape[1]
    block_y = field_now.shape[2]
    depth = field_now.shape[3]
    columns = slot_target // depth
    layer_z = slot_target % depth
    weighted = traces * occupied[None, :]
    column_hot = (
        jnp.arange(3 * block_x * block_y, dtype=jnp.int32)[:, None] == columns[None, :]
    ).astype(jnp.float32)
    depth_hot = (layer_z[:, None] == jnp.arange(depth, dtype=jnp.int32)[None, :]).astype(
        jnp.float32
    )
    previous, current = (field_old, field_now)
    faces = faces_of(field_now, 2)
    for instant in range(STEPS):
        spread = weighted[instant][:, None] * depth_hot
        source = jnp.dot(column_hot, spread, precision=lax.Precision.HIGHEST)
        source = source.reshape(3, block_x, block_y, depth)
        xlo, xhi, ylo, yhi = halos(faces, 2)
        advanced, *faces = elastic_step(current, xlo, xhi, ylo, yhi, previous, moduli, source)
        previous, current = (current, advanced)
    return (current, previous)


def solution(mesh):
    in_specs = (
        P(),
        P(),
        P(),
        P(),
        P(),
        P(),
        P(("gx", "gy")),
        P(("gx", "gy")),
        P(None, "gx", "gy", None),
        P(None, "gx", "gy", None),
        P(None, "gx", "gy", None),
    )
    out_specs = (P(None, "gx", "gy", None), P(None, "gx", "gy", None))
    return jax.shard_map(shards, mesh=mesh, in_specs=in_specs, out_specs=out_specs, check_vma=False)
```

```python
import math

import jax
import jax.numpy as jnp
from jax import lax
from jax.sharding import PartitionSpec as P
from jax.experimental import pallas as pl
from jax.experimental.pallas import tpu as pltpu
import functools

F = 128
NK = 1024
NR = 2048
ND = 32
STEPS = 4
TSTART = 32


step_depth = 0.25


def padded_2(block, sides, width):
    for axis, dim in sides:
        count = lax.axis_size(axis)
        forward = [(i, i + 1) for i in range(count - 1)]
        backward = [(target, source) for source, target in forward]
        low = lax.ppermute(
            lax.slice_in_dim(block, block.shape[dim] - width, None, axis=dim), axis, forward
        )
        high = lax.ppermute(lax.slice_in_dim(block, 0, width, axis=dim), axis, backward)
        block = jnp.concatenate([low, block, high], axis=dim)
    return block


YPAD = 8


def step_kernel(u_ref, xlo_ref, xhi_ref, ylo_ref, yhi_ref, prev_ref, mod_ref, src_ref, out_ref, up_ref, sem, *, bx):
    i = pl.program_id(0)
    nx, ny = u_ref.shape[1], u_ref.shape[2]

    @pl.when(i == 0)
    def _():
        fill = pltpu.make_async_copy(u_ref, up_ref.at[:, pl.ds(2, nx), pl.ds(YPAD, ny), :], sem)
        fill.start()
        up_ref[:, 0:2, pl.ds(YPAD, ny), :] = xlo_ref[...]
        up_ref[:, nx + 2:nx + 4, pl.ds(YPAD, ny), :] = xhi_ref[...]
        up_ref[:, :, pl.ds(YPAD - 2, 2), :] = ylo_ref[...]
        up_ref[:, :, pl.ds(YPAD + ny, 2), :] = yhi_ref[...]
        fill.wait()

    depth = out_ref.shape[3]
    lane = lax.broadcasted_iota(jnp.int32, (8, depth), 1)
    masks = {dz: (lane + dz >= 0) & (lane + dz < depth) for dz in (-2, -1, 1, 2)}

    def zs(v, dz):
        if dz == 0:
            return v
        return jnp.where(masks[dz], pltpu.roll(v, (-dz) % depth, 1), 0.0)

    def plane(p, carry):
        xp = i * bx + p + 2
        for g in range(out_ref.shape[2] // 8):
            def load(c, dx, dy):
                return up_ref[c, xp + dx, pl.ds(8 * g + YPAD + dy, 8), :]

            lam = mod_ref[0, p, pl.ds(8 * g, 8), :]
            mu = mod_ref[1, p, pl.ds(8 * g, 8), :]
            stiff = lam + 2.0 * mu
            coup = lam + mu
            centers = [load(c, 0, 0) for c in range(3)]

            def curv(c, axis):
                center = centers[c]
                near = None
                far = None
                for off in (-1, 1, -2, 2):
                    if axis == 0:
                        t = load(c, off, 0)
                    elif axis == 1:
                        t = load(c, 0, off)
                    else:
                        t = zs(center, off)
                    if abs(off) == 1:
                        near = t if near is None else near + t
                    else:
                        far = t if far is None else far + t
                return 16.0 * near - far - 30.0 * center

            def mixed(p_c, a, b):
                if 2 in (a, b):
                    n = a + b - 2
                    d = [0, 0]
                    d[n] = 1
                    step = load(p_c, d[0], d[1])
                    d[n] = -1
                    diff = step - load(p_c, d[0], d[1])
                    return zs(diff, 1) - zs(diff, -1)
                acc = None
                for sa in (1, -1):
                    for sb in (1, -1):
                        d = [0, 0, 0]
                        d[a] = sa
                        d[b] = sb
                        t = zs(load(p_c, d[0], d[1]), d[2])
                        if acc is None:
                            acc = t
                        elif sa * sb > 0:
                            acc = acc + t
                        else:
                            acc = acc - t
                return acc

            for c in range(3):
                others = [e for e in range(3) if e != c]
                second = stiff * curv(c, c) + mu * (curv(c, others[0]) + curv(c, others[1]))
                cross = mixed(others[0], c, others[0]) + mixed(others[1], c, others[1])
                upd = second * (1.0 / 12.0) + coup * (cross * 0.25)
                prev = prev_ref[c, p, pl.ds(8 * g, 8), :]
                src = src_ref[c, p, pl.ds(8 * g, 8), :]
                out_ref[c, p, pl.ds(8 * g, 8), :] = (2.0 * centers[c] - prev + upd) + src
        return carry

    lax.fori_loop(0, bx, plane, 0)


def elastic_step(u, xlo, xhi, ylo, yhi, prev, moduli, sources, bx=8):
    _, nx, ny, depth = u.shape
    kernel = functools.partial(step_kernel, bx=bx)
    block = lambda i: (0, i, 0, 0)
    whole = lambda i: (0, 0, 0, 0)
    return pl.pallas_call(
        kernel,
        grid=(nx // bx,),
        in_specs=[
            pl.BlockSpec(memory_space=pl.ANY),
            pl.BlockSpec(xlo.shape, whole),
            pl.BlockSpec(xhi.shape, whole),
            pl.BlockSpec(ylo.shape, whole),
            pl.BlockSpec(yhi.shape, whole),
            pl.BlockSpec((3, bx, ny, depth), block),
            pl.BlockSpec((2, bx, ny, depth), block),
            pl.BlockSpec((3, bx, ny, depth), block),
        ],
        out_specs=pl.BlockSpec((3, bx, ny, depth), block),
        out_shape=jax.ShapeDtypeStruct((3, nx, ny, depth), jnp.float32),
        scratch_shapes=[
            pltpu.VMEM((3, nx + 4, ny + 2 * YPAD, depth), jnp.float32),
            pltpu.SemaphoreType.DMA(()),
        ],
        compiler_params=pltpu.CompilerParams(dimension_semantics=("arbitrary",)),
    )(u, xlo, xhi, ylo, yhi, prev, moduli, sources)


def halos(block, width):
    size_x = lax.axis_size("gx")
    size_y = lax.axis_size("gy")
    nx, ny = block.shape[1], block.shape[2]
    forward_x = [(i, i + 1) for i in range(size_x - 1)]
    backward_x = [(t, s) for s, t in forward_x]
    xlo = lax.ppermute(block[:, nx - width:], "gx", forward_x)
    xhi = lax.ppermute(block[:, :width], "gx", backward_x)
    forward_y = [(i, i + 1) for i in range(size_y - 1)]
    backward_y = [(t, s) for s, t in forward_y]
    rows = lambda sl: jnp.concatenate([xlo[:, :, sl], block[:, :, sl], xhi[:, :, sl]], axis=1)
    ylo = lax.ppermute(rows(slice(ny - width, ny)), "gy", forward_y)
    yhi = lax.ppermute(rows(slice(0, width)), "gy", backward_y)
    return xlo, xhi, ylo, yhi


def level_table(values, layer_of_level):
    one_hot = (
        layer_of_level[:, None] == jnp.arange(values.shape[0], dtype=jnp.int32)[None, :]
    ).astype(jnp.float32)
    return jnp.sum(one_hot * values[None, :], axis=1)


def wave_kernel(angular, slowness, rigidity, damping, count_k):
    wavenum = (jnp.arange(count_k, dtype=jnp.float32) + 0.5) * (4.0 / count_k)
    spread = angular[None, :, None] * slowness[:, None, None]
    vertical = jnp.sqrt(wavenum[None, None, :] * wavenum[None, None, :] + spread * spread)
    impedance = rigidity[:, None, None] * vertical
    beneath = jnp.concatenate([impedance[1:], impedance[-1:]], axis=0)
    reflect = (impedance - beneath) / (impedance + beneath)
    fading = jnp.exp(-2.0 * step_depth * vertical * damping[:, None, None])
    two_way = 2.0 * step_depth * vertical
    trip_re = fading * jnp.cos(two_way)
    trip_im = -fading * jnp.sin(two_way)

    def upward(state_in, layer_data):
        refl_re, refl_im = state_in
        coefficient, along_re, along_im = layer_data
        upper_re = coefficient + refl_re
        lower_re = 1.0 + coefficient * refl_re
        lower_im = coefficient * refl_im
        magnitude = lower_re * lower_re + lower_im * lower_im
        ratio_re = (upper_re * lower_re + refl_im * lower_im) / magnitude
        ratio_im = (refl_im * lower_re - upper_re * lower_im) / magnitude
        fresh_re = along_re * ratio_re - along_im * ratio_im
        fresh_im = along_re * ratio_im + along_im * ratio_re
        return ((fresh_re, fresh_im), (fresh_re, fresh_im))

    bottom = jnp.zeros(vertical.shape[1:], jnp.float32)
    _, (refl_re, refl_im) = lax.scan(
        upward, (bottom, bottom), (reflect, trip_re, trip_im), reverse=True
    )
    travel = step_depth * vertical
    phases = jnp.cumsum(travel, axis=0) - travel
    absorbed = travel * damping[:, None, None]
    losses = jnp.cumsum(absorbed, axis=0) - absorbed
    down_size = jnp.exp(-losses)
    down_re = down_size * jnp.cos(phases)
    down_im = -down_size * jnp.sin(phases)
    weight = 1.0 / math.sqrt(count_k)
    kernel_re = weight * (down_re * (1.0 + refl_re) - down_im * refl_im)
    kernel_im = weight * (down_re * refl_im + down_im * (1.0 + refl_re))
    return jnp.transpose(jnp.stack([kernel_re, kernel_im]), (0, 2, 1, 3))


def offset_basis(count_k, count_r):
    modulus = count_k * count_r // 2
    low_count = 64
    odd_index = 2 * jnp.arange(count_k, dtype=jnp.int32) + 1
    high = jnp.arange(count_r // low_count, dtype=jnp.int32) * low_count
    low = jnp.arange(low_count, dtype=jnp.int32)
    scale = 2.0 * math.pi / modulus
    high_angle = (odd_index[:, None] * high[None, :] % modulus).astype(jnp.float32) * scale
    low_angle = (odd_index[:, None] * low[None, :] % modulus).astype(jnp.float32) * scale
    cos_h, sin_h = jnp.cos(high_angle), jnp.sin(high_angle)
    cos_l, sin_l = jnp.cos(low_angle), jnp.sin(low_angle)
    basis = cos_h[:, :, None] * cos_l[:, None, :] - sin_h[:, :, None] * sin_l[:, None, :]
    basis = basis.reshape(count_k, count_r).astype(jnp.bfloat16)
    return lax.optimization_barrier(basis)


def time_basis(freq_ids, count_f, count_steps, first_time):
    period = 2 * count_f
    times = first_time + jnp.arange(count_steps, dtype=jnp.int32)
    turns = (freq_ids[None, :] + 1) * times[:, None] % period
    angles = turns.astype(jnp.float32) * (2.0 * math.pi / period)
    weight = 1.0 / math.sqrt(count_f)
    return jnp.stack([weight * jnp.cos(angles), -weight * jnp.sin(angles)], axis=1)


def shifted(grid_block, step_x, step_y, step_z):
    width_x = grid_block.shape[0] - 4
    width_y = grid_block.shape[1] - 4
    width_z = grid_block.shape[2] - 4
    return grid_block[
        2 + step_x : 2 + step_x + width_x,
        2 + step_y : 2 + step_y + width_y,
        2 + step_z : 2 + step_z + width_z,
    ]


def curvature(grid_block, first_axis):
    summed = None
    for offset, factor in [(-2, -1.0), (-1, 16.0), (0, -30.0), (1, 16.0), (2, -1.0)]:
        moves = tuple((offset if index == first_axis else 0 for index in range(3)))
        contrib = factor * shifted(grid_block, moves[0], moves[1], moves[2])
        summed = contrib if summed is None else summed + contrib
    return summed / 12.0


def mixed(grid_block, first_axis, second_axis):
    summed = None
    for sign_a, sign_b, factor in [(1, 1, 1.0), (1, -1, -1.0), (-1, 1, -1.0), (-1, -1, 1.0)]:
        moves = tuple(
            (
                sign_a if index == first_axis else sign_b if index == second_axis else 0
                for index in range(3)
            )
        )
        contrib = factor * shifted(grid_block, moves[0], moves[1], moves[2])
        summed = contrib if summed is None else summed + contrib
    return summed / 4.0


def elastic(padded, moduli):
    first_lame = moduli[0]
    shear_mod = moduli[1]
    stiffness = first_lame + 2.0 * shear_mod
    coupling = first_lame + shear_mod
    result = []
    for component in range(3):
        update = stiffness * curvature(padded[component], component)
        for partner in range(3):
            if partner != component:
                update = update + shear_mod * curvature(padded[component], partner)
                update = update + coupling * mixed(padded[partner], component, partner)
        result.append(update)
    return jnp.stack(result)


def shards(
    layer_slowness,
    layer_rigidity,
    layer_damping,
    layer_of_level,
    slot_offset,
    slot_level,
    slot_target,
    live_count,
    moduli,
    field_old,
    field_now,
):
    size_gx = lax.axis_size("gx")
    size_gy = lax.axis_size("gy")
    groups = size_gx * size_gy
    per_device = F // groups
    device = lax.axis_index("gx") * size_gy + lax.axis_index("gy")
    freq_ids = device * per_device + jnp.arange(per_device, dtype=jnp.int32)
    angular = (freq_ids + 1).astype(jnp.float32) * (4.0 / F)
    slowness = level_table(layer_slowness, layer_of_level)
    rigidity = level_table(layer_rigidity, layer_of_level)
    damping = level_table(layer_damping, layer_of_level)
    kernel = wave_kernel(angular, slowness, rigidity, damping, NK).astype(jnp.bfloat16)
    cosines = offset_basis(NK, NR)
    spectrum_table = jnp.dot(
        kernel.reshape(2 * per_device * ND, NK), cosines, preferred_element_type=jnp.float32
    )
    table_rounded = spectrum_table.astype(jnp.bfloat16)
    all_slots = slot_offset.shape[0]
    width = math.gcd(all_slots, 4096)
    count_blocks = all_slots // width
    offset_blocks = slot_offset.reshape(count_blocks, width)
    level_blocks = slot_level.reshape(count_blocks, width)

    def select_block(pair):
        offsets, levels = pair
        offset_hot = (jnp.arange(NR, dtype=jnp.int32)[:, None] == offsets[None, :]).astype(
            jnp.bfloat16
        )
        rows = jnp.dot(table_rounded, offset_hot, preferred_element_type=jnp.float32).reshape(
            2, per_device, ND, width
        )
        level_hot = (jnp.arange(ND, dtype=jnp.int32)[:, None] == levels[None, :]).astype(
            jnp.float32
        )
        return jnp.sum(rows * level_hot[None, None, :, :], axis=2)

    selected = lax.map(select_block, (offset_blocks, level_blocks))
    spectra = (
        jnp.transpose(selected, (1, 2, 0, 3)).reshape(2, per_device, all_slots).astype(jnp.bfloat16)
    )
    slots_dev = slot_target.shape[0]
    occupied = (jnp.arange(slots_dev, dtype=jnp.int32) < live_count[0]).astype(jnp.float32)
    parcel = spectra.reshape(2, per_device, groups, slots_dev)
    arrived = lax.all_to_all(parcel, ("gx", "gy"), split_axis=2, concat_axis=1, tiled=True)
    freq_order = jnp.arange(F, dtype=jnp.int32)
    waveforms = time_basis(freq_order, F, STEPS, TSTART).reshape(STEPS, 2 * F)
    traces = jnp.dot(
        waveforms,
        arrived.reshape(2 * F, slots_dev).astype(jnp.float32),
        precision=lax.Precision.HIGHEST,
    )
    block_x = field_now.shape[1]
    block_y = field_now.shape[2]
    depth = field_now.shape[3]
    columns = slot_target // depth
    layer_z = slot_target % depth
    weighted = traces * occupied[None, :]
    column_hot = (
        jnp.arange(3 * block_x * block_y, dtype=jnp.int32)[:, None] == columns[None, :]
    ).astype(jnp.float32)
    depth_hot = (layer_z[:, None] == jnp.arange(depth, dtype=jnp.int32)[None, :]).astype(
        jnp.float32
    )
    previous, current = (field_old, field_now)
    for instant in range(STEPS):
        spread = weighted[instant][:, None] * depth_hot
        source = jnp.dot(column_hot, spread, precision=lax.Precision.HIGHEST)
        source = source.reshape(3, block_x, block_y, depth)
        xlo, xhi, ylo, yhi = halos(current, 2)
        advanced = elastic_step(current, xlo, xhi, ylo, yhi, previous, moduli, source)
        previous, current = (current, advanced)
    return (current, previous)


def solution(mesh):
    in_specs = (
        P(),
        P(),
        P(),
        P(),
        P(),
        P(),
        P(("gx", "gy")),
        P(("gx", "gy")),
        P(None, "gx", "gy", None),
        P(None, "gx", "gy", None),
        P(None, "gx", "gy", None),
    )
    out_specs = (P(None, "gx", "gy", None), P(None, "gx", "gy", None))
    return jax.shard_map(shards, mesh=mesh, in_specs=in_specs, out_specs=out_specs, check_vma=False)
```

```python
import math

import jax
import jax.numpy as jnp
from jax import lax
from jax.sharding import PartitionSpec as P
from jax.experimental import pallas as pl
from jax.experimental.pallas import tpu as pltpu
import functools

F = 128
NK = 1024
NR = 2048
ND = 32
STEPS = 4
TSTART = 32


step_depth = 0.25


def padded_2(block, sides, width):
    for axis, dim in sides:
        count = lax.axis_size(axis)
        forward = [(i, i + 1) for i in range(count - 1)]
        backward = [(target, source) for source, target in forward]
        low = lax.ppermute(
            lax.slice_in_dim(block, block.shape[dim] - width, None, axis=dim), axis, forward
        )
        high = lax.ppermute(lax.slice_in_dim(block, 0, width, axis=dim), axis, backward)
        block = jnp.concatenate([low, block, high], axis=dim)
    return block


YPAD = 8


def step_kernel(u_ref, xlo_ref, xhi_ref, ylo_ref, yhi_ref, prev_ref, mod_ref, src_ref, out_ref, up_ref, *, bx):
    i = pl.program_id(0)
    nx, ny = u_ref.shape[1], u_ref.shape[2]

    @pl.when(i == 0)
    def _():
        for c in range(3):
            def fill(x, carry):
                up_ref[c, x + 2, pl.ds(YPAD, ny), :] = u_ref[c, x]
                return carry

            lax.fori_loop(0, nx, fill, 0)
        up_ref[:, 0:2, pl.ds(YPAD, ny), :] = xlo_ref[...]
        up_ref[:, nx + 2:nx + 4, pl.ds(YPAD, ny), :] = xhi_ref[...]
        up_ref[:, :, pl.ds(YPAD - 2, 2), :] = ylo_ref[...]
        up_ref[:, :, pl.ds(YPAD + ny, 2), :] = yhi_ref[...]

    depth = out_ref.shape[3]
    lane = lax.broadcasted_iota(jnp.int32, (8, depth), 1)
    masks = {dz: (lane + dz >= 0) & (lane + dz < depth) for dz in (-2, -1, 1, 2)}

    def zs(v, dz):
        if dz == 0:
            return v
        return jnp.where(masks[dz], pltpu.roll(v, (-dz) % depth, 1), 0.0)

    def plane(p, carry):
        xp = i * bx + p + 2
        for g in range(out_ref.shape[2] // 8):
            def load(c, dx, dy):
                return up_ref[c, xp + dx, pl.ds(8 * g + YPAD + dy, 8), :]

            lam = mod_ref[0, p, pl.ds(8 * g, 8), :]
            mu = mod_ref[1, p, pl.ds(8 * g, 8), :]
            stiff = lam + 2.0 * mu
            coup = lam + mu
            centers = [load(c, 0, 0) for c in range(3)]

            def curv(c, axis):
                center = centers[c]
                near = None
                far = None
                for off in (-1, 1, -2, 2):
                    if axis == 0:
                        t = load(c, off, 0)
                    elif axis == 1:
                        t = load(c, 0, off)
                    else:
                        t = zs(center, off)
                    if abs(off) == 1:
                        near = t if near is None else near + t
                    else:
                        far = t if far is None else far + t
                return 16.0 * near - far - 30.0 * center

            def mixed(p_c, a, b):
                if 2 in (a, b):
                    n = a + b - 2
                    d = [0, 0]
                    d[n] = 1
                    step = load(p_c, d[0], d[1])
                    d[n] = -1
                    diff = step - load(p_c, d[0], d[1])
                    return zs(diff, 1) - zs(diff, -1)
                acc = None
                for sa in (1, -1):
                    for sb in (1, -1):
                        d = [0, 0, 0]
                        d[a] = sa
                        d[b] = sb
                        t = zs(load(p_c, d[0], d[1]), d[2])
                        if acc is None:
                            acc = t
                        elif sa * sb > 0:
                            acc = acc + t
                        else:
                            acc = acc - t
                return acc

            for c in range(3):
                others = [e for e in range(3) if e != c]
                second = stiff * curv(c, c) + mu * (curv(c, others[0]) + curv(c, others[1]))
                cross = mixed(others[0], c, others[0]) + mixed(others[1], c, others[1])
                upd = second * (1.0 / 12.0) + coup * (cross * 0.25)
                prev = prev_ref[c, p, pl.ds(8 * g, 8), :]
                src = src_ref[c, p, pl.ds(8 * g, 8), :]
                out_ref[c, p, pl.ds(8 * g, 8), :] = (2.0 * centers[c] - prev + upd) + src
        return carry

    lax.fori_loop(0, bx, plane, 0)


def elastic_step(u, xlo, xhi, ylo, yhi, prev, moduli, sources, bx=8):
    _, nx, ny, depth = u.shape
    kernel = functools.partial(step_kernel, bx=bx)
    block = lambda i: (0, i, 0, 0)
    whole = lambda i: (0, 0, 0, 0)
    return pl.pallas_call(
        kernel,
        grid=(nx // bx,),
        in_specs=[
            pl.BlockSpec(u.shape, whole),
            pl.BlockSpec(xlo.shape, whole),
            pl.BlockSpec(xhi.shape, whole),
            pl.BlockSpec(ylo.shape, whole),
            pl.BlockSpec(yhi.shape, whole),
            pl.BlockSpec((3, bx, ny, depth), block),
            pl.BlockSpec((2, bx, ny, depth), block),
            pl.BlockSpec((3, bx, ny, depth), block),
        ],
        out_specs=pl.BlockSpec((3, bx, ny, depth), block),
        out_shape=jax.ShapeDtypeStruct((3, nx, ny, depth), jnp.float32),
        scratch_shapes=[pltpu.VMEM((3, nx + 4, ny + 2 * YPAD, depth), jnp.float32)],
        compiler_params=pltpu.CompilerParams(dimension_semantics=("arbitrary",)),
    )(u, xlo, xhi, ylo, yhi, prev, moduli, sources)


def x_halos(block, width):
    size_x = lax.axis_size("gx")
    nx = block.shape[1]
    forward_x = [(i, i + 1) for i in range(size_x - 1)]
    backward_x = [(t, s) for s, t in forward_x]
    xlo = lax.ppermute(block[:, nx - width:], "gx", forward_x)
    xhi = lax.ppermute(block[:, :width], "gx", backward_x)
    return xlo, xhi


def y_halos(block, xlo, xhi, width):
    size_y = lax.axis_size("gy")
    ny = block.shape[2]
    forward_y = [(i, i + 1) for i in range(size_y - 1)]
    backward_y = [(t, s) for s, t in forward_y]
    rows = lambda sl: jnp.concatenate([xlo[:, :, sl], block[:, :, sl], xhi[:, :, sl]], axis=1)
    ylo = lax.ppermute(rows(slice(ny - width, ny)), "gy", forward_y)
    yhi = lax.ppermute(rows(slice(0, width)), "gy", backward_y)
    return ylo, yhi


def halos(block, width):
    xlo, xhi = x_halos(block, width)
    ylo, yhi = y_halos(block, xlo, xhi, width)
    return xlo, xhi, ylo, yhi


def level_table(values, layer_of_level):
    one_hot = (
        layer_of_level[:, None] == jnp.arange(values.shape[0], dtype=jnp.int32)[None, :]
    ).astype(jnp.float32)
    return jnp.sum(one_hot * values[None, :], axis=1)


def wave_kernel(angular, slowness, rigidity, damping, count_k):
    wavenum = (jnp.arange(count_k, dtype=jnp.float32) + 0.5) * (4.0 / count_k)
    spread = angular[None, :, None] * slowness[:, None, None]
    vertical = jnp.sqrt(wavenum[None, None, :] * wavenum[None, None, :] + spread * spread)
    impedance = rigidity[:, None, None] * vertical
    beneath = jnp.concatenate([impedance[1:], impedance[-1:]], axis=0)
    reflect = (impedance - beneath) / (impedance + beneath)
    fading = jnp.exp(-2.0 * step_depth * vertical * damping[:, None, None])
    two_way = 2.0 * step_depth * vertical
    trip_re = fading * jnp.cos(two_way)
    trip_im = -fading * jnp.sin(two_way)

    def upward(state_in, layer_data):
        refl_re, refl_im = state_in
        coefficient, along_re, along_im = layer_data
        upper_re = coefficient + refl_re
        lower_re = 1.0 + coefficient * refl_re
        lower_im = coefficient * refl_im
        magnitude = lower_re * lower_re + lower_im * lower_im
        ratio_re = (upper_re * lower_re + refl_im * lower_im) / magnitude
        ratio_im = (refl_im * lower_re - upper_re * lower_im) / magnitude
        fresh_re = along_re * ratio_re - along_im * ratio_im
        fresh_im = along_re * ratio_im + along_im * ratio_re
        return ((fresh_re, fresh_im), (fresh_re, fresh_im))

    bottom = jnp.zeros(vertical.shape[1:], jnp.float32)
    _, (refl_re, refl_im) = lax.scan(
        upward, (bottom, bottom), (reflect, trip_re, trip_im), reverse=True
    )
    travel = step_depth * vertical
    phases = jnp.cumsum(travel, axis=0) - travel
    absorbed = travel * damping[:, None, None]
    losses = jnp.cumsum(absorbed, axis=0) - absorbed
    down_size = jnp.exp(-losses)
    down_re = down_size * jnp.cos(phases)
    down_im = -down_size * jnp.sin(phases)
    weight = 1.0 / math.sqrt(count_k)
    kernel_re = weight * (down_re * (1.0 + refl_re) - down_im * refl_im)
    kernel_im = weight * (down_re * refl_im + down_im * (1.0 + refl_re))
    return jnp.transpose(jnp.stack([kernel_re, kernel_im]), (0, 2, 1, 3))


def offset_basis(count_k, count_r):
    modulus = count_k * count_r // 2
    low_count = 64
    odd_index = 2 * jnp.arange(count_k, dtype=jnp.int32) + 1
    high = jnp.arange(count_r // low_count, dtype=jnp.int32) * low_count
    low = jnp.arange(low_count, dtype=jnp.int32)
    scale = 2.0 * math.pi / modulus
    high_angle = (odd_index[:, None] * high[None, :] % modulus).astype(jnp.float32) * scale
    low_angle = (odd_index[:, None] * low[None, :] % modulus).astype(jnp.float32) * scale
    cos_h, sin_h = jnp.cos(high_angle), jnp.sin(high_angle)
    cos_l, sin_l = jnp.cos(low_angle), jnp.sin(low_angle)
    basis = cos_h[:, :, None] * cos_l[:, None, :] - sin_h[:, :, None] * sin_l[:, None, :]
    basis = basis.reshape(count_k, count_r).astype(jnp.bfloat16)
    return lax.optimization_barrier(basis)


def time_basis(freq_ids, count_f, count_steps, first_time):
    period = 2 * count_f
    times = first_time + jnp.arange(count_steps, dtype=jnp.int32)
    turns = (freq_ids[None, :] + 1) * times[:, None] % period
    angles = turns.astype(jnp.float32) * (2.0 * math.pi / period)
    weight = 1.0 / math.sqrt(count_f)
    return jnp.stack([weight * jnp.cos(angles), -weight * jnp.sin(angles)], axis=1)


def shifted(grid_block, step_x, step_y, step_z):
    width_x = grid_block.shape[0] - 4
    width_y = grid_block.shape[1] - 4
    width_z = grid_block.shape[2] - 4
    return grid_block[
        2 + step_x : 2 + step_x + width_x,
        2 + step_y : 2 + step_y + width_y,
        2 + step_z : 2 + step_z + width_z,
    ]


def curvature(grid_block, first_axis):
    summed = None
    for offset, factor in [(-2, -1.0), (-1, 16.0), (0, -30.0), (1, 16.0), (2, -1.0)]:
        moves = tuple((offset if index == first_axis else 0 for index in range(3)))
        contrib = factor * shifted(grid_block, moves[0], moves[1], moves[2])
        summed = contrib if summed is None else summed + contrib
    return summed / 12.0


def mixed(grid_block, first_axis, second_axis):
    summed = None
    for sign_a, sign_b, factor in [(1, 1, 1.0), (1, -1, -1.0), (-1, 1, -1.0), (-1, -1, 1.0)]:
        moves = tuple(
            (
                sign_a if index == first_axis else sign_b if index == second_axis else 0
                for index in range(3)
            )
        )
        contrib = factor * shifted(grid_block, moves[0], moves[1], moves[2])
        summed = contrib if summed is None else summed + contrib
    return summed / 4.0


def elastic(padded, moduli):
    first_lame = moduli[0]
    shear_mod = moduli[1]
    stiffness = first_lame + 2.0 * shear_mod
    coupling = first_lame + shear_mod
    result = []
    for component in range(3):
        update = stiffness * curvature(padded[component], component)
        for partner in range(3):
            if partner != component:
                update = update + shear_mod * curvature(padded[component], partner)
                update = update + coupling * mixed(padded[partner], component, partner)
        result.append(update)
    return jnp.stack(result)


def shards(
    layer_slowness,
    layer_rigidity,
    layer_damping,
    layer_of_level,
    slot_offset,
    slot_level,
    slot_target,
    live_count,
    moduli,
    field_old,
    field_now,
):
    size_gx = lax.axis_size("gx")
    size_gy = lax.axis_size("gy")
    groups = size_gx * size_gy
    per_device = F // groups
    device = lax.axis_index("gx") * size_gy + lax.axis_index("gy")
    freq_ids = device * per_device + jnp.arange(per_device, dtype=jnp.int32)
    angular = (freq_ids + 1).astype(jnp.float32) * (4.0 / F)
    slowness = level_table(layer_slowness, layer_of_level)
    rigidity = level_table(layer_rigidity, layer_of_level)
    damping = level_table(layer_damping, layer_of_level)
    kernel = wave_kernel(angular, slowness, rigidity, damping, NK).astype(jnp.bfloat16)
    cosines = offset_basis(NK, NR)
    spectrum_table = jnp.dot(
        kernel.reshape(2 * per_device * ND, NK), cosines, preferred_element_type=jnp.float32
    )
    table_rounded = spectrum_table.astype(jnp.bfloat16)
    first_x = x_halos(field_now, 2)
    first_x, table_rounded = lax.optimization_barrier((first_x, table_rounded))
    all_slots = slot_offset.shape[0]
    width = math.gcd(all_slots, 4096)
    count_blocks = all_slots // width
    offset_blocks = slot_offset.reshape(count_blocks, width)
    level_blocks = slot_level.reshape(count_blocks, width)

    def select_block(pair):
        offsets, levels = pair
        offset_hot = (jnp.arange(NR, dtype=jnp.int32)[:, None] == offsets[None, :]).astype(
            jnp.bfloat16
        )
        rows = jnp.dot(table_rounded, offset_hot, preferred_element_type=jnp.float32).reshape(
            2, per_device, ND, width
        )
        level_hot = (jnp.arange(ND, dtype=jnp.int32)[:, None] == levels[None, :]).astype(
            jnp.float32
        )
        return jnp.sum(rows * level_hot[None, None, :, :], axis=2)

    selected = lax.map(select_block, (offset_blocks, level_blocks))
    spectra = (
        jnp.transpose(selected, (1, 2, 0, 3)).reshape(2, per_device, all_slots).astype(jnp.bfloat16)
    )
    slots_dev = slot_target.shape[0]
    occupied = (jnp.arange(slots_dev, dtype=jnp.int32) < live_count[0]).astype(jnp.float32)
    first_y = y_halos(field_now, first_x[0], first_x[1], 2)
    first_y, spectra = lax.optimization_barrier((first_y, spectra))
    parcel = spectra.reshape(2, per_device, groups, slots_dev)
    arrived = lax.all_to_all(parcel, ("gx", "gy"), split_axis=2, concat_axis=1, tiled=True)
    freq_order = jnp.arange(F, dtype=jnp.int32)
    waveforms = time_basis(freq_order, F, STEPS, TSTART).reshape(STEPS, 2 * F)
    traces = jnp.dot(
        waveforms,
        arrived.reshape(2 * F, slots_dev).astype(jnp.float32),
        precision=lax.Precision.HIGHEST,
    )
    block_x = field_now.shape[1]
    block_y = field_now.shape[2]
    depth = field_now.shape[3]
    columns = slot_target // depth
    layer_z = slot_target % depth
    weighted = traces * occupied[None, :]
    column_hot = (
        jnp.arange(3 * block_x * block_y, dtype=jnp.int32)[:, None] == columns[None, :]
    ).astype(jnp.float32)
    depth_hot = (layer_z[:, None] == jnp.arange(depth, dtype=jnp.int32)[None, :]).astype(
        jnp.float32
    )
    previous, current = (field_old, field_now)
    for instant in range(STEPS):
        spread = weighted[instant][:, None] * depth_hot
        source = jnp.dot(column_hot, spread, precision=lax.Precision.HIGHEST)
        source = source.reshape(3, block_x, block_y, depth)
        if instant == 0:
            xlo, xhi, ylo, yhi = first_x + first_y
        else:
            xlo, xhi, ylo, yhi = halos(current, 2)
        advanced = elastic_step(current, xlo, xhi, ylo, yhi, previous, moduli, source)
        previous, current = (current, advanced)
    return (current, previous)


def solution(mesh):
    in_specs = (
        P(),
        P(),
        P(),
        P(),
        P(),
        P(),
        P(("gx", "gy")),
        P(("gx", "gy")),
        P(None, "gx", "gy", None),
        P(None, "gx", "gy", None),
        P(None, "gx", "gy", None),
    )
    out_specs = (P(None, "gx", "gy", None), P(None, "gx", "gy", None))
    return jax.shard_map(shards, mesh=mesh, in_specs=in_specs, out_specs=out_specs, check_vma=False)
```

```python
import math

import jax
import jax.numpy as jnp
from jax import lax
from jax.sharding import PartitionSpec as P
from jax.experimental import pallas as pl
from jax.experimental.pallas import tpu as pltpu
import functools

F = 128
NK = 1024
NR = 2048
ND = 32
STEPS = 4
TSTART = 32


step_depth = 0.25


def padded_2(block, sides, width):
    for axis, dim in sides:
        count = lax.axis_size(axis)
        forward = [(i, i + 1) for i in range(count - 1)]
        backward = [(target, source) for source, target in forward]
        low = lax.ppermute(
            lax.slice_in_dim(block, block.shape[dim] - width, None, axis=dim), axis, forward
        )
        high = lax.ppermute(lax.slice_in_dim(block, 0, width, axis=dim), axis, backward)
        block = jnp.concatenate([low, block, high], axis=dim)
    return block


YPAD = 8


def step_kernel(u_ref, xlo_ref, xhi_ref, ylo_ref, yhi_ref, prev_ref, mod_ref, src_ref, out_ref, up_ref, *, bx):
    i = pl.program_id(0)
    nx, ny = u_ref.shape[1], u_ref.shape[2]

    @pl.when(i == 0)
    def _():
        for c in range(3):
            def fill(x, carry):
                up_ref[c, x + 2, pl.ds(YPAD, ny), :] = u_ref[c, x]
                return carry

            lax.fori_loop(0, nx, fill, 0)
        up_ref[:, 0:2, pl.ds(YPAD, ny), :] = xlo_ref[...]
        up_ref[:, nx + 2:nx + 4, pl.ds(YPAD, ny), :] = xhi_ref[...]
        up_ref[:, :, pl.ds(YPAD - 2, 2), :] = ylo_ref[...]
        up_ref[:, :, pl.ds(YPAD + ny, 2), :] = yhi_ref[...]

    depth = out_ref.shape[3]
    lane = lax.broadcasted_iota(jnp.int32, (8, depth), 1)
    masks = {dz: (lane + dz >= 0) & (lane + dz < depth) for dz in (-2, -1, 1, 2)}

    def zs(v, dz):
        if dz == 0:
            return v
        return jnp.where(masks[dz], pltpu.roll(v, (-dz) % depth, 1), 0.0)

    def plane(p, carry):
        xp = i * bx + p + 2
        for g in range(out_ref.shape[2] // 8):
            def load(c, dx, dy):
                return up_ref[c, xp + dx, pl.ds(8 * g + YPAD + dy, 8), :]

            lam = mod_ref[0, p, pl.ds(8 * g, 8), :]
            mu = mod_ref[1, p, pl.ds(8 * g, 8), :]
            shear = mu * (1.0 / 12.0)
            stiff = lam * (1.0 / 12.0) + 2.0 * shear
            coup = (lam + mu) * 0.25
            centre_weight = -30.0 * (stiff + 2.0 * shear)
            centers = [load(c, 0, 0) for c in range(3)]

            def sums(c, axis):
                center = centers[c]
                near = None
                far = None
                for off in (-1, 1, -2, 2):
                    if axis == 0:
                        t = load(c, off, 0)
                    elif axis == 1:
                        t = load(c, 0, off)
                    else:
                        t = zs(center, off)
                    if abs(off) == 1:
                        near = t if near is None else near + t
                    else:
                        far = t if far is None else far + t
                return near, far

            def mixed(p_c, a, b):
                if 2 in (a, b):
                    n = a + b - 2
                    d = [0, 0]
                    d[n] = 1
                    step = load(p_c, d[0], d[1])
                    d[n] = -1
                    diff = step - load(p_c, d[0], d[1])
                    return zs(diff, 1) - zs(diff, -1)
                acc = None
                for sa in (1, -1):
                    for sb in (1, -1):
                        d = [0, 0, 0]
                        d[a] = sa
                        d[b] = sb
                        t = zs(load(p_c, d[0], d[1]), d[2])
                        if acc is None:
                            acc = t
                        elif sa * sb > 0:
                            acc = acc + t
                        else:
                            acc = acc - t
                return acc

            for c in range(3):
                others = [e for e in range(3) if e != c]
                near_c, far_c = sums(c, c)
                near_a, far_a = sums(c, others[0])
                near_b, far_b = sums(c, others[1])
                near = stiff * near_c + shear * (near_a + near_b)
                far = stiff * far_c + shear * (far_a + far_b)
                second = 16.0 * near - far + centre_weight * centers[c]
                cross = mixed(others[0], c, others[0]) + mixed(others[1], c, others[1])
                upd = second + coup * cross
                prev = prev_ref[c, p, pl.ds(8 * g, 8), :]
                src = src_ref[c, p, pl.ds(8 * g, 8), :]
                out_ref[c, p, pl.ds(8 * g, 8), :] = (2.0 * centers[c] - prev + upd) + src
        return carry

    lax.fori_loop(0, bx, plane, 0)


def elastic_step(u, xlo, xhi, ylo, yhi, prev, moduli, sources, bx=8):
    _, nx, ny, depth = u.shape
    kernel = functools.partial(step_kernel, bx=bx)
    block = lambda i: (0, i, 0, 0)
    whole = lambda i: (0, 0, 0, 0)
    return pl.pallas_call(
        kernel,
        grid=(nx // bx,),
        in_specs=[
            pl.BlockSpec(u.shape, whole),
            pl.BlockSpec(xlo.shape, whole),
            pl.BlockSpec(xhi.shape, whole),
            pl.BlockSpec(ylo.shape, whole),
            pl.BlockSpec(yhi.shape, whole),
            pl.BlockSpec((3, bx, ny, depth), block),
            pl.BlockSpec((2, bx, ny, depth), block),
            pl.BlockSpec((3, bx, ny, depth), block),
        ],
        out_specs=pl.BlockSpec((3, bx, ny, depth), block),
        out_shape=jax.ShapeDtypeStruct((3, nx, ny, depth), jnp.float32),
        scratch_shapes=[pltpu.VMEM((3, nx + 4, ny + 2 * YPAD, depth), jnp.float32)],
        compiler_params=pltpu.CompilerParams(dimension_semantics=("arbitrary",)),
    )(u, xlo, xhi, ylo, yhi, prev, moduli, sources)


def halos(block, width):
    size_x = lax.axis_size("gx")
    size_y = lax.axis_size("gy")
    nx, ny = block.shape[1], block.shape[2]
    forward_x = [(i, i + 1) for i in range(size_x - 1)]
    backward_x = [(t, s) for s, t in forward_x]
    xlo = lax.ppermute(block[:, nx - width:], "gx", forward_x)
    xhi = lax.ppermute(block[:, :width], "gx", backward_x)
    forward_y = [(i, i + 1) for i in range(size_y - 1)]
    backward_y = [(t, s) for s, t in forward_y]
    rows = lambda sl: jnp.concatenate([xlo[:, :, sl], block[:, :, sl], xhi[:, :, sl]], axis=1)
    ylo = lax.ppermute(rows(slice(ny - width, ny)), "gy", forward_y)
    yhi = lax.ppermute(rows(slice(0, width)), "gy", backward_y)
    return xlo, xhi, ylo, yhi


def level_table(values, layer_of_level):
    one_hot = (
        layer_of_level[:, None] == jnp.arange(values.shape[0], dtype=jnp.int32)[None, :]
    ).astype(jnp.float32)
    return jnp.sum(one_hot * values[None, :], axis=1)


def wave_kernel(angular, slowness, rigidity, damping, count_k):
    wavenum = (jnp.arange(count_k, dtype=jnp.float32) + 0.5) * (4.0 / count_k)
    spread = angular[None, :, None] * slowness[:, None, None]
    vertical = jnp.sqrt(wavenum[None, None, :] * wavenum[None, None, :] + spread * spread)
    impedance = rigidity[:, None, None] * vertical
    beneath = jnp.concatenate([impedance[1:], impedance[-1:]], axis=0)
    reflect = (impedance - beneath) / (impedance + beneath)
    fading = jnp.exp(-2.0 * step_depth * vertical * damping[:, None, None])
    two_way = 2.0 * step_depth * vertical
    trip_re = fading * jnp.cos(two_way)
    trip_im = -fading * jnp.sin(two_way)

    def upward(state_in, layer_data):
        refl_re, refl_im = state_in
        coefficient, along_re, along_im = layer_data
        upper_re = coefficient + refl_re
        lower_re = 1.0 + coefficient * refl_re
        lower_im = coefficient * refl_im
        magnitude = lower_re * lower_re + lower_im * lower_im
        ratio_re = (upper_re * lower_re + refl_im * lower_im) / magnitude
        ratio_im = (refl_im * lower_re - upper_re * lower_im) / magnitude
        fresh_re = along_re * ratio_re - along_im * ratio_im
        fresh_im = along_re * ratio_im + along_im * ratio_re
        return ((fresh_re, fresh_im), (fresh_re, fresh_im))

    bottom = jnp.zeros(vertical.shape[1:], jnp.float32)
    _, (refl_re, refl_im) = lax.scan(
        upward, (bottom, bottom), (reflect, trip_re, trip_im), reverse=True
    )
    travel = step_depth * vertical
    phases = jnp.cumsum(travel, axis=0) - travel
    absorbed = travel * damping[:, None, None]
    losses = jnp.cumsum(absorbed, axis=0) - absorbed
    down_size = jnp.exp(-losses)
    down_re = down_size * jnp.cos(phases)
    down_im = -down_size * jnp.sin(phases)
    weight = 1.0 / math.sqrt(count_k)
    kernel_re = weight * (down_re * (1.0 + refl_re) - down_im * refl_im)
    kernel_im = weight * (down_re * refl_im + down_im * (1.0 + refl_re))
    return jnp.transpose(jnp.stack([kernel_re, kernel_im]), (0, 2, 1, 3))


def offset_basis(count_k, count_r):
    modulus = count_k * count_r // 2
    low_count = 64
    odd_index = 2 * jnp.arange(count_k, dtype=jnp.int32) + 1
    high = jnp.arange(count_r // low_count, dtype=jnp.int32) * low_count
    low = jnp.arange(low_count, dtype=jnp.int32)
    scale = 2.0 * math.pi / modulus
    high_angle = (odd_index[:, None] * high[None, :] % modulus).astype(jnp.float32) * scale
    low_angle = (odd_index[:, None] * low[None, :] % modulus).astype(jnp.float32) * scale
    cos_h, sin_h = jnp.cos(high_angle), jnp.sin(high_angle)
    cos_l, sin_l = jnp.cos(low_angle), jnp.sin(low_angle)
    basis = cos_h[:, :, None] * cos_l[:, None, :] - sin_h[:, :, None] * sin_l[:, None, :]
    basis = basis.reshape(count_k, count_r).astype(jnp.bfloat16)
    return lax.optimization_barrier(basis)


def time_basis(freq_ids, count_f, count_steps, first_time):
    period = 2 * count_f
    times = first_time + jnp.arange(count_steps, dtype=jnp.int32)
    turns = (freq_ids[None, :] + 1) * times[:, None] % period
    angles = turns.astype(jnp.float32) * (2.0 * math.pi / period)
    weight = 1.0 / math.sqrt(count_f)
    return jnp.stack([weight * jnp.cos(angles), -weight * jnp.sin(angles)], axis=1)


def shifted(grid_block, step_x, step_y, step_z):
    width_x = grid_block.shape[0] - 4
    width_y = grid_block.shape[1] - 4
    width_z = grid_block.shape[2] - 4
    return grid_block[
        2 + step_x : 2 + step_x + width_x,
        2 + step_y : 2 + step_y + width_y,
        2 + step_z : 2 + step_z + width_z,
    ]


def curvature(grid_block, first_axis):
    summed = None
    for offset, factor in [(-2, -1.0), (-1, 16.0), (0, -30.0), (1, 16.0), (2, -1.0)]:
        moves = tuple((offset if index == first_axis else 0 for index in range(3)))
        contrib = factor * shifted(grid_block, moves[0], moves[1], moves[2])
        summed = contrib if summed is None else summed + contrib
    return summed / 12.0


def mixed(grid_block, first_axis, second_axis):
    summed = None
    for sign_a, sign_b, factor in [(1, 1, 1.0), (1, -1, -1.0), (-1, 1, -1.0), (-1, -1, 1.0)]:
        moves = tuple(
            (
                sign_a if index == first_axis else sign_b if index == second_axis else 0
                for index in range(3)
            )
        )
        contrib = factor * shifted(grid_block, moves[0], moves[1], moves[2])
        summed = contrib if summed is None else summed + contrib
    return summed / 4.0


def elastic(padded, moduli):
    first_lame = moduli[0]
    shear_mod = moduli[1]
    stiffness = first_lame + 2.0 * shear_mod
    coupling = first_lame + shear_mod
    result = []
    for component in range(3):
        update = stiffness * curvature(padded[component], component)
        for partner in range(3):
            if partner != component:
                update = update + shear_mod * curvature(padded[component], partner)
                update = update + coupling * mixed(padded[partner], component, partner)
        result.append(update)
    return jnp.stack(result)


def shards(
    layer_slowness,
    layer_rigidity,
    layer_damping,
    layer_of_level,
    slot_offset,
    slot_level,
    slot_target,
    live_count,
    moduli,
    field_old,
    field_now,
):
    size_gx = lax.axis_size("gx")
    size_gy = lax.axis_size("gy")
    groups = size_gx * size_gy
    per_device = F // groups
    device = lax.axis_index("gx") * size_gy + lax.axis_index("gy")
    freq_ids = device * per_device + jnp.arange(per_device, dtype=jnp.int32)
    angular = (freq_ids + 1).astype(jnp.float32) * (4.0 / F)
    slowness = level_table(layer_slowness, layer_of_level)
    rigidity = level_table(layer_rigidity, layer_of_level)
    damping = level_table(layer_damping, layer_of_level)
    kernel = wave_kernel(angular, slowness, rigidity, damping, NK).astype(jnp.bfloat16)
    cosines = offset_basis(NK, NR)
    spectrum_table = jnp.dot(
        kernel.reshape(2 * per_device * ND, NK), cosines, preferred_element_type=jnp.float32
    )
    table_rounded = spectrum_table.astype(jnp.bfloat16)
    all_slots = slot_offset.shape[0]
    width = math.gcd(all_slots, 4096)
    count_blocks = all_slots // width
    offset_blocks = slot_offset.reshape(count_blocks, width)
    level_blocks = slot_level.reshape(count_blocks, width)

    def select_block(pair):
        offsets, levels = pair
        offset_hot = (jnp.arange(NR, dtype=jnp.int32)[:, None] == offsets[None, :]).astype(
            jnp.bfloat16
        )
        rows = jnp.dot(table_rounded, offset_hot, preferred_element_type=jnp.float32).reshape(
            2, per_device, ND, width
        )
        level_hot = (jnp.arange(ND, dtype=jnp.int32)[:, None] == levels[None, :]).astype(
            jnp.float32
        )
        return jnp.sum(rows * level_hot[None, None, :, :], axis=2)

    selected = lax.map(select_block, (offset_blocks, level_blocks))
    spectra = (
        jnp.transpose(selected, (1, 2, 0, 3)).reshape(2, per_device, all_slots).astype(jnp.bfloat16)
    )
    slots_dev = slot_target.shape[0]
    occupied = (jnp.arange(slots_dev, dtype=jnp.int32) < live_count[0]).astype(jnp.float32)
    parcel = spectra.reshape(2, per_device, groups, slots_dev)
    arrived = lax.all_to_all(parcel, ("gx", "gy"), split_axis=2, concat_axis=1, tiled=True)
    freq_order = jnp.arange(F, dtype=jnp.int32)
    waveforms = time_basis(freq_order, F, STEPS, TSTART).reshape(STEPS, 2 * F)
    traces = jnp.dot(
        waveforms,
        arrived.reshape(2 * F, slots_dev).astype(jnp.float32),
        precision=lax.Precision.HIGHEST,
    )
    block_x = field_now.shape[1]
    block_y = field_now.shape[2]
    depth = field_now.shape[3]
    columns = slot_target // depth
    layer_z = slot_target % depth
    weighted = traces * occupied[None, :]
    column_hot = (
        jnp.arange(3 * block_x * block_y, dtype=jnp.int32)[:, None] == columns[None, :]
    ).astype(jnp.float32)
    depth_hot = (layer_z[:, None] == jnp.arange(depth, dtype=jnp.int32)[None, :]).astype(
        jnp.float32
    )
    previous, current = (field_old, field_now)
    for instant in range(STEPS):
        spread = weighted[instant][:, None] * depth_hot
        source = jnp.dot(column_hot, spread, precision=lax.Precision.HIGHEST)
        source = source.reshape(3, block_x, block_y, depth)
        xlo, xhi, ylo, yhi = halos(current, 2)
        advanced = elastic_step(current, xlo, xhi, ylo, yhi, previous, moduli, source)
        previous, current = (current, advanced)
    return (current, previous)


def solution(mesh):
    in_specs = (
        P(),
        P(),
        P(),
        P(),
        P(),
        P(),
        P(("gx", "gy")),
        P(("gx", "gy")),
        P(None, "gx", "gy", None),
        P(None, "gx", "gy", None),
        P(None, "gx", "gy", None),
    )
    out_specs = (P(None, "gx", "gy", None), P(None, "gx", "gy", None))
    return jax.shard_map(shards, mesh=mesh, in_specs=in_specs, out_specs=out_specs, check_vma=False)
```

```python
import math

import jax
import jax.numpy as jnp
from jax import lax
from jax.sharding import PartitionSpec as P
from jax.experimental import pallas as pl
from jax.experimental.pallas import tpu as pltpu
import functools

F = 128
NK = 1024
NR = 2048
ND = 32
STEPS = 4
TSTART = 32


step_depth = 0.25


def padded_2(block, sides, width):
    for axis, dim in sides:
        count = lax.axis_size(axis)
        forward = [(i, i + 1) for i in range(count - 1)]
        backward = [(target, source) for source, target in forward]
        low = lax.ppermute(
            lax.slice_in_dim(block, block.shape[dim] - width, None, axis=dim), axis, forward
        )
        high = lax.ppermute(lax.slice_in_dim(block, 0, width, axis=dim), axis, backward)
        block = jnp.concatenate([low, block, high], axis=dim)
    return block


YPAD = 8


def step_kernel(u_ref, xlo_ref, xhi_ref, ylo_ref, yhi_ref, prev_ref, mod_ref, src_ref, *rest, bx, first, stride):
    out_ref, up_ref = rest[-2], rest[-1]
    i = first + pl.program_id(0) * stride
    nx, ny = u_ref.shape[1], u_ref.shape[2]

    @pl.when(pl.program_id(0) == 0)
    def _():
        for c in range(3):
            def fill(x, carry):
                up_ref[c, x + 2, pl.ds(YPAD, ny), :] = u_ref[c, x]
                return carry

            lax.fori_loop(0, nx, fill, 0)
        up_ref[:, 0:2, pl.ds(YPAD, ny), :] = xlo_ref[...]
        up_ref[:, nx + 2:nx + 4, pl.ds(YPAD, ny), :] = xhi_ref[...]
        up_ref[:, :, pl.ds(YPAD - 2, 2), :] = ylo_ref[...]
        up_ref[:, :, pl.ds(YPAD + ny, 2), :] = yhi_ref[...]

    depth = out_ref.shape[3]
    lane = lax.broadcasted_iota(jnp.int32, (8, depth), 1)
    masks = {dz: (lane + dz >= 0) & (lane + dz < depth) for dz in (-2, -1, 1, 2)}

    def zs(v, dz):
        if dz == 0:
            return v
        return jnp.where(masks[dz], pltpu.roll(v, (-dz) % depth, 1), 0.0)

    def plane(p, carry):
        xp = i * bx + p + 2
        for g in range(out_ref.shape[2] // 8):
            def load(c, dx, dy):
                return up_ref[c, xp + dx, pl.ds(8 * g + YPAD + dy, 8), :]

            lam = mod_ref[0, p, pl.ds(8 * g, 8), :]
            mu = mod_ref[1, p, pl.ds(8 * g, 8), :]
            shear = mu * (1.0 / 12.0)
            stiff = lam * (1.0 / 12.0) + 2.0 * shear
            coup = (lam + mu) * 0.25
            centre_weight = -30.0 * (stiff + 2.0 * shear)
            centers = [load(c, 0, 0) for c in range(3)]

            def sums(c, axis):
                center = centers[c]
                near = None
                far = None
                for off in (-1, 1, -2, 2):
                    if axis == 0:
                        t = load(c, off, 0)
                    elif axis == 1:
                        t = load(c, 0, off)
                    else:
                        t = zs(center, off)
                    if abs(off) == 1:
                        near = t if near is None else near + t
                    else:
                        far = t if far is None else far + t
                return near, far

            def mixed(p_c, a, b):
                if 2 in (a, b):
                    n = a + b - 2
                    d = [0, 0]
                    d[n] = 1
                    step = load(p_c, d[0], d[1])
                    d[n] = -1
                    diff = step - load(p_c, d[0], d[1])
                    return zs(diff, 1) - zs(diff, -1)
                acc = None
                for sa in (1, -1):
                    for sb in (1, -1):
                        d = [0, 0, 0]
                        d[a] = sa
                        d[b] = sb
                        t = zs(load(p_c, d[0], d[1]), d[2])
                        if acc is None:
                            acc = t
                        elif sa * sb > 0:
                            acc = acc + t
                        else:
                            acc = acc - t
                return acc

            for c in range(3):
                others = [e for e in range(3) if e != c]
                near_c, far_c = sums(c, c)
                near_a, far_a = sums(c, others[0])
                near_b, far_b = sums(c, others[1])
                near = stiff * near_c + shear * (near_a + near_b)
                far = stiff * far_c + shear * (far_a + far_b)
                second = 16.0 * near - far + centre_weight * centers[c]
                cross = mixed(others[0], c, others[0]) + mixed(others[1], c, others[1])
                upd = second + coup * cross
                prev = prev_ref[c, p, pl.ds(8 * g, 8), :]
                src = src_ref[c, p, pl.ds(8 * g, 8), :]
                out_ref[c, p, pl.ds(8 * g, 8), :] = (2.0 * centers[c] - prev + upd) + src
        return carry

    lax.fori_loop(0, bx, plane, 0)


def elastic_part(u, xlo, xhi, ylo, yhi, prev, moduli, sources, bx, first, stride, count, into=None):
    _, nx, ny, depth = u.shape
    kernel = functools.partial(step_kernel, bx=bx, first=first, stride=stride)
    block = lambda i: (0, first + i * stride, 0, 0)
    whole = lambda i: (0, 0, 0, 0)
    in_specs = [
        pl.BlockSpec(u.shape, whole),
        pl.BlockSpec(xlo.shape, whole),
        pl.BlockSpec(xhi.shape, whole),
        pl.BlockSpec(ylo.shape, whole),
        pl.BlockSpec(yhi.shape, whole),
        pl.BlockSpec((3, bx, ny, depth), block),
        pl.BlockSpec((2, bx, ny, depth), block),
        pl.BlockSpec((3, bx, ny, depth), block),
    ]
    operands = [u, xlo, xhi, ylo, yhi, prev, moduli, sources]
    aliases = {}
    if into is not None:
        in_specs.append(pl.BlockSpec(memory_space=pl.ANY))
        operands.append(into)
        aliases = {8: 0}
    return pl.pallas_call(
        kernel,
        grid=(count,),
        in_specs=in_specs,
        out_specs=pl.BlockSpec((3, bx, ny, depth), block),
        out_shape=jax.ShapeDtypeStruct((3, nx, ny, depth), jnp.float32),
        scratch_shapes=[pltpu.VMEM((3, nx + 4, ny + 2 * YPAD, depth), jnp.float32)],
        compiler_params=pltpu.CompilerParams(dimension_semantics=("arbitrary",)),
        input_output_aliases=aliases,
    )(*operands)


def elastic_step(u, xlo, xhi, ylo, yhi, prev, moduli, sources, bx=4):
    blocks = u.shape[1] // bx
    args = (u, xlo, xhi, ylo, yhi, prev, moduli, sources, bx)
    edge = elastic_part(*args, 0, blocks - 1, 2)
    whole = elastic_part(*args, 1, 1, blocks - 2, into=edge)
    return edge, whole


def x_halos(block, width):
    size_x = lax.axis_size("gx")
    nx = block.shape[1]
    forward_x = [(i, i + 1) for i in range(size_x - 1)]
    backward_x = [(t, s) for s, t in forward_x]
    xlo = lax.ppermute(block[:, nx - width:], "gx", forward_x)
    xhi = lax.ppermute(block[:, :width], "gx", backward_x)
    return xlo, xhi


def y_halos(block, xlo, xhi, width):
    size_y = lax.axis_size("gy")
    ny = block.shape[2]
    forward_y = [(i, i + 1) for i in range(size_y - 1)]
    backward_y = [(t, s) for s, t in forward_y]
    rows = lambda sl: jnp.concatenate([xlo[:, :, sl], block[:, :, sl], xhi[:, :, sl]], axis=1)
    ylo = lax.ppermute(rows(slice(ny - width, ny)), "gy", forward_y)
    yhi = lax.ppermute(rows(slice(0, width)), "gy", backward_y)
    return ylo, yhi


def level_table(values, layer_of_level):
    one_hot = (
        layer_of_level[:, None] == jnp.arange(values.shape[0], dtype=jnp.int32)[None, :]
    ).astype(jnp.float32)
    return jnp.sum(one_hot * values[None, :], axis=1)


def wave_kernel(angular, slowness, rigidity, damping, count_k):
    wavenum = (jnp.arange(count_k, dtype=jnp.float32) + 0.5) * (4.0 / count_k)
    spread = angular[None, :, None] * slowness[:, None, None]
    vertical = jnp.sqrt(wavenum[None, None, :] * wavenum[None, None, :] + spread * spread)
    impedance = rigidity[:, None, None] * vertical
    beneath = jnp.concatenate([impedance[1:], impedance[-1:]], axis=0)
    reflect = (impedance - beneath) / (impedance + beneath)
    fading = jnp.exp(-2.0 * step_depth * vertical * damping[:, None, None])
    two_way = 2.0 * step_depth * vertical
    trip_re = fading * jnp.cos(two_way)
    trip_im = -fading * jnp.sin(two_way)

    def upward(state_in, layer_data):
        refl_re, refl_im = state_in
        coefficient, along_re, along_im = layer_data
        upper_re = coefficient + refl_re
        lower_re = 1.0 + coefficient * refl_re
        lower_im = coefficient * refl_im
        magnitude = lower_re * lower_re + lower_im * lower_im
        ratio_re = (upper_re * lower_re + refl_im * lower_im) / magnitude
        ratio_im = (refl_im * lower_re - upper_re * lower_im) / magnitude
        fresh_re = along_re * ratio_re - along_im * ratio_im
        fresh_im = along_re * ratio_im + along_im * ratio_re
        return ((fresh_re, fresh_im), (fresh_re, fresh_im))

    bottom = jnp.zeros(vertical.shape[1:], jnp.float32)
    _, (refl_re, refl_im) = lax.scan(
        upward, (bottom, bottom), (reflect, trip_re, trip_im), reverse=True
    )
    travel = step_depth * vertical
    phases = jnp.cumsum(travel, axis=0) - travel
    absorbed = travel * damping[:, None, None]
    losses = jnp.cumsum(absorbed, axis=0) - absorbed
    down_size = jnp.exp(-losses)
    down_re = down_size * jnp.cos(phases)
    down_im = -down_size * jnp.sin(phases)
    weight = 1.0 / math.sqrt(count_k)
    kernel_re = weight * (down_re * (1.0 + refl_re) - down_im * refl_im)
    kernel_im = weight * (down_re * refl_im + down_im * (1.0 + refl_re))
    return jnp.transpose(jnp.stack([kernel_re, kernel_im]), (0, 2, 1, 3))


def offset_basis(count_k, count_r):
    modulus = count_k * count_r // 2
    low_count = 64
    odd_index = 2 * jnp.arange(count_k, dtype=jnp.int32) + 1
    high = jnp.arange(count_r // low_count, dtype=jnp.int32) * low_count
    low = jnp.arange(low_count, dtype=jnp.int32)
    scale = 2.0 * math.pi / modulus
    high_angle = (odd_index[:, None] * high[None, :] % modulus).astype(jnp.float32) * scale
    low_angle = (odd_index[:, None] * low[None, :] % modulus).astype(jnp.float32) * scale
    cos_h, sin_h = jnp.cos(high_angle), jnp.sin(high_angle)
    cos_l, sin_l = jnp.cos(low_angle), jnp.sin(low_angle)
    basis = cos_h[:, :, None] * cos_l[:, None, :] - sin_h[:, :, None] * sin_l[:, None, :]
    basis = basis.reshape(count_k, count_r).astype(jnp.bfloat16)
    return lax.optimization_barrier(basis)


def time_basis(freq_ids, count_f, count_steps, first_time):
    period = 2 * count_f
    times = first_time + jnp.arange(count_steps, dtype=jnp.int32)
    turns = (freq_ids[None, :] + 1) * times[:, None] % period
    angles = turns.astype(jnp.float32) * (2.0 * math.pi / period)
    weight = 1.0 / math.sqrt(count_f)
    return jnp.stack([weight * jnp.cos(angles), -weight * jnp.sin(angles)], axis=1)


def shifted(grid_block, step_x, step_y, step_z):
    width_x = grid_block.shape[0] - 4
    width_y = grid_block.shape[1] - 4
    width_z = grid_block.shape[2] - 4
    return grid_block[
        2 + step_x : 2 + step_x + width_x,
        2 + step_y : 2 + step_y + width_y,
        2 + step_z : 2 + step_z + width_z,
    ]


def curvature(grid_block, first_axis):
    summed = None
    for offset, factor in [(-2, -1.0), (-1, 16.0), (0, -30.0), (1, 16.0), (2, -1.0)]:
        moves = tuple((offset if index == first_axis else 0 for index in range(3)))
        contrib = factor * shifted(grid_block, moves[0], moves[1], moves[2])
        summed = contrib if summed is None else summed + contrib
    return summed / 12.0


def mixed(grid_block, first_axis, second_axis):
    summed = None
    for sign_a, sign_b, factor in [(1, 1, 1.0), (1, -1, -1.0), (-1, 1, -1.0), (-1, -1, 1.0)]:
        moves = tuple(
            (
                sign_a if index == first_axis else sign_b if index == second_axis else 0
                for index in range(3)
            )
        )
        contrib = factor * shifted(grid_block, moves[0], moves[1], moves[2])
        summed = contrib if summed is None else summed + contrib
    return summed / 4.0


def elastic(padded, moduli):
    first_lame = moduli[0]
    shear_mod = moduli[1]
    stiffness = first_lame + 2.0 * shear_mod
    coupling = first_lame + shear_mod
    result = []
    for component in range(3):
        update = stiffness * curvature(padded[component], component)
        for partner in range(3):
            if partner != component:
                update = update + shear_mod * curvature(padded[component], partner)
                update = update + coupling * mixed(padded[partner], component, partner)
        result.append(update)
    return jnp.stack(result)


def shards(
    layer_slowness,
    layer_rigidity,
    layer_damping,
    layer_of_level,
    slot_offset,
    slot_level,
    slot_target,
    live_count,
    moduli,
    field_old,
    field_now,
):
    size_gx = lax.axis_size("gx")
    size_gy = lax.axis_size("gy")
    groups = size_gx * size_gy
    per_device = F // groups
    device = lax.axis_index("gx") * size_gy + lax.axis_index("gy")
    freq_ids = device * per_device + jnp.arange(per_device, dtype=jnp.int32)
    angular = (freq_ids + 1).astype(jnp.float32) * (4.0 / F)
    slowness = level_table(layer_slowness, layer_of_level)
    rigidity = level_table(layer_rigidity, layer_of_level)
    damping = level_table(layer_damping, layer_of_level)
    kernel = wave_kernel(angular, slowness, rigidity, damping, NK).astype(jnp.bfloat16)
    cosines = offset_basis(NK, NR)
    spectrum_table = jnp.dot(
        kernel.reshape(2 * per_device * ND, NK), cosines, preferred_element_type=jnp.float32
    )
    table_rounded = spectrum_table.astype(jnp.bfloat16)
    all_slots = slot_offset.shape[0]
    width = math.gcd(all_slots, 4096)
    count_blocks = all_slots // width
    offset_blocks = slot_offset.reshape(count_blocks, width)
    level_blocks = slot_level.reshape(count_blocks, width)

    def select_block(pair):
        offsets, levels = pair
        offset_hot = (jnp.arange(NR, dtype=jnp.int32)[:, None] == offsets[None, :]).astype(
            jnp.bfloat16
        )
        rows = jnp.dot(table_rounded, offset_hot, preferred_element_type=jnp.float32).reshape(
            2, per_device, ND, width
        )
        level_hot = (jnp.arange(ND, dtype=jnp.int32)[:, None] == levels[None, :]).astype(
            jnp.float32
        )
        return jnp.sum(rows * level_hot[None, None, :, :], axis=2)

    selected = lax.map(select_block, (offset_blocks, level_blocks))
    spectra = (
        jnp.transpose(selected, (1, 2, 0, 3)).reshape(2, per_device, all_slots).astype(jnp.bfloat16)
    )
    slots_dev = slot_target.shape[0]
    occupied = (jnp.arange(slots_dev, dtype=jnp.int32) < live_count[0]).astype(jnp.float32)
    parcel = spectra.reshape(2, per_device, groups, slots_dev)
    arrived = lax.all_to_all(parcel, ("gx", "gy"), split_axis=2, concat_axis=1, tiled=True)
    freq_order = jnp.arange(F, dtype=jnp.int32)
    waveforms = time_basis(freq_order, F, STEPS, TSTART).reshape(STEPS, 2 * F)
    traces = jnp.dot(
        waveforms,
        arrived.reshape(2 * F, slots_dev).astype(jnp.float32),
        precision=lax.Precision.HIGHEST,
    )
    block_x = field_now.shape[1]
    block_y = field_now.shape[2]
    depth = field_now.shape[3]
    columns = slot_target // depth
    layer_z = slot_target % depth
    weighted = traces * occupied[None, :]
    column_hot = (
        jnp.arange(3 * block_x * block_y, dtype=jnp.int32)[:, None] == columns[None, :]
    ).astype(jnp.float32)
    depth_hot = (layer_z[:, None] == jnp.arange(depth, dtype=jnp.int32)[None, :]).astype(
        jnp.float32
    )
    previous, current = (field_old, field_now)
    edge = field_now
    for instant in range(STEPS):
        spread = weighted[instant][:, None] * depth_hot
        source = jnp.dot(column_hot, spread, precision=lax.Precision.HIGHEST)
        source = source.reshape(3, block_x, block_y, depth)
        xlo, xhi = x_halos(edge, 2)
        ylo, yhi = y_halos(current, xlo, xhi, 2)
        edge, advanced = elastic_step(current, xlo, xhi, ylo, yhi, previous, moduli, source)
        previous, current = (current, advanced)
    return (current, previous)


def solution(mesh):
    in_specs = (
        P(),
        P(),
        P(),
        P(),
        P(),
        P(),
        P(("gx", "gy")),
        P(("gx", "gy")),
        P(None, "gx", "gy", None),
        P(None, "gx", "gy", None),
        P(None, "gx", "gy", None),
    )
    out_specs = (P(None, "gx", "gy", None), P(None, "gx", "gy", None))
    return jax.shard_map(shards, mesh=mesh, in_specs=in_specs, out_specs=out_specs, check_vma=False)
```

```python
import math

import jax
import jax.numpy as jnp
from jax import lax
from jax.sharding import PartitionSpec as P
from jax.experimental import pallas as pl
from jax.experimental.pallas import tpu as pltpu
import functools

F = 128
NK = 1024
NR = 2048
ND = 32
STEPS = 4
TSTART = 32


step_depth = 0.25


def padded_2(block, sides, width):
    for axis, dim in sides:
        count = lax.axis_size(axis)
        forward = [(i, i + 1) for i in range(count - 1)]
        backward = [(target, source) for source, target in forward]
        low = lax.ppermute(
            lax.slice_in_dim(block, block.shape[dim] - width, None, axis=dim), axis, forward
        )
        high = lax.ppermute(lax.slice_in_dim(block, 0, width, axis=dim), axis, backward)
        block = jnp.concatenate([low, block, high], axis=dim)
    return block


YPAD = 8


def step_kernel(u_ref, xlo_ref, xhi_ref, ylo_ref, yhi_ref, prev_ref, mod_ref, src_ref, *rest, bx, first, stride, spans):
    out_ref, up_ref, sems = rest[-3], rest[-2], rest[-1]
    i = first + pl.program_id(0) * stride
    nx, ny = u_ref.shape[1], u_ref.shape[2]

    @pl.when(pl.program_id(0) == 0)
    def _():
        fills = []
        for k, (start, size) in enumerate(spans):
            fill = pltpu.make_async_copy(
                u_ref.at[:, pl.ds(start, size)],
                up_ref.at[:, pl.ds(start + 2, size), pl.ds(YPAD, ny), :],
                sems.at[k],
            )
            fill.start()
            fills.append(fill)
        up_ref[:, 0:2, pl.ds(YPAD, ny), :] = xlo_ref[...]
        up_ref[:, nx + 2:nx + 4, pl.ds(YPAD, ny), :] = xhi_ref[...]
        up_ref[:, :, pl.ds(YPAD - 2, 2), :] = ylo_ref[...]
        up_ref[:, :, pl.ds(YPAD + ny, 2), :] = yhi_ref[...]
        for fill in fills:
            fill.wait()

    depth = out_ref.shape[3]
    lane = lax.broadcasted_iota(jnp.int32, (8, depth), 1)
    masks = {dz: (lane + dz >= 0) & (lane + dz < depth) for dz in (-2, -1, 1, 2)}

    def zs(v, dz):
        if dz == 0:
            return v
        return jnp.where(masks[dz], pltpu.roll(v, (-dz) % depth, 1), 0.0)

    def plane(p, carry):
        xp = i * bx + p + 2
        for g in range(out_ref.shape[2] // 8):
            def load(c, dx, dy):
                return up_ref[c, xp + dx, pl.ds(8 * g + YPAD + dy, 8), :]

            lam = mod_ref[0, p, pl.ds(8 * g, 8), :]
            mu = mod_ref[1, p, pl.ds(8 * g, 8), :]
            shear = mu * (1.0 / 12.0)
            stiff = lam * (1.0 / 12.0) + 2.0 * shear
            coup = (lam + mu) * 0.25
            centre_weight = -30.0 * (stiff + 2.0 * shear)
            centers = [load(c, 0, 0) for c in range(3)]

            def sums(c, axis):
                center = centers[c]
                near = None
                far = None
                for off in (-1, 1, -2, 2):
                    if axis == 0:
                        t = load(c, off, 0)
                    elif axis == 1:
                        t = load(c, 0, off)
                    else:
                        t = zs(center, off)
                    if abs(off) == 1:
                        near = t if near is None else near + t
                    else:
                        far = t if far is None else far + t
                return near, far

            def mixed(p_c, a, b):
                if 2 in (a, b):
                    n = a + b - 2
                    d = [0, 0]
                    d[n] = 1
                    step = load(p_c, d[0], d[1])
                    d[n] = -1
                    diff = step - load(p_c, d[0], d[1])
                    return zs(diff, 1) - zs(diff, -1)
                acc = None
                for sa in (1, -1):
                    for sb in (1, -1):
                        d = [0, 0, 0]
                        d[a] = sa
                        d[b] = sb
                        t = zs(load(p_c, d[0], d[1]), d[2])
                        if acc is None:
                            acc = t
                        elif sa * sb > 0:
                            acc = acc + t
                        else:
                            acc = acc - t
                return acc

            for c in range(3):
                others = [e for e in range(3) if e != c]
                near_c, far_c = sums(c, c)
                near_a, far_a = sums(c, others[0])
                near_b, far_b = sums(c, others[1])
                near = stiff * near_c + shear * (near_a + near_b)
                far = stiff * far_c + shear * (far_a + far_b)
                second = 16.0 * near - far + centre_weight * centers[c]
                cross = mixed(others[0], c, others[0]) + mixed(others[1], c, others[1])
                upd = second + coup * cross
                prev = prev_ref[c, p, pl.ds(8 * g, 8), :]
                src = src_ref[c, p, pl.ds(8 * g, 8), :]
                out_ref[c, p, pl.ds(8 * g, 8), :] = (2.0 * centers[c] - prev + upd) + src
        return carry

    lax.fori_loop(0, bx, plane, 0)


def elastic_part(u, xlo, xhi, ylo, yhi, prev, moduli, sources, bx, first, stride, count, into=None):
    _, nx, ny, depth = u.shape
    if first == 0:
        spans = ((0, bx + 2), (nx - bx - 2, bx + 2))
    else:
        spans = ((bx - 2, nx - 2 * bx + 4),)
    kernel = functools.partial(step_kernel, bx=bx, first=first, stride=stride, spans=spans)
    block = lambda i: (0, first + i * stride, 0, 0)
    whole = lambda i: (0, 0, 0, 0)
    in_specs = [
        pl.BlockSpec(memory_space=pl.ANY),
        pl.BlockSpec(xlo.shape, whole),
        pl.BlockSpec(xhi.shape, whole),
        pl.BlockSpec(ylo.shape, whole),
        pl.BlockSpec(yhi.shape, whole),
        pl.BlockSpec((3, bx, ny, depth), block),
        pl.BlockSpec((2, bx, ny, depth), block),
        pl.BlockSpec((3, bx, ny, depth), block),
    ]
    operands = [u, xlo, xhi, ylo, yhi, prev, moduli, sources]
    aliases = {}
    if into is not None:
        in_specs.append(pl.BlockSpec(memory_space=pl.ANY))
        operands.append(into)
        aliases = {8: 0}
    return pl.pallas_call(
        kernel,
        grid=(count,),
        in_specs=in_specs,
        out_specs=pl.BlockSpec((3, bx, ny, depth), block),
        out_shape=jax.ShapeDtypeStruct((3, nx, ny, depth), jnp.float32),
        scratch_shapes=[
            pltpu.VMEM((3, nx + 4, ny + 2 * YPAD, depth), jnp.float32),
            pltpu.SemaphoreType.DMA((len(spans),)),
        ],
        compiler_params=pltpu.CompilerParams(dimension_semantics=("arbitrary",)),
        input_output_aliases=aliases,
    )(*operands)


def elastic_step(u, xlo, xhi, ylo, yhi, prev, moduli, sources, bx=4):
    blocks = u.shape[1] // bx
    args = (u, xlo, xhi, ylo, yhi, prev, moduli, sources, bx)
    edge = elastic_part(*args, 0, blocks - 1, 2)
    whole = elastic_part(*args, 1, 1, blocks - 2, into=edge)
    return edge, whole


def x_halos(block, width):
    size_x = lax.axis_size("gx")
    nx = block.shape[1]
    forward_x = [(i, i + 1) for i in range(size_x - 1)]
    backward_x = [(t, s) for s, t in forward_x]
    xlo = lax.ppermute(block[:, nx - width:], "gx", forward_x)
    xhi = lax.ppermute(block[:, :width], "gx", backward_x)
    return xlo, xhi


def y_halos(block, xlo, xhi, width):
    size_y = lax.axis_size("gy")
    ny = block.shape[2]
    forward_y = [(i, i + 1) for i in range(size_y - 1)]
    backward_y = [(t, s) for s, t in forward_y]
    rows = lambda sl: jnp.concatenate([xlo[:, :, sl], block[:, :, sl], xhi[:, :, sl]], axis=1)
    ylo = lax.ppermute(rows(slice(ny - width, ny)), "gy", forward_y)
    yhi = lax.ppermute(rows(slice(0, width)), "gy", backward_y)
    return ylo, yhi


def level_table(values, layer_of_level):
    one_hot = (
        layer_of_level[:, None] == jnp.arange(values.shape[0], dtype=jnp.int32)[None, :]
    ).astype(jnp.float32)
    return jnp.sum(one_hot * values[None, :], axis=1)


def wave_kernel(angular, slowness, rigidity, damping, count_k):
    wavenum = (jnp.arange(count_k, dtype=jnp.float32) + 0.5) * (4.0 / count_k)
    spread = angular[None, :, None] * slowness[:, None, None]
    vertical = jnp.sqrt(wavenum[None, None, :] * wavenum[None, None, :] + spread * spread)
    impedance = rigidity[:, None, None] * vertical
    beneath = jnp.concatenate([impedance[1:], impedance[-1:]], axis=0)
    reflect = (impedance - beneath) / (impedance + beneath)
    fading = jnp.exp(-2.0 * step_depth * vertical * damping[:, None, None])
    two_way = 2.0 * step_depth * vertical
    trip_re = fading * jnp.cos(two_way)
    trip_im = -fading * jnp.sin(two_way)

    def upward(state_in, layer_data):
        refl_re, refl_im = state_in
        coefficient, along_re, along_im = layer_data
        upper_re = coefficient + refl_re
        lower_re = 1.0 + coefficient * refl_re
        lower_im = coefficient * refl_im
        magnitude = lower_re * lower_re + lower_im * lower_im
        ratio_re = (upper_re * lower_re + refl_im * lower_im) / magnitude
        ratio_im = (refl_im * lower_re - upper_re * lower_im) / magnitude
        fresh_re = along_re * ratio_re - along_im * ratio_im
        fresh_im = along_re * ratio_im + along_im * ratio_re
        return ((fresh_re, fresh_im), (fresh_re, fresh_im))

    bottom = jnp.zeros(vertical.shape[1:], jnp.float32)
    _, (refl_re, refl_im) = lax.scan(
        upward, (bottom, bottom), (reflect, trip_re, trip_im), reverse=True
    )
    travel = step_depth * vertical
    phases = jnp.cumsum(travel, axis=0) - travel
    absorbed = travel * damping[:, None, None]
    losses = jnp.cumsum(absorbed, axis=0) - absorbed
    down_size = jnp.exp(-losses)
    down_re = down_size * jnp.cos(phases)
    down_im = -down_size * jnp.sin(phases)
    weight = 1.0 / math.sqrt(count_k)
    kernel_re = weight * (down_re * (1.0 + refl_re) - down_im * refl_im)
    kernel_im = weight * (down_re * refl_im + down_im * (1.0 + refl_re))
    return jnp.transpose(jnp.stack([kernel_re, kernel_im]), (0, 2, 1, 3))


def offset_basis(count_k, count_r):
    modulus = count_k * count_r // 2
    low_count = 64
    odd_index = 2 * jnp.arange(count_k, dtype=jnp.int32) + 1
    high = jnp.arange(count_r // low_count, dtype=jnp.int32) * low_count
    low = jnp.arange(low_count, dtype=jnp.int32)
    scale = 2.0 * math.pi / modulus
    high_angle = (odd_index[:, None] * high[None, :] % modulus).astype(jnp.float32) * scale
    low_angle = (odd_index[:, None] * low[None, :] % modulus).astype(jnp.float32) * scale
    cos_h, sin_h = jnp.cos(high_angle), jnp.sin(high_angle)
    cos_l, sin_l = jnp.cos(low_angle), jnp.sin(low_angle)
    basis = cos_h[:, :, None] * cos_l[:, None, :] - sin_h[:, :, None] * sin_l[:, None, :]
    basis = basis.reshape(count_k, count_r).astype(jnp.bfloat16)
    return lax.optimization_barrier(basis)


def time_basis(freq_ids, count_f, count_steps, first_time):
    period = 2 * count_f
    times = first_time + jnp.arange(count_steps, dtype=jnp.int32)
    turns = (freq_ids[None, :] + 1) * times[:, None] % period
    angles = turns.astype(jnp.float32) * (2.0 * math.pi / period)
    weight = 1.0 / math.sqrt(count_f)
    return jnp.stack([weight * jnp.cos(angles), -weight * jnp.sin(angles)], axis=1)


def shifted(grid_block, step_x, step_y, step_z):
    width_x = grid_block.shape[0] - 4
    width_y = grid_block.shape[1] - 4
    width_z = grid_block.shape[2] - 4
    return grid_block[
        2 + step_x : 2 + step_x + width_x,
        2 + step_y : 2 + step_y + width_y,
        2 + step_z : 2 + step_z + width_z,
    ]


def curvature(grid_block, first_axis):
    summed = None
    for offset, factor in [(-2, -1.0), (-1, 16.0), (0, -30.0), (1, 16.0), (2, -1.0)]:
        moves = tuple((offset if index == first_axis else 0 for index in range(3)))
        contrib = factor * shifted(grid_block, moves[0], moves[1], moves[2])
        summed = contrib if summed is None else summed + contrib
    return summed / 12.0


def mixed(grid_block, first_axis, second_axis):
    summed = None
    for sign_a, sign_b, factor in [(1, 1, 1.0), (1, -1, -1.0), (-1, 1, -1.0), (-1, -1, 1.0)]:
        moves = tuple(
            (
                sign_a if index == first_axis else sign_b if index == second_axis else 0
                for index in range(3)
            )
        )
        contrib = factor * shifted(grid_block, moves[0], moves[1], moves[2])
        summed = contrib if summed is None else summed + contrib
    return summed / 4.0


def elastic(padded, moduli):
    first_lame = moduli[0]
    shear_mod = moduli[1]
    stiffness = first_lame + 2.0 * shear_mod
    coupling = first_lame + shear_mod
    result = []
    for component in range(3):
        update = stiffness * curvature(padded[component], component)
        for partner in range(3):
            if partner != component:
                update = update + shear_mod * curvature(padded[component], partner)
                update = update + coupling * mixed(padded[partner], component, partner)
        result.append(update)
    return jnp.stack(result)


def shards(
    layer_slowness,
    layer_rigidity,
    layer_damping,
    layer_of_level,
    slot_offset,
    slot_level,
    slot_target,
    live_count,
    moduli,
    field_old,
    field_now,
):
    size_gx = lax.axis_size("gx")
    size_gy = lax.axis_size("gy")
    groups = size_gx * size_gy
    per_device = F // groups
    device = lax.axis_index("gx") * size_gy + lax.axis_index("gy")
    freq_ids = device * per_device + jnp.arange(per_device, dtype=jnp.int32)
    angular = (freq_ids + 1).astype(jnp.float32) * (4.0 / F)
    slowness = level_table(layer_slowness, layer_of_level)
    rigidity = level_table(layer_rigidity, layer_of_level)
    damping = level_table(layer_damping, layer_of_level)
    kernel = wave_kernel(angular, slowness, rigidity, damping, NK).astype(jnp.bfloat16)
    cosines = offset_basis(NK, NR)
    spectrum_table = jnp.dot(
        kernel.reshape(2 * per_device * ND, NK), cosines, preferred_element_type=jnp.float32
    )
    table_rounded = spectrum_table.astype(jnp.bfloat16)
    all_slots = slot_offset.shape[0]
    width = math.gcd(all_slots, 4096)
    count_blocks = all_slots // width
    offset_blocks = slot_offset.reshape(count_blocks, width)
    level_blocks = slot_level.reshape(count_blocks, width)

    def select_block(pair):
        offsets, levels = pair
        offset_hot = (jnp.arange(NR, dtype=jnp.int32)[:, None] == offsets[None, :]).astype(
            jnp.bfloat16
        )
        rows = jnp.dot(table_rounded, offset_hot, preferred_element_type=jnp.float32).reshape(
            2, per_device, ND, width
        )
        level_hot = (jnp.arange(ND, dtype=jnp.int32)[:, None] == levels[None, :]).astype(
            jnp.float32
        )
        return jnp.sum(rows * level_hot[None, None, :, :], axis=2)

    selected = lax.map(select_block, (offset_blocks, level_blocks))
    spectra = (
        jnp.transpose(selected, (1, 2, 0, 3)).reshape(2, per_device, all_slots).astype(jnp.bfloat16)
    )
    slots_dev = slot_target.shape[0]
    occupied = (jnp.arange(slots_dev, dtype=jnp.int32) < live_count[0]).astype(jnp.float32)
    parcel = spectra.reshape(2, per_device, groups, slots_dev)
    arrived = lax.all_to_all(parcel, ("gx", "gy"), split_axis=2, concat_axis=1, tiled=True)
    freq_order = jnp.arange(F, dtype=jnp.int32)
    waveforms = time_basis(freq_order, F, STEPS, TSTART).reshape(STEPS, 2 * F)
    traces = jnp.dot(
        waveforms,
        arrived.reshape(2 * F, slots_dev).astype(jnp.float32),
        precision=lax.Precision.HIGHEST,
    )
    block_x = field_now.shape[1]
    block_y = field_now.shape[2]
    depth = field_now.shape[3]
    columns = slot_target // depth
    layer_z = slot_target % depth
    weighted = traces * occupied[None, :]
    column_hot = (
        jnp.arange(3 * block_x * block_y, dtype=jnp.int32)[:, None] == columns[None, :]
    ).astype(jnp.float32)
    depth_hot = (layer_z[:, None] == jnp.arange(depth, dtype=jnp.int32)[None, :]).astype(
        jnp.float32
    )
    previous, current = (field_old, field_now)
    edge = field_now
    for instant in range(STEPS):
        spread = weighted[instant][:, None] * depth_hot
        source = jnp.dot(column_hot, spread, precision=lax.Precision.HIGHEST)
        source = source.reshape(3, block_x, block_y, depth)
        xlo, xhi = x_halos(edge, 2)
        ylo, yhi = y_halos(current, xlo, xhi, 2)
        edge, advanced = elastic_step(current, xlo, xhi, ylo, yhi, previous, moduli, source)
        previous, current = (current, advanced)
    return (current, previous)


def solution(mesh):
    in_specs = (
        P(),
        P(),
        P(),
        P(),
        P(),
        P(),
        P(("gx", "gy")),
        P(("gx", "gy")),
        P(None, "gx", "gy", None),
        P(None, "gx", "gy", None),
        P(None, "gx", "gy", None),
    )
    out_specs = (P(None, "gx", "gy", None), P(None, "gx", "gy", None))
    return jax.shard_map(shards, mesh=mesh, in_specs=in_specs, out_specs=out_specs, check_vma=False)
```

```python
import math

import jax
import jax.numpy as jnp
from jax import lax
from jax.sharding import PartitionSpec as P
from jax.experimental import pallas as pl
from jax.experimental.pallas import tpu as pltpu
import functools

F = 128
NK = 1024
NR = 2048
ND = 32
STEPS = 4
TSTART = 32


step_depth = 0.25


def padded_2(block, sides, width):
    for axis, dim in sides:
        count = lax.axis_size(axis)
        forward = [(i, i + 1) for i in range(count - 1)]
        backward = [(target, source) for source, target in forward]
        low = lax.ppermute(
            lax.slice_in_dim(block, block.shape[dim] - width, None, axis=dim), axis, forward
        )
        high = lax.ppermute(lax.slice_in_dim(block, 0, width, axis=dim), axis, backward)
        block = jnp.concatenate([low, block, high], axis=dim)
    return block


YPAD = 8


def step_kernel(u_ref, xlo_ref, xhi_ref, ylo_ref, yhi_ref, prev_ref, mod_ref, src_ref, out_ref, up_ref, *, bx):
    i = pl.program_id(0)
    nx, ny = u_ref.shape[1], u_ref.shape[2]

    @pl.when(i == 0)
    def _():
        for c in range(3):
            def fill(x, carry):
                up_ref[c, x + 2, pl.ds(YPAD, ny), :] = u_ref[c, x]
                return carry

            lax.fori_loop(0, nx, fill, 0)
        up_ref[:, 0:2, pl.ds(YPAD, ny), :] = xlo_ref[...]
        up_ref[:, nx + 2:nx + 4, pl.ds(YPAD, ny), :] = xhi_ref[...]
        up_ref[:, :, pl.ds(YPAD - 2, 2), :] = ylo_ref[...]
        up_ref[:, :, pl.ds(YPAD + ny, 2), :] = yhi_ref[...]

    depth = out_ref.shape[3]
    lane = lax.broadcasted_iota(jnp.int32, (8, depth), 1)
    masks = {dz: (lane + dz >= 0) & (lane + dz < depth) for dz in (-2, -1, 1, 2)}

    def zs(v, dz):
        if dz == 0:
            return v
        return jnp.where(masks[dz], pltpu.roll(v, (-dz) % depth, 1), 0.0)

    def plane(p, carry):
        xp = i * bx + p + 2
        for g in range(out_ref.shape[2] // 8):
            def load(c, dx, dy):
                return up_ref[c, xp + dx, pl.ds(8 * g + YPAD + dy, 8), :]

            lam = mod_ref[0, p, pl.ds(8 * g, 8), :]
            mu = mod_ref[1, p, pl.ds(8 * g, 8), :]
            shear = mu * (1.0 / 12.0)
            stiff = lam * (1.0 / 12.0) + 2.0 * shear
            coup = (lam + mu) * 0.25
            centre_weight = -30.0 * (stiff + 2.0 * shear)
            centers = [load(c, 0, 0) for c in range(3)]

            def sums(c, axis):
                center = centers[c]
                near = None
                far = None
                for off in (-1, 1, -2, 2):
                    if axis == 0:
                        t = load(c, off, 0)
                    elif axis == 1:
                        t = load(c, 0, off)
                    else:
                        t = zs(center, off)
                    if abs(off) == 1:
                        near = t if near is None else near + t
                    else:
                        far = t if far is None else far + t
                return near, far

            def mixed(p_c, a, b):
                if 2 in (a, b):
                    n = a + b - 2
                    d = [0, 0]
                    d[n] = 1
                    step = load(p_c, d[0], d[1])
                    d[n] = -1
                    diff = step - load(p_c, d[0], d[1])
                    return zs(diff, 1) - zs(diff, -1)
                acc = None
                for sa in (1, -1):
                    for sb in (1, -1):
                        d = [0, 0, 0]
                        d[a] = sa
                        d[b] = sb
                        t = zs(load(p_c, d[0], d[1]), d[2])
                        if acc is None:
                            acc = t
                        elif sa * sb > 0:
                            acc = acc + t
                        else:
                            acc = acc - t
                return acc

            for c in range(3):
                others = [e for e in range(3) if e != c]
                near_c, far_c = sums(c, c)
                near_a, far_a = sums(c, others[0])
                near_b, far_b = sums(c, others[1])
                near = stiff * near_c + shear * (near_a + near_b)
                far = stiff * far_c + shear * (far_a + far_b)
                second = 16.0 * near - far + centre_weight * centers[c]
                cross = mixed(others[0], c, others[0]) + mixed(others[1], c, others[1])
                upd = second + coup * cross
                prev = prev_ref[c, p, pl.ds(8 * g, 8), :]
                src = src_ref[c, p, pl.ds(8 * g, 8), :]
                out_ref[c, p, pl.ds(8 * g, 8), :] = (2.0 * centers[c] - prev + upd) + src
        return carry

    lax.fori_loop(0, bx, plane, 0)


def elastic_step(u, xlo, xhi, ylo, yhi, prev, moduli, sources, bx=16):
    _, nx, ny, depth = u.shape
    kernel = functools.partial(step_kernel, bx=bx)
    block = lambda i: (0, i, 0, 0)
    whole = lambda i: (0, 0, 0, 0)
    return pl.pallas_call(
        kernel,
        grid=(nx // bx,),
        in_specs=[
            pl.BlockSpec(u.shape, whole),
            pl.BlockSpec(xlo.shape, whole),
            pl.BlockSpec(xhi.shape, whole),
            pl.BlockSpec(ylo.shape, whole),
            pl.BlockSpec(yhi.shape, whole),
            pl.BlockSpec((3, bx, ny, depth), block),
            pl.BlockSpec((2, bx, ny, depth), block),
            pl.BlockSpec((3, bx, ny, depth), block),
        ],
        out_specs=pl.BlockSpec((3, bx, ny, depth), block),
        out_shape=jax.ShapeDtypeStruct((3, nx, ny, depth), jnp.float32),
        scratch_shapes=[pltpu.VMEM((3, nx + 4, ny + 2 * YPAD, depth), jnp.float32)],
        compiler_params=pltpu.CompilerParams(dimension_semantics=("arbitrary",)),
    )(u, xlo, xhi, ylo, yhi, prev, moduli, sources)


def halos(block, width):
    size_x = lax.axis_size("gx")
    size_y = lax.axis_size("gy")
    nx, ny = block.shape[1], block.shape[2]
    forward_x = [(i, i + 1) for i in range(size_x - 1)]
    backward_x = [(t, s) for s, t in forward_x]
    xlo = lax.ppermute(block[:, nx - width:], "gx", forward_x)
    xhi = lax.ppermute(block[:, :width], "gx", backward_x)
    forward_y = [(i, i + 1) for i in range(size_y - 1)]
    backward_y = [(t, s) for s, t in forward_y]
    rows = lambda sl: jnp.concatenate([xlo[:, :, sl], block[:, :, sl], xhi[:, :, sl]], axis=1)
    ylo = lax.ppermute(rows(slice(ny - width, ny)), "gy", forward_y)
    yhi = lax.ppermute(rows(slice(0, width)), "gy", backward_y)
    return xlo, xhi, ylo, yhi


def level_table(values, layer_of_level):
    one_hot = (
        layer_of_level[:, None] == jnp.arange(values.shape[0], dtype=jnp.int32)[None, :]
    ).astype(jnp.float32)
    return jnp.sum(one_hot * values[None, :], axis=1)


def wave_kernel(angular, slowness, rigidity, damping, count_k):
    wavenum = (jnp.arange(count_k, dtype=jnp.float32) + 0.5) * (4.0 / count_k)
    spread = angular[None, :, None] * slowness[:, None, None]
    vertical = jnp.sqrt(wavenum[None, None, :] * wavenum[None, None, :] + spread * spread)
    impedance = rigidity[:, None, None] * vertical
    beneath = jnp.concatenate([impedance[1:], impedance[-1:]], axis=0)
    reflect = (impedance - beneath) / (impedance + beneath)
    fading = jnp.exp(-2.0 * step_depth * vertical * damping[:, None, None])
    two_way = 2.0 * step_depth * vertical
    trip_re = fading * jnp.cos(two_way)
    trip_im = -fading * jnp.sin(two_way)

    def upward(state_in, layer_data):
        refl_re, refl_im = state_in
        coefficient, along_re, along_im = layer_data
        upper_re = coefficient + refl_re
        lower_re = 1.0 + coefficient * refl_re
        lower_im = coefficient * refl_im
        magnitude = lower_re * lower_re + lower_im * lower_im
        ratio_re = (upper_re * lower_re + refl_im * lower_im) / magnitude
        ratio_im = (refl_im * lower_re - upper_re * lower_im) / magnitude
        fresh_re = along_re * ratio_re - along_im * ratio_im
        fresh_im = along_re * ratio_im + along_im * ratio_re
        return ((fresh_re, fresh_im), (fresh_re, fresh_im))

    bottom = jnp.zeros(vertical.shape[1:], jnp.float32)
    _, (refl_re, refl_im) = lax.scan(
        upward, (bottom, bottom), (reflect, trip_re, trip_im), reverse=True
    )
    travel = step_depth * vertical
    phases = jnp.cumsum(travel, axis=0) - travel
    absorbed = travel * damping[:, None, None]
    losses = jnp.cumsum(absorbed, axis=0) - absorbed
    down_size = jnp.exp(-losses)
    down_re = down_size * jnp.cos(phases)
    down_im = -down_size * jnp.sin(phases)
    weight = 1.0 / math.sqrt(count_k)
    kernel_re = weight * (down_re * (1.0 + refl_re) - down_im * refl_im)
    kernel_im = weight * (down_re * refl_im + down_im * (1.0 + refl_re))
    return jnp.transpose(jnp.stack([kernel_re, kernel_im]), (0, 2, 1, 3))


def offset_basis(count_k, count_r):
    modulus = count_k * count_r // 2
    low_count = 64
    odd_index = 2 * jnp.arange(count_k, dtype=jnp.int32) + 1
    high = jnp.arange(count_r // low_count, dtype=jnp.int32) * low_count
    low = jnp.arange(low_count, dtype=jnp.int32)
    scale = 2.0 * math.pi / modulus
    high_angle = (odd_index[:, None] * high[None, :] % modulus).astype(jnp.float32) * scale
    low_angle = (odd_index[:, None] * low[None, :] % modulus).astype(jnp.float32) * scale
    cos_h, sin_h = jnp.cos(high_angle), jnp.sin(high_angle)
    cos_l, sin_l = jnp.cos(low_angle), jnp.sin(low_angle)
    basis = cos_h[:, :, None] * cos_l[:, None, :] - sin_h[:, :, None] * sin_l[:, None, :]
    basis = basis.reshape(count_k, count_r).astype(jnp.bfloat16)
    return lax.optimization_barrier(basis)


def time_basis(freq_ids, count_f, count_steps, first_time):
    period = 2 * count_f
    times = first_time + jnp.arange(count_steps, dtype=jnp.int32)
    turns = (freq_ids[None, :] + 1) * times[:, None] % period
    angles = turns.astype(jnp.float32) * (2.0 * math.pi / period)
    weight = 1.0 / math.sqrt(count_f)
    return jnp.stack([weight * jnp.cos(angles), -weight * jnp.sin(angles)], axis=1)


def shifted(grid_block, step_x, step_y, step_z):
    width_x = grid_block.shape[0] - 4
    width_y = grid_block.shape[1] - 4
    width_z = grid_block.shape[2] - 4
    return grid_block[
        2 + step_x : 2 + step_x + width_x,
        2 + step_y : 2 + step_y + width_y,
        2 + step_z : 2 + step_z + width_z,
    ]


def curvature(grid_block, first_axis):
    summed = None
    for offset, factor in [(-2, -1.0), (-1, 16.0), (0, -30.0), (1, 16.0), (2, -1.0)]:
        moves = tuple((offset if index == first_axis else 0 for index in range(3)))
        contrib = factor * shifted(grid_block, moves[0], moves[1], moves[2])
        summed = contrib if summed is None else summed + contrib
    return summed / 12.0


def mixed(grid_block, first_axis, second_axis):
    summed = None
    for sign_a, sign_b, factor in [(1, 1, 1.0), (1, -1, -1.0), (-1, 1, -1.0), (-1, -1, 1.0)]:
        moves = tuple(
            (
                sign_a if index == first_axis else sign_b if index == second_axis else 0
                for index in range(3)
            )
        )
        contrib = factor * shifted(grid_block, moves[0], moves[1], moves[2])
        summed = contrib if summed is None else summed + contrib
    return summed / 4.0


def elastic(padded, moduli):
    first_lame = moduli[0]
    shear_mod = moduli[1]
    stiffness = first_lame + 2.0 * shear_mod
    coupling = first_lame + shear_mod
    result = []
    for component in range(3):
        update = stiffness * curvature(padded[component], component)
        for partner in range(3):
            if partner != component:
                update = update + shear_mod * curvature(padded[component], partner)
                update = update + coupling * mixed(padded[partner], component, partner)
        result.append(update)
    return jnp.stack(result)


def shards(
    layer_slowness,
    layer_rigidity,
    layer_damping,
    layer_of_level,
    slot_offset,
    slot_level,
    slot_target,
    live_count,
    moduli,
    field_old,
    field_now,
):
    size_gx = lax.axis_size("gx")
    size_gy = lax.axis_size("gy")
    groups = size_gx * size_gy
    per_device = F // groups
    device = lax.axis_index("gx") * size_gy + lax.axis_index("gy")
    freq_ids = device * per_device + jnp.arange(per_device, dtype=jnp.int32)
    angular = (freq_ids + 1).astype(jnp.float32) * (4.0 / F)
    slowness = level_table(layer_slowness, layer_of_level)
    rigidity = level_table(layer_rigidity, layer_of_level)
    damping = level_table(layer_damping, layer_of_level)
    kernel = wave_kernel(angular, slowness, rigidity, damping, NK).astype(jnp.bfloat16)
    cosines = offset_basis(NK, NR)
    spectrum_table = jnp.dot(
        kernel.reshape(2 * per_device * ND, NK), cosines, preferred_element_type=jnp.float32
    )
    table_rounded = spectrum_table.astype(jnp.bfloat16)
    all_slots = slot_offset.shape[0]
    width = math.gcd(all_slots, 4096)
    count_blocks = all_slots // width
    offset_blocks = slot_offset.reshape(count_blocks, width)
    level_blocks = slot_level.reshape(count_blocks, width)

    def select_block(pair):
        offsets, levels = pair
        offset_hot = (jnp.arange(NR, dtype=jnp.int32)[:, None] == offsets[None, :]).astype(
            jnp.bfloat16
        )
        rows = jnp.dot(table_rounded, offset_hot, preferred_element_type=jnp.float32).reshape(
            2, per_device, ND, width
        )
        level_hot = (jnp.arange(ND, dtype=jnp.int32)[:, None] == levels[None, :]).astype(
            jnp.float32
        )
        return jnp.sum(rows * level_hot[None, None, :, :], axis=2)

    selected = lax.map(select_block, (offset_blocks, level_blocks))
    spectra = (
        jnp.transpose(selected, (1, 2, 0, 3)).reshape(2, per_device, all_slots).astype(jnp.bfloat16)
    )
    slots_dev = slot_target.shape[0]
    occupied = (jnp.arange(slots_dev, dtype=jnp.int32) < live_count[0]).astype(jnp.float32)
    parcel = spectra.reshape(2, per_device, groups, slots_dev)
    arrived = lax.all_to_all(parcel, ("gx", "gy"), split_axis=2, concat_axis=1, tiled=True)
    freq_order = jnp.arange(F, dtype=jnp.int32)
    waveforms = time_basis(freq_order, F, STEPS, TSTART).reshape(STEPS, 2 * F)
    traces = jnp.dot(
        waveforms,
        arrived.reshape(2 * F, slots_dev).astype(jnp.float32),
        precision=lax.Precision.HIGHEST,
    )
    block_x = field_now.shape[1]
    block_y = field_now.shape[2]
    depth = field_now.shape[3]
    columns = slot_target // depth
    layer_z = slot_target % depth
    weighted = traces * occupied[None, :]
    column_hot = (
        jnp.arange(3 * block_x * block_y, dtype=jnp.int32)[:, None] == columns[None, :]
    ).astype(jnp.float32)
    depth_hot = (layer_z[:, None] == jnp.arange(depth, dtype=jnp.int32)[None, :]).astype(
        jnp.float32
    )
    previous, current = (field_old, field_now)
    for instant in range(STEPS):
        spread = weighted[instant][:, None] * depth_hot
        source = jnp.dot(column_hot, spread, precision=lax.Precision.HIGHEST)
        source = source.reshape(3, block_x, block_y, depth)
        xlo, xhi, ylo, yhi = halos(current, 2)
        advanced = elastic_step(current, xlo, xhi, ylo, yhi, previous, moduli, source)
        previous, current = (current, advanced)
    return (current, previous)


def solution(mesh):
    in_specs = (
        P(),
        P(),
        P(),
        P(),
        P(),
        P(),
        P(("gx", "gy")),
        P(("gx", "gy")),
        P(None, "gx", "gy", None),
        P(None, "gx", "gy", None),
        P(None, "gx", "gy", None),
    )
    out_specs = (P(None, "gx", "gy", None), P(None, "gx", "gy", None))
    return jax.shard_map(shards, mesh=mesh, in_specs=in_specs, out_specs=out_specs, check_vma=False)
```

```python
import math

import jax
import jax.numpy as jnp
from jax import lax
from jax.sharding import PartitionSpec as P
from jax.experimental import pallas as pl
from jax.experimental.pallas import tpu as pltpu
import functools

F = 128
NK = 1024
NR = 2048
ND = 32
STEPS = 4
TSTART = 32


step_depth = 0.25


def padded_2(block, sides, width):
    for axis, dim in sides:
        count = lax.axis_size(axis)
        forward = [(i, i + 1) for i in range(count - 1)]
        backward = [(target, source) for source, target in forward]
        low = lax.ppermute(
            lax.slice_in_dim(block, block.shape[dim] - width, None, axis=dim), axis, forward
        )
        high = lax.ppermute(lax.slice_in_dim(block, 0, width, axis=dim), axis, backward)
        block = jnp.concatenate([low, block, high], axis=dim)
    return block


YPAD = 8


def step_kernel(u_ref, xlo_ref, xhi_ref, ylo_ref, yhi_ref, prev_ref, mod_ref, src_ref, out_ref, up_ref, *, bx):
    i = pl.program_id(0)
    nx, ny = u_ref.shape[1], u_ref.shape[2]

    @pl.when(i == 0)
    def _():
        for c in range(3):
            def fill(x, carry):
                up_ref[c, x + 2, pl.ds(YPAD, ny), :] = u_ref[c, x]
                return carry

            lax.fori_loop(0, nx, fill, 0)
        up_ref[:, 0:2, pl.ds(YPAD, ny), :] = xlo_ref[...]
        up_ref[:, nx + 2:nx + 4, pl.ds(YPAD, ny), :] = xhi_ref[...]
        up_ref[:, :, pl.ds(YPAD - 2, 2), :] = ylo_ref[...]
        up_ref[:, :, pl.ds(YPAD + ny, 2), :] = yhi_ref[...]

    depth = out_ref.shape[3]
    lane = lax.broadcasted_iota(jnp.int32, (8, depth), 1)
    masks = {dz: (lane + dz >= 0) & (lane + dz < depth) for dz in (-2, -1, 1, 2)}

    def zs(v, dz):
        if dz == 0:
            return v
        return jnp.where(masks[dz], pltpu.roll(v, (-dz) % depth, 1), 0.0)

    def plane(p, carry):
        xp = i * bx + p + 2
        for g in range(out_ref.shape[2] // 8):
            def load(c, dx, dy):
                return up_ref[c, xp + dx, pl.ds(8 * g + YPAD + dy, 8), :]

            lam = mod_ref[0, p, pl.ds(8 * g, 8), :]
            mu = mod_ref[1, p, pl.ds(8 * g, 8), :]
            shear = mu * (1.0 / 12.0)
            stiff = lam * (1.0 / 12.0) + 2.0 * shear
            coup = (lam + mu) * 0.25
            centre_weight = -30.0 * (stiff + 2.0 * shear)
            centers = [load(c, 0, 0) for c in range(3)]

            def sums(c, axis):
                center = centers[c]
                near = None
                far = None
                for off in (-1, 1, -2, 2):
                    if axis == 0:
                        t = load(c, off, 0)
                    elif axis == 1:
                        t = load(c, 0, off)
                    else:
                        t = zs(center, off)
                    if abs(off) == 1:
                        near = t if near is None else near + t
                    else:
                        far = t if far is None else far + t
                return near, far

            def mixed(p_c, a, b):
                if 2 in (a, b):
                    n = a + b - 2
                    d = [0, 0]
                    d[n] = 1
                    step = load(p_c, d[0], d[1])
                    d[n] = -1
                    diff = step - load(p_c, d[0], d[1])
                    return zs(diff, 1) - zs(diff, -1)
                acc = None
                for sa in (1, -1):
                    for sb in (1, -1):
                        d = [0, 0, 0]
                        d[a] = sa
                        d[b] = sb
                        t = zs(load(p_c, d[0], d[1]), d[2])
                        if acc is None:
                            acc = t
                        elif sa * sb > 0:
                            acc = acc + t
                        else:
                            acc = acc - t
                return acc

            for c in range(3):
                others = [e for e in range(3) if e != c]
                near_c, far_c = sums(c, c)
                near_a, far_a = sums(c, others[0])
                near_b, far_b = sums(c, others[1])
                near = stiff * near_c + shear * (near_a + near_b)
                far = stiff * far_c + shear * (far_a + far_b)
                second = 16.0 * near - far + centre_weight * centers[c]
                cross = mixed(others[0], c, others[0]) + mixed(others[1], c, others[1])
                upd = second + coup * cross
                prev = prev_ref[c, p, pl.ds(8 * g, 8), :]
                src = src_ref[c, p, pl.ds(8 * g, 8), :]
                out_ref[c, p, pl.ds(8 * g, 8), :] = (2.0 * centers[c] - prev + upd) + src
        return carry

    lax.fori_loop(0, bx, plane, 0)


def elastic_step(u, xlo, xhi, ylo, yhi, prev, moduli, sources, bx=4):
    _, nx, ny, depth = u.shape
    kernel = functools.partial(step_kernel, bx=bx)
    block = lambda i: (0, i, 0, 0)
    whole = lambda i: (0, 0, 0, 0)
    return pl.pallas_call(
        kernel,
        grid=(nx // bx,),
        in_specs=[
            pl.BlockSpec(u.shape, whole),
            pl.BlockSpec(xlo.shape, whole),
            pl.BlockSpec(xhi.shape, whole),
            pl.BlockSpec(ylo.shape, whole),
            pl.BlockSpec(yhi.shape, whole),
            pl.BlockSpec((3, bx, ny, depth), block),
            pl.BlockSpec((2, bx, ny, depth), block),
            pl.BlockSpec((3, bx, ny, depth), block),
        ],
        out_specs=pl.BlockSpec((3, bx, ny, depth), block),
        out_shape=jax.ShapeDtypeStruct((3, nx, ny, depth), jnp.float32),
        scratch_shapes=[pltpu.VMEM((3, nx + 4, ny + 2 * YPAD, depth), jnp.float32)],
        compiler_params=pltpu.CompilerParams(dimension_semantics=("arbitrary",)),
    )(u, xlo, xhi, ylo, yhi, prev, moduli, sources)


def halos(block, width):
    size_x = lax.axis_size("gx")
    size_y = lax.axis_size("gy")
    nx, ny = block.shape[1], block.shape[2]
    forward_x = [(i, i + 1) for i in range(size_x - 1)]
    backward_x = [(t, s) for s, t in forward_x]
    xlo = lax.ppermute(block[:, nx - width:], "gx", forward_x)
    xhi = lax.ppermute(block[:, :width], "gx", backward_x)
    forward_y = [(i, i + 1) for i in range(size_y - 1)]
    backward_y = [(t, s) for s, t in forward_y]
    rows = lambda sl: jnp.concatenate([xlo[:, :, sl], block[:, :, sl], xhi[:, :, sl]], axis=1)
    ylo = lax.ppermute(rows(slice(ny - width, ny)), "gy", forward_y)
    yhi = lax.ppermute(rows(slice(0, width)), "gy", backward_y)
    return xlo, xhi, ylo, yhi


def level_table(values, layer_of_level):
    one_hot = (
        layer_of_level[:, None] == jnp.arange(values.shape[0], dtype=jnp.int32)[None, :]
    ).astype(jnp.float32)
    return jnp.sum(one_hot * values[None, :], axis=1)


def wave_kernel(angular, slowness, rigidity, damping, count_k):
    wavenum = (jnp.arange(count_k, dtype=jnp.float32) + 0.5) * (4.0 / count_k)
    spread = angular[None, :, None] * slowness[:, None, None]
    vertical = jnp.sqrt(wavenum[None, None, :] * wavenum[None, None, :] + spread * spread)
    impedance = rigidity[:, None, None] * vertical
    beneath = jnp.concatenate([impedance[1:], impedance[-1:]], axis=0)
    reflect = (impedance - beneath) / (impedance + beneath)
    fading = jnp.exp(-2.0 * step_depth * vertical * damping[:, None, None])
    two_way = 2.0 * step_depth * vertical
    trip_re = fading * jnp.cos(two_way)
    trip_im = -fading * jnp.sin(two_way)

    def upward(state_in, layer_data):
        refl_re, refl_im = state_in
        coefficient, along_re, along_im = layer_data
        upper_re = coefficient + refl_re
        lower_re = 1.0 + coefficient * refl_re
        lower_im = coefficient * refl_im
        magnitude = lower_re * lower_re + lower_im * lower_im
        ratio_re = (upper_re * lower_re + refl_im * lower_im) / magnitude
        ratio_im = (refl_im * lower_re - upper_re * lower_im) / magnitude
        fresh_re = along_re * ratio_re - along_im * ratio_im
        fresh_im = along_re * ratio_im + along_im * ratio_re
        return ((fresh_re, fresh_im), (fresh_re, fresh_im))

    bottom = jnp.zeros(vertical.shape[1:], jnp.float32)
    _, (refl_re, refl_im) = lax.scan(
        upward, (bottom, bottom), (reflect, trip_re, trip_im), reverse=True
    )
    travel = step_depth * vertical
    phases = jnp.cumsum(travel, axis=0) - travel
    absorbed = travel * damping[:, None, None]
    losses = jnp.cumsum(absorbed, axis=0) - absorbed
    down_size = jnp.exp(-losses)
    down_re = down_size * jnp.cos(phases)
    down_im = -down_size * jnp.sin(phases)
    weight = 1.0 / math.sqrt(count_k)
    kernel_re = weight * (down_re * (1.0 + refl_re) - down_im * refl_im)
    kernel_im = weight * (down_re * refl_im + down_im * (1.0 + refl_re))
    return jnp.transpose(jnp.stack([kernel_re, kernel_im]), (0, 2, 1, 3))


def offset_basis(count_k, count_r):
    modulus = count_k * count_r // 2
    low_count = 64
    odd_index = 2 * jnp.arange(count_k, dtype=jnp.int32) + 1
    high = jnp.arange(count_r // low_count, dtype=jnp.int32) * low_count
    low = jnp.arange(low_count, dtype=jnp.int32)
    scale = 2.0 * math.pi / modulus
    high_angle = (odd_index[:, None] * high[None, :] % modulus).astype(jnp.float32) * scale
    low_angle = (odd_index[:, None] * low[None, :] % modulus).astype(jnp.float32) * scale
    cos_h, sin_h = jnp.cos(high_angle), jnp.sin(high_angle)
    cos_l, sin_l = jnp.cos(low_angle), jnp.sin(low_angle)
    basis = cos_h[:, :, None] * cos_l[:, None, :] - sin_h[:, :, None] * sin_l[:, None, :]
    basis = basis.reshape(count_k, count_r).astype(jnp.bfloat16)
    return lax.optimization_barrier(basis)


def time_basis(freq_ids, count_f, count_steps, first_time):
    period = 2 * count_f
    times = first_time + jnp.arange(count_steps, dtype=jnp.int32)
    turns = (freq_ids[None, :] + 1) * times[:, None] % period
    angles = turns.astype(jnp.float32) * (2.0 * math.pi / period)
    weight = 1.0 / math.sqrt(count_f)
    return jnp.stack([weight * jnp.cos(angles), -weight * jnp.sin(angles)], axis=1)


def shifted(grid_block, step_x, step_y, step_z):
    width_x = grid_block.shape[0] - 4
    width_y = grid_block.shape[1] - 4
    width_z = grid_block.shape[2] - 4
    return grid_block[
        2 + step_x : 2 + step_x + width_x,
        2 + step_y : 2 + step_y + width_y,
        2 + step_z : 2 + step_z + width_z,
    ]


def curvature(grid_block, first_axis):
    summed = None
    for offset, factor in [(-2, -1.0), (-1, 16.0), (0, -30.0), (1, 16.0), (2, -1.0)]:
        moves = tuple((offset if index == first_axis else 0 for index in range(3)))
        contrib = factor * shifted(grid_block, moves[0], moves[1], moves[2])
        summed = contrib if summed is None else summed + contrib
    return summed / 12.0


def mixed(grid_block, first_axis, second_axis):
    summed = None
    for sign_a, sign_b, factor in [(1, 1, 1.0), (1, -1, -1.0), (-1, 1, -1.0), (-1, -1, 1.0)]:
        moves = tuple(
            (
                sign_a if index == first_axis else sign_b if index == second_axis else 0
                for index in range(3)
            )
        )
        contrib = factor * shifted(grid_block, moves[0], moves[1], moves[2])
        summed = contrib if summed is None else summed + contrib
    return summed / 4.0


def elastic(padded, moduli):
    first_lame = moduli[0]
    shear_mod = moduli[1]
    stiffness = first_lame + 2.0 * shear_mod
    coupling = first_lame + shear_mod
    result = []
    for component in range(3):
        update = stiffness * curvature(padded[component], component)
        for partner in range(3):
            if partner != component:
                update = update + shear_mod * curvature(padded[component], partner)
                update = update + coupling * mixed(padded[partner], component, partner)
        result.append(update)
    return jnp.stack(result)


def shards(
    layer_slowness,
    layer_rigidity,
    layer_damping,
    layer_of_level,
    slot_offset,
    slot_level,
    slot_target,
    live_count,
    moduli,
    field_old,
    field_now,
):
    size_gx = lax.axis_size("gx")
    size_gy = lax.axis_size("gy")
    groups = size_gx * size_gy
    per_device = F // groups
    device = lax.axis_index("gx") * size_gy + lax.axis_index("gy")
    freq_ids = device * per_device + jnp.arange(per_device, dtype=jnp.int32)
    angular = (freq_ids + 1).astype(jnp.float32) * (4.0 / F)
    slowness = level_table(layer_slowness, layer_of_level)
    rigidity = level_table(layer_rigidity, layer_of_level)
    damping = level_table(layer_damping, layer_of_level)
    kernel = wave_kernel(angular, slowness, rigidity, damping, NK).astype(jnp.bfloat16)
    cosines = offset_basis(NK, NR)
    spectrum_table = jnp.dot(
        kernel.reshape(2 * per_device * ND, NK), cosines, preferred_element_type=jnp.float32
    )
    table_rounded = spectrum_table.astype(jnp.bfloat16)
    all_slots = slot_offset.shape[0]
    width = math.gcd(all_slots, 4096)
    count_blocks = all_slots // width
    offset_blocks = slot_offset.reshape(count_blocks, width)
    level_blocks = slot_level.reshape(count_blocks, width)

    def select_block(pair):
        offsets, levels = pair
        offset_hot = (jnp.arange(NR, dtype=jnp.int32)[:, None] == offsets[None, :]).astype(
            jnp.bfloat16
        )
        rows = jnp.dot(table_rounded, offset_hot, preferred_element_type=jnp.float32).reshape(
            2, per_device, ND, width
        )
        level_hot = (jnp.arange(ND, dtype=jnp.int32)[:, None] == levels[None, :]).astype(
            jnp.float32
        )
        return jnp.sum(rows * level_hot[None, None, :, :], axis=2)

    selected = lax.map(select_block, (offset_blocks, level_blocks))
    spectra = (
        jnp.transpose(selected, (1, 2, 0, 3)).reshape(2, per_device, all_slots).astype(jnp.bfloat16)
    )
    slots_dev = slot_target.shape[0]
    occupied = (jnp.arange(slots_dev, dtype=jnp.int32) < live_count[0]).astype(jnp.float32)
    parcel = spectra.reshape(2, per_device, groups, slots_dev)
    arrived = lax.all_to_all(parcel, ("gx", "gy"), split_axis=2, concat_axis=1, tiled=True)
    freq_order = jnp.arange(F, dtype=jnp.int32)
    waveforms = time_basis(freq_order, F, STEPS, TSTART).reshape(STEPS, 2 * F)
    traces = jnp.dot(
        waveforms,
        arrived.reshape(2 * F, slots_dev).astype(jnp.float32),
        precision=lax.Precision.HIGHEST,
    )
    block_x = field_now.shape[1]
    block_y = field_now.shape[2]
    depth = field_now.shape[3]
    columns = slot_target // depth
    layer_z = slot_target % depth
    weighted = traces * occupied[None, :]
    column_hot = (
        jnp.arange(3 * block_x * block_y, dtype=jnp.int32)[:, None] == columns[None, :]
    ).astype(jnp.float32)
    depth_hot = (layer_z[:, None] == jnp.arange(depth, dtype=jnp.int32)[None, :]).astype(
        jnp.float32
    )
    previous, current = (field_old, field_now)
    for instant in range(STEPS):
        spread = weighted[instant][:, None] * depth_hot
        source = jnp.dot(column_hot, spread, precision=lax.Precision.HIGHEST)
        source = source.reshape(3, block_x, block_y, depth)
        xlo, xhi, ylo, yhi = halos(current, 2)
        advanced = elastic_step(current, xlo, xhi, ylo, yhi, previous, moduli, source)
        previous, current = (current, advanced)
    return (current, previous)


def solution(mesh):
    in_specs = (
        P(),
        P(),
        P(),
        P(),
        P(),
        P(),
        P(("gx", "gy")),
        P(("gx", "gy")),
        P(None, "gx", "gy", None),
        P(None, "gx", "gy", None),
        P(None, "gx", "gy", None),
    )
    out_specs = (P(None, "gx", "gy", None), P(None, "gx", "gy", None))
    return jax.shard_map(shards, mesh=mesh, in_specs=in_specs, out_specs=out_specs, check_vma=False)
```

```python
import math

import jax
import jax.numpy as jnp
from jax import lax
from jax.sharding import PartitionSpec as P
from jax.experimental import pallas as pl
from jax.experimental.pallas import tpu as pltpu
import functools

F = 128
NK = 1024
NR = 2048
ND = 32
STEPS = 4
TSTART = 32


step_depth = 0.25


def padded_2(block, sides, width):
    for axis, dim in sides:
        count = lax.axis_size(axis)
        forward = [(i, i + 1) for i in range(count - 1)]
        backward = [(target, source) for source, target in forward]
        low = lax.ppermute(
            lax.slice_in_dim(block, block.shape[dim] - width, None, axis=dim), axis, forward
        )
        high = lax.ppermute(lax.slice_in_dim(block, 0, width, axis=dim), axis, backward)
        block = jnp.concatenate([low, block, high], axis=dim)
    return block


YPAD = 8


def step_kernel(u_ref, xlo_ref, xhi_ref, ylo_ref, yhi_ref, prev_ref, mod_ref, src_ref, out_ref, up_ref, *, bx):
    i = pl.program_id(0)
    nx, ny = u_ref.shape[1], u_ref.shape[2]

    @pl.when(i == 0)
    def _():
        for c in range(3):
            def fill(x, carry):
                up_ref[c, x + 2, pl.ds(YPAD, ny), :] = u_ref[c, x]
                return carry

            lax.fori_loop(0, nx, fill, 0)
        up_ref[:, 0:2, pl.ds(YPAD, ny), :] = xlo_ref[...]
        up_ref[:, nx + 2:nx + 4, pl.ds(YPAD, ny), :] = xhi_ref[...]
        up_ref[:, :, pl.ds(YPAD - 2, 2), :] = ylo_ref[...]
        up_ref[:, :, pl.ds(YPAD + ny, 2), :] = yhi_ref[...]

    depth = out_ref.shape[3]
    lane = lax.broadcasted_iota(jnp.int32, (8, depth), 1)
    masks = {dz: (lane + dz >= 0) & (lane + dz < depth) for dz in (-2, -1, 1, 2)}

    def zs(v, dz):
        if dz == 0:
            return v
        return jnp.where(masks[dz], pltpu.roll(v, (-dz) % depth, 1), 0.0)

    def plane(p, carry):
        xp = i * bx + p + 2
        for g in range(out_ref.shape[2] // 8):
            def load(c, dx, dy):
                return up_ref[c, xp + dx, pl.ds(8 * g + YPAD + dy, 8), :]

            lam = mod_ref[0, p, pl.ds(8 * g, 8), :]
            mu = mod_ref[1, p, pl.ds(8 * g, 8), :]
            shear = mu * (1.0 / 12.0)
            stiff = lam * (1.0 / 12.0) + 2.0 * shear
            coup = (lam + mu) * 0.25
            centre_weight = -30.0 * (stiff + 2.0 * shear)
            centers = [load(c, 0, 0) for c in range(3)]

            def sums(c, axis):
                center = centers[c]
                near = None
                far = None
                for off in (-1, 1, -2, 2):
                    if axis == 0:
                        t = load(c, off, 0)
                    elif axis == 1:
                        t = load(c, 0, off)
                    else:
                        t = zs(center, off)
                    if abs(off) == 1:
                        near = t if near is None else near + t
                    else:
                        far = t if far is None else far + t
                return near, far

            def mixed(p_c, a, b):
                if 2 in (a, b):
                    n = a + b - 2
                    d = [0, 0]
                    d[n] = 1
                    step = load(p_c, d[0], d[1])
                    d[n] = -1
                    diff = step - load(p_c, d[0], d[1])
                    return zs(diff, 1) - zs(diff, -1)
                acc = None
                for sa in (1, -1):
                    for sb in (1, -1):
                        d = [0, 0, 0]
                        d[a] = sa
                        d[b] = sb
                        t = zs(load(p_c, d[0], d[1]), d[2])
                        if acc is None:
                            acc = t
                        elif sa * sb > 0:
                            acc = acc + t
                        else:
                            acc = acc - t
                return acc

            for c in range(3):
                others = [e for e in range(3) if e != c]
                near_c, far_c = sums(c, c)
                near_a, far_a = sums(c, others[0])
                near_b, far_b = sums(c, others[1])
                near = stiff * near_c + shear * (near_a + near_b)
                far = stiff * far_c + shear * (far_a + far_b)
                second = 16.0 * near - far + centre_weight * centers[c]
                cross = mixed(others[0], c, others[0]) + mixed(others[1], c, others[1])
                upd = second + coup * cross
                prev = prev_ref[c, p, pl.ds(8 * g, 8), :]
                src = src_ref[c, p, pl.ds(8 * g, 8), :]
                out_ref[c, p, pl.ds(8 * g, 8), :] = (2.0 * centers[c] - prev + upd) + src
        return carry

    lax.fori_loop(0, bx, plane, 0)


def elastic_step(u, xlo, xhi, ylo, yhi, prev, moduli, sources, bx=8):
    _, nx, ny, depth = u.shape
    kernel = functools.partial(step_kernel, bx=bx)
    block = lambda i: (0, i, 0, 0)
    whole = lambda i: (0, 0, 0, 0)
    return pl.pallas_call(
        kernel,
        grid=(nx // bx,),
        in_specs=[
            pl.BlockSpec(u.shape, whole),
            pl.BlockSpec(xlo.shape, whole),
            pl.BlockSpec(xhi.shape, whole),
            pl.BlockSpec(ylo.shape, whole),
            pl.BlockSpec(yhi.shape, whole),
            pl.BlockSpec((3, bx, ny, depth), block),
            pl.BlockSpec((2, bx, ny, depth), block),
            pl.BlockSpec((3, bx, ny, depth), block),
        ],
        out_specs=pl.BlockSpec((3, bx, ny, depth), block),
        out_shape=jax.ShapeDtypeStruct((3, nx, ny, depth), jnp.float32),
        scratch_shapes=[pltpu.VMEM((3, nx + 4, ny + 2 * YPAD, depth), jnp.float32)],
        compiler_params=pltpu.CompilerParams(dimension_semantics=("arbitrary",)),
    )(u, xlo, xhi, ylo, yhi, prev, moduli, sources)


def x_halos(block, width):
    size_x = lax.axis_size("gx")
    nx = block.shape[1]
    forward_x = [(i, i + 1) for i in range(size_x - 1)]
    backward_x = [(t, s) for s, t in forward_x]
    xlo = lax.ppermute(block[:, nx - width:], "gx", forward_x)
    xhi = lax.ppermute(block[:, :width], "gx", backward_x)
    return xlo, xhi


def y_halos(block, xlo, xhi, width):
    size_y = lax.axis_size("gy")
    ny = block.shape[2]
    forward_y = [(i, i + 1) for i in range(size_y - 1)]
    backward_y = [(t, s) for s, t in forward_y]
    rows = lambda sl: jnp.concatenate([xlo[:, :, sl], block[:, :, sl], xhi[:, :, sl]], axis=1)
    ylo = lax.ppermute(rows(slice(ny - width, ny)), "gy", forward_y)
    yhi = lax.ppermute(rows(slice(0, width)), "gy", backward_y)
    return ylo, yhi


def halos(block, width):
    xlo, xhi = x_halos(block, width)
    ylo, yhi = y_halos(block, xlo, xhi, width)
    return xlo, xhi, ylo, yhi


def level_table(values, layer_of_level):
    one_hot = (
        layer_of_level[:, None] == jnp.arange(values.shape[0], dtype=jnp.int32)[None, :]
    ).astype(jnp.float32)
    return jnp.sum(one_hot * values[None, :], axis=1)


def wave_kernel(angular, slowness, rigidity, damping, count_k):
    wavenum = (jnp.arange(count_k, dtype=jnp.float32) + 0.5) * (4.0 / count_k)
    spread = angular[None, :, None] * slowness[:, None, None]
    vertical = jnp.sqrt(wavenum[None, None, :] * wavenum[None, None, :] + spread * spread)
    impedance = rigidity[:, None, None] * vertical
    beneath = jnp.concatenate([impedance[1:], impedance[-1:]], axis=0)
    reflect = (impedance - beneath) / (impedance + beneath)
    fading = jnp.exp(-2.0 * step_depth * vertical * damping[:, None, None])
    two_way = 2.0 * step_depth * vertical
    trip_re = fading * jnp.cos(two_way)
    trip_im = -fading * jnp.sin(two_way)

    def upward(state_in, layer_data):
        refl_re, refl_im = state_in
        coefficient, along_re, along_im = layer_data
        upper_re = coefficient + refl_re
        lower_re = 1.0 + coefficient * refl_re
        lower_im = coefficient * refl_im
        magnitude = lower_re * lower_re + lower_im * lower_im
        ratio_re = (upper_re * lower_re + refl_im * lower_im) / magnitude
        ratio_im = (refl_im * lower_re - upper_re * lower_im) / magnitude
        fresh_re = along_re * ratio_re - along_im * ratio_im
        fresh_im = along_re * ratio_im + along_im * ratio_re
        return ((fresh_re, fresh_im), (fresh_re, fresh_im))

    bottom = jnp.zeros(vertical.shape[1:], jnp.float32)
    _, (refl_re, refl_im) = lax.scan(
        upward, (bottom, bottom), (reflect, trip_re, trip_im), reverse=True
    )
    travel = step_depth * vertical
    phases = jnp.cumsum(travel, axis=0) - travel
    absorbed = travel * damping[:, None, None]
    losses = jnp.cumsum(absorbed, axis=0) - absorbed
    down_size = jnp.exp(-losses)
    down_re = down_size * jnp.cos(phases)
    down_im = -down_size * jnp.sin(phases)
    weight = 1.0 / math.sqrt(count_k)
    kernel_re = weight * (down_re * (1.0 + refl_re) - down_im * refl_im)
    kernel_im = weight * (down_re * refl_im + down_im * (1.0 + refl_re))
    return jnp.transpose(jnp.stack([kernel_re, kernel_im]), (0, 2, 1, 3))


def offset_basis(count_k, count_r):
    modulus = count_k * count_r // 2
    low_count = 64
    odd_index = 2 * jnp.arange(count_k, dtype=jnp.int32) + 1
    high = jnp.arange(count_r // low_count, dtype=jnp.int32) * low_count
    low = jnp.arange(low_count, dtype=jnp.int32)
    scale = 2.0 * math.pi / modulus
    high_angle = (odd_index[:, None] * high[None, :] % modulus).astype(jnp.float32) * scale
    low_angle = (odd_index[:, None] * low[None, :] % modulus).astype(jnp.float32) * scale
    cos_h, sin_h = jnp.cos(high_angle), jnp.sin(high_angle)
    cos_l, sin_l = jnp.cos(low_angle), jnp.sin(low_angle)
    basis = cos_h[:, :, None] * cos_l[:, None, :] - sin_h[:, :, None] * sin_l[:, None, :]
    basis = basis.reshape(count_k, count_r).astype(jnp.bfloat16)
    return lax.optimization_barrier(basis)


def time_basis(freq_ids, count_f, count_steps, first_time):
    period = 2 * count_f
    times = first_time + jnp.arange(count_steps, dtype=jnp.int32)
    turns = (freq_ids[None, :] + 1) * times[:, None] % period
    angles = turns.astype(jnp.float32) * (2.0 * math.pi / period)
    weight = 1.0 / math.sqrt(count_f)
    return jnp.stack([weight * jnp.cos(angles), -weight * jnp.sin(angles)], axis=1)


def shifted(grid_block, step_x, step_y, step_z):
    width_x = grid_block.shape[0] - 4
    width_y = grid_block.shape[1] - 4
    width_z = grid_block.shape[2] - 4
    return grid_block[
        2 + step_x : 2 + step_x + width_x,
        2 + step_y : 2 + step_y + width_y,
        2 + step_z : 2 + step_z + width_z,
    ]


def curvature(grid_block, first_axis):
    summed = None
    for offset, factor in [(-2, -1.0), (-1, 16.0), (0, -30.0), (1, 16.0), (2, -1.0)]:
        moves = tuple((offset if index == first_axis else 0 for index in range(3)))
        contrib = factor * shifted(grid_block, moves[0], moves[1], moves[2])
        summed = contrib if summed is None else summed + contrib
    return summed / 12.0


def mixed(grid_block, first_axis, second_axis):
    summed = None
    for sign_a, sign_b, factor in [(1, 1, 1.0), (1, -1, -1.0), (-1, 1, -1.0), (-1, -1, 1.0)]:
        moves = tuple(
            (
                sign_a if index == first_axis else sign_b if index == second_axis else 0
                for index in range(3)
            )
        )
        contrib = factor * shifted(grid_block, moves[0], moves[1], moves[2])
        summed = contrib if summed is None else summed + contrib
    return summed / 4.0


def elastic(padded, moduli):
    first_lame = moduli[0]
    shear_mod = moduli[1]
    stiffness = first_lame + 2.0 * shear_mod
    coupling = first_lame + shear_mod
    result = []
    for component in range(3):
        update = stiffness * curvature(padded[component], component)
        for partner in range(3):
            if partner != component:
                update = update + shear_mod * curvature(padded[component], partner)
                update = update + coupling * mixed(padded[partner], component, partner)
        result.append(update)
    return jnp.stack(result)


def shards(
    layer_slowness,
    layer_rigidity,
    layer_damping,
    layer_of_level,
    slot_offset,
    slot_level,
    slot_target,
    live_count,
    moduli,
    field_old,
    field_now,
):
    size_gx = lax.axis_size("gx")
    size_gy = lax.axis_size("gy")
    groups = size_gx * size_gy
    per_device = F // groups
    device = lax.axis_index("gx") * size_gy + lax.axis_index("gy")
    freq_ids = device * per_device + jnp.arange(per_device, dtype=jnp.int32)
    angular = (freq_ids + 1).astype(jnp.float32) * (4.0 / F)
    slowness = level_table(layer_slowness, layer_of_level)
    rigidity = level_table(layer_rigidity, layer_of_level)
    damping = level_table(layer_damping, layer_of_level)
    kernel = wave_kernel(angular, slowness, rigidity, damping, NK).astype(jnp.bfloat16)
    cosines = offset_basis(NK, NR)
    spectrum_table = jnp.dot(
        kernel.reshape(2 * per_device * ND, NK), cosines, preferred_element_type=jnp.float32
    )
    table_rounded = spectrum_table.astype(jnp.bfloat16)
    later_now, table_rounded = lax.optimization_barrier((field_now, table_rounded))
    first_x = x_halos(later_now, 2)
    all_slots = slot_offset.shape[0]
    width = math.gcd(all_slots, 4096)
    count_blocks = all_slots // width
    offset_blocks = slot_offset.reshape(count_blocks, width)
    level_blocks = slot_level.reshape(count_blocks, width)

    def select_block(pair):
        offsets, levels = pair
        offset_hot = (jnp.arange(NR, dtype=jnp.int32)[:, None] == offsets[None, :]).astype(
            jnp.bfloat16
        )
        rows = jnp.dot(table_rounded, offset_hot, preferred_element_type=jnp.float32).reshape(
            2, per_device, ND, width
        )
        level_hot = (jnp.arange(ND, dtype=jnp.int32)[:, None] == levels[None, :]).astype(
            jnp.float32
        )
        return jnp.sum(rows * level_hot[None, None, :, :], axis=2)

    selected = lax.map(select_block, (offset_blocks, level_blocks))
    spectra = (
        jnp.transpose(selected, (1, 2, 0, 3)).reshape(2, per_device, all_slots).astype(jnp.bfloat16)
    )
    slots_dev = slot_target.shape[0]
    occupied = (jnp.arange(slots_dev, dtype=jnp.int32) < live_count[0]).astype(jnp.float32)
    first_x, spectra = lax.optimization_barrier((first_x, spectra))
    parcel = spectra.reshape(2, per_device, groups, slots_dev)
    arrived = lax.all_to_all(parcel, ("gx", "gy"), split_axis=2, concat_axis=1, tiled=True)
    freq_order = jnp.arange(F, dtype=jnp.int32)
    waveforms = time_basis(freq_order, F, STEPS, TSTART).reshape(STEPS, 2 * F)
    traces = jnp.dot(
        waveforms,
        arrived.reshape(2 * F, slots_dev).astype(jnp.float32),
        precision=lax.Precision.HIGHEST,
    )
    block_x = field_now.shape[1]
    block_y = field_now.shape[2]
    depth = field_now.shape[3]
    columns = slot_target // depth
    layer_z = slot_target % depth
    weighted = traces * occupied[None, :]
    column_hot = (
        jnp.arange(3 * block_x * block_y, dtype=jnp.int32)[:, None] == columns[None, :]
    ).astype(jnp.float32)
    depth_hot = (layer_z[:, None] == jnp.arange(depth, dtype=jnp.int32)[None, :]).astype(
        jnp.float32
    )
    previous, current = (field_old, field_now)
    for instant in range(STEPS):
        spread = weighted[instant][:, None] * depth_hot
        source = jnp.dot(column_hot, spread, precision=lax.Precision.HIGHEST)
        source = source.reshape(3, block_x, block_y, depth)
        if instant == 0:
            xlo, xhi = first_x
            ylo, yhi = y_halos(current, xlo, xhi, 2)
        else:
            xlo, xhi, ylo, yhi = halos(current, 2)
        advanced = elastic_step(current, xlo, xhi, ylo, yhi, previous, moduli, source)
        previous, current = (current, advanced)
    return (current, previous)


def solution(mesh):
    in_specs = (
        P(),
        P(),
        P(),
        P(),
        P(),
        P(),
        P(("gx", "gy")),
        P(("gx", "gy")),
        P(None, "gx", "gy", None),
        P(None, "gx", "gy", None),
        P(None, "gx", "gy", None),
    )
    out_specs = (P(None, "gx", "gy", None), P(None, "gx", "gy", None))
    return jax.shard_map(shards, mesh=mesh, in_specs=in_specs, out_specs=out_specs, check_vma=False)
```

```python
import math

import jax
import jax.numpy as jnp
from jax import lax
from jax.sharding import PartitionSpec as P
from jax.experimental import pallas as pl
from jax.experimental.pallas import tpu as pltpu
import functools

F = 128
NK = 1024
NR = 2048
ND = 32
STEPS = 4
TSTART = 32


step_depth = 0.25


def padded_2(block, sides, width):
    for axis, dim in sides:
        count = lax.axis_size(axis)
        forward = [(i, i + 1) for i in range(count - 1)]
        backward = [(target, source) for source, target in forward]
        low = lax.ppermute(
            lax.slice_in_dim(block, block.shape[dim] - width, None, axis=dim), axis, forward
        )
        high = lax.ppermute(lax.slice_in_dim(block, 0, width, axis=dim), axis, backward)
        block = jnp.concatenate([low, block, high], axis=dim)
    return block


YPAD = 8


def step_kernel(u_ref, xlo_ref, xhi_ref, ylo_ref, yhi_ref, prev_ref, mod_ref, src_ref, out_ref, up_ref, *, bx):
    i = pl.program_id(0)
    nx, ny = u_ref.shape[1], u_ref.shape[2]

    @pl.when(i == 0)
    def _():
        for c in range(3):
            def fill(x, carry):
                up_ref[c, x + 2, pl.ds(YPAD, ny), :] = u_ref[c, x]
                return carry

            lax.fori_loop(0, nx, fill, 0)
        up_ref[:, 0:2, pl.ds(YPAD, ny), :] = xlo_ref[...]
        up_ref[:, nx + 2:nx + 4, pl.ds(YPAD, ny), :] = xhi_ref[...]
        up_ref[:, :, pl.ds(YPAD - 2, 2), :] = ylo_ref[...]
        up_ref[:, :, pl.ds(YPAD + ny, 2), :] = yhi_ref[...]

    depth = out_ref.shape[3]
    lane = lax.broadcasted_iota(jnp.int32, (8, depth), 1)
    masks = {dz: (lane + dz >= 0) & (lane + dz < depth) for dz in (-2, -1, 1, 2)}

    def zs(v, dz):
        if dz == 0:
            return v
        return jnp.where(masks[dz], pltpu.roll(v, (-dz) % depth, 1), 0.0)

    def plane(p, carry):
        xp = i * bx + p + 2
        for g in range(out_ref.shape[2] // 8):
            def load(c, dx, dy):
                return up_ref[c, xp + dx, pl.ds(8 * g + YPAD + dy, 8), :]

            lam = mod_ref[0, p, pl.ds(8 * g, 8), :]
            mu = mod_ref[1, p, pl.ds(8 * g, 8), :]
            shear = mu * (1.0 / 12.0)
            stiff = lam * (1.0 / 12.0) + 2.0 * shear
            coup = (lam + mu) * 0.25
            centre_weight = -30.0 * (stiff + 2.0 * shear)
            centers = [load(c, 0, 0) for c in range(3)]

            def sums(c, axis):
                center = centers[c]
                near = None
                far = None
                for off in (-1, 1, -2, 2):
                    if axis == 0:
                        t = load(c, off, 0)
                    elif axis == 1:
                        t = load(c, 0, off)
                    else:
                        t = zs(center, off)
                    if abs(off) == 1:
                        near = t if near is None else near + t
                    else:
                        far = t if far is None else far + t
                return near, far

            def mixed(p_c, a, b):
                if 2 in (a, b):
                    n = a + b - 2
                    d = [0, 0]
                    d[n] = 1
                    step = load(p_c, d[0], d[1])
                    d[n] = -1
                    diff = step - load(p_c, d[0], d[1])
                    return zs(diff, 1) - zs(diff, -1)
                acc = None
                for sa in (1, -1):
                    for sb in (1, -1):
                        d = [0, 0, 0]
                        d[a] = sa
                        d[b] = sb
                        t = zs(load(p_c, d[0], d[1]), d[2])
                        if acc is None:
                            acc = t
                        elif sa * sb > 0:
                            acc = acc + t
                        else:
                            acc = acc - t
                return acc

            for c in range(3):
                others = [e for e in range(3) if e != c]
                near_c, far_c = sums(c, c)
                near_a, far_a = sums(c, others[0])
                near_b, far_b = sums(c, others[1])
                near = stiff * near_c + shear * (near_a + near_b)
                far = stiff * far_c + shear * (far_a + far_b)
                second = 16.0 * near - far + centre_weight * centers[c]
                cross = mixed(others[0], c, others[0]) + mixed(others[1], c, others[1])
                upd = second + coup * cross
                prev = prev_ref[c, p, pl.ds(8 * g, 8), :]
                src = src_ref[c, p, pl.ds(8 * g, 8), :]
                out_ref[c, p, pl.ds(8 * g, 8), :] = (2.0 * centers[c] - prev + upd) + src
        return carry

    lax.fori_loop(0, bx, plane, 0)


def elastic_step(u, xlo, xhi, ylo, yhi, prev, moduli, sources, bx=8):
    _, nx, ny, depth = u.shape
    kernel = functools.partial(step_kernel, bx=bx)
    block = lambda i: (0, i, 0, 0)
    whole = lambda i: (0, 0, 0, 0)
    return pl.pallas_call(
        kernel,
        grid=(nx // bx,),
        in_specs=[
            pl.BlockSpec(u.shape, whole),
            pl.BlockSpec(xlo.shape, whole),
            pl.BlockSpec(xhi.shape, whole),
            pl.BlockSpec(ylo.shape, whole),
            pl.BlockSpec(yhi.shape, whole),
            pl.BlockSpec((3, bx, ny, depth), block),
            pl.BlockSpec((2, bx, ny, depth), block),
            pl.BlockSpec((3, bx, ny, depth), block),
        ],
        out_specs=pl.BlockSpec((3, bx, ny, depth), block),
        out_shape=jax.ShapeDtypeStruct((3, nx, ny, depth), jnp.float32),
        scratch_shapes=[pltpu.VMEM((3, nx + 4, ny + 2 * YPAD, depth), jnp.float32)],
        compiler_params=pltpu.CompilerParams(dimension_semantics=("arbitrary",)),
    )(u, xlo, xhi, ylo, yhi, prev, moduli, sources)


def x_halos(block, width):
    size_x = lax.axis_size("gx")
    nx = block.shape[1]
    forward_x = [(i, i + 1) for i in range(size_x - 1)]
    backward_x = [(t, s) for s, t in forward_x]
    xlo = lax.ppermute(block[:, nx - width:], "gx", forward_x)
    xhi = lax.ppermute(block[:, :width], "gx", backward_x)
    return xlo, xhi


def y_halos(block, xlo, xhi, width):
    size_y = lax.axis_size("gy")
    ny = block.shape[2]
    forward_y = [(i, i + 1) for i in range(size_y - 1)]
    backward_y = [(t, s) for s, t in forward_y]
    rows = lambda sl: jnp.concatenate([xlo[:, :, sl], block[:, :, sl], xhi[:, :, sl]], axis=1)
    ylo = lax.ppermute(rows(slice(ny - width, ny)), "gy", forward_y)
    yhi = lax.ppermute(rows(slice(0, width)), "gy", backward_y)
    return ylo, yhi


def halos(block, width):
    xlo, xhi = x_halos(block, width)
    ylo, yhi = y_halos(block, xlo, xhi, width)
    return xlo, xhi, ylo, yhi


def level_table(values, layer_of_level):
    one_hot = (
        layer_of_level[:, None] == jnp.arange(values.shape[0], dtype=jnp.int32)[None, :]
    ).astype(jnp.float32)
    return jnp.sum(one_hot * values[None, :], axis=1)


def wave_kernel(angular, slowness, rigidity, damping, count_k):
    wavenum = (jnp.arange(count_k, dtype=jnp.float32) + 0.5) * (4.0 / count_k)
    spread = angular[None, :, None] * slowness[:, None, None]
    vertical = jnp.sqrt(wavenum[None, None, :] * wavenum[None, None, :] + spread * spread)
    impedance = rigidity[:, None, None] * vertical
    beneath = jnp.concatenate([impedance[1:], impedance[-1:]], axis=0)
    reflect = (impedance - beneath) / (impedance + beneath)
    fading = jnp.exp(-2.0 * step_depth * vertical * damping[:, None, None])
    two_way = 2.0 * step_depth * vertical
    trip_re = fading * jnp.cos(two_way)
    trip_im = -fading * jnp.sin(two_way)

    def upward(state_in, layer_data):
        refl_re, refl_im = state_in
        coefficient, along_re, along_im = layer_data
        upper_re = coefficient + refl_re
        lower_re = 1.0 + coefficient * refl_re
        lower_im = coefficient * refl_im
        magnitude = lower_re * lower_re + lower_im * lower_im
        ratio_re = (upper_re * lower_re + refl_im * lower_im) / magnitude
        ratio_im = (refl_im * lower_re - upper_re * lower_im) / magnitude
        fresh_re = along_re * ratio_re - along_im * ratio_im
        fresh_im = along_re * ratio_im + along_im * ratio_re
        return ((fresh_re, fresh_im), (fresh_re, fresh_im))

    bottom = jnp.zeros(vertical.shape[1:], jnp.float32)
    _, (refl_re, refl_im) = lax.scan(
        upward, (bottom, bottom), (reflect, trip_re, trip_im), reverse=True
    )
    travel = step_depth * vertical
    phases = jnp.cumsum(travel, axis=0) - travel
    absorbed = travel * damping[:, None, None]
    losses = jnp.cumsum(absorbed, axis=0) - absorbed
    down_size = jnp.exp(-losses)
    down_re = down_size * jnp.cos(phases)
    down_im = -down_size * jnp.sin(phases)
    weight = 1.0 / math.sqrt(count_k)
    kernel_re = weight * (down_re * (1.0 + refl_re) - down_im * refl_im)
    kernel_im = weight * (down_re * refl_im + down_im * (1.0 + refl_re))
    return jnp.transpose(jnp.stack([kernel_re, kernel_im]), (0, 2, 1, 3))


def offset_basis(count_k, count_r):
    modulus = count_k * count_r // 2
    low_count = 64
    odd_index = 2 * jnp.arange(count_k, dtype=jnp.int32) + 1
    high = jnp.arange(count_r // low_count, dtype=jnp.int32) * low_count
    low = jnp.arange(low_count, dtype=jnp.int32)
    scale = 2.0 * math.pi / modulus
    high_angle = (odd_index[:, None] * high[None, :] % modulus).astype(jnp.float32) * scale
    low_angle = (odd_index[:, None] * low[None, :] % modulus).astype(jnp.float32) * scale
    cos_h, sin_h = jnp.cos(high_angle), jnp.sin(high_angle)
    cos_l, sin_l = jnp.cos(low_angle), jnp.sin(low_angle)
    basis = cos_h[:, :, None] * cos_l[:, None, :] - sin_h[:, :, None] * sin_l[:, None, :]
    basis = basis.reshape(count_k, count_r).astype(jnp.bfloat16)
    return lax.optimization_barrier(basis)


def time_basis(freq_ids, count_f, count_steps, first_time):
    period = 2 * count_f
    times = first_time + jnp.arange(count_steps, dtype=jnp.int32)
    turns = (freq_ids[None, :] + 1) * times[:, None] % period
    angles = turns.astype(jnp.float32) * (2.0 * math.pi / period)
    weight = 1.0 / math.sqrt(count_f)
    return jnp.stack([weight * jnp.cos(angles), -weight * jnp.sin(angles)], axis=1)


def shifted(grid_block, step_x, step_y, step_z):
    width_x = grid_block.shape[0] - 4
    width_y = grid_block.shape[1] - 4
    width_z = grid_block.shape[2] - 4
    return grid_block[
        2 + step_x : 2 + step_x + width_x,
        2 + step_y : 2 + step_y + width_y,
        2 + step_z : 2 + step_z + width_z,
    ]


def curvature(grid_block, first_axis):
    summed = None
    for offset, factor in [(-2, -1.0), (-1, 16.0), (0, -30.0), (1, 16.0), (2, -1.0)]:
        moves = tuple((offset if index == first_axis else 0 for index in range(3)))
        contrib = factor * shifted(grid_block, moves[0], moves[1], moves[2])
        summed = contrib if summed is None else summed + contrib
    return summed / 12.0


def mixed(grid_block, first_axis, second_axis):
    summed = None
    for sign_a, sign_b, factor in [(1, 1, 1.0), (1, -1, -1.0), (-1, 1, -1.0), (-1, -1, 1.0)]:
        moves = tuple(
            (
                sign_a if index == first_axis else sign_b if index == second_axis else 0
                for index in range(3)
            )
        )
        contrib = factor * shifted(grid_block, moves[0], moves[1], moves[2])
        summed = contrib if summed is None else summed + contrib
    return summed / 4.0


def elastic(padded, moduli):
    first_lame = moduli[0]
    shear_mod = moduli[1]
    stiffness = first_lame + 2.0 * shear_mod
    coupling = first_lame + shear_mod
    result = []
    for component in range(3):
        update = stiffness * curvature(padded[component], component)
        for partner in range(3):
            if partner != component:
                update = update + shear_mod * curvature(padded[component], partner)
                update = update + coupling * mixed(padded[partner], component, partner)
        result.append(update)
    return jnp.stack(result)


def shards(
    layer_slowness,
    layer_rigidity,
    layer_damping,
    layer_of_level,
    slot_offset,
    slot_level,
    slot_target,
    live_count,
    moduli,
    field_old,
    field_now,
):
    size_gx = lax.axis_size("gx")
    size_gy = lax.axis_size("gy")
    groups = size_gx * size_gy
    per_device = F // groups
    device = lax.axis_index("gx") * size_gy + lax.axis_index("gy")
    freq_ids = device * per_device + jnp.arange(per_device, dtype=jnp.int32)
    angular = (freq_ids + 1).astype(jnp.float32) * (4.0 / F)
    slowness = level_table(layer_slowness, layer_of_level)
    rigidity = level_table(layer_rigidity, layer_of_level)
    damping = level_table(layer_damping, layer_of_level)
    kernel = wave_kernel(angular, slowness, rigidity, damping, NK).astype(jnp.bfloat16)
    later_now, kernel = lax.optimization_barrier((field_now, kernel))
    first_x = x_halos(later_now, 2)
    cosines = offset_basis(NK, NR)
    spectrum_table = jnp.dot(
        kernel.reshape(2 * per_device * ND, NK), cosines, preferred_element_type=jnp.float32
    )
    table_rounded = spectrum_table.astype(jnp.bfloat16)
    first_x, table_rounded = lax.optimization_barrier((first_x, table_rounded))
    first_y = y_halos(field_now, first_x[0], first_x[1], 2)
    all_slots = slot_offset.shape[0]
    width = math.gcd(all_slots, 4096)
    count_blocks = all_slots // width
    offset_blocks = slot_offset.reshape(count_blocks, width)
    level_blocks = slot_level.reshape(count_blocks, width)

    def select_block(pair):
        offsets, levels = pair
        offset_hot = (jnp.arange(NR, dtype=jnp.int32)[:, None] == offsets[None, :]).astype(
            jnp.bfloat16
        )
        rows = jnp.dot(table_rounded, offset_hot, preferred_element_type=jnp.float32).reshape(
            2, per_device, ND, width
        )
        level_hot = (jnp.arange(ND, dtype=jnp.int32)[:, None] == levels[None, :]).astype(
            jnp.float32
        )
        return jnp.sum(rows * level_hot[None, None, :, :], axis=2)

    selected = lax.map(select_block, (offset_blocks, level_blocks))
    spectra = (
        jnp.transpose(selected, (1, 2, 0, 3)).reshape(2, per_device, all_slots).astype(jnp.bfloat16)
    )
    slots_dev = slot_target.shape[0]
    occupied = (jnp.arange(slots_dev, dtype=jnp.int32) < live_count[0]).astype(jnp.float32)
    first_y, spectra = lax.optimization_barrier((first_y, spectra))
    parcel = spectra.reshape(2, per_device, groups, slots_dev)
    arrived = lax.all_to_all(parcel, ("gx", "gy"), split_axis=2, concat_axis=1, tiled=True)
    freq_order = jnp.arange(F, dtype=jnp.int32)
    waveforms = time_basis(freq_order, F, STEPS, TSTART).reshape(STEPS, 2 * F)
    traces = jnp.dot(
        waveforms,
        arrived.reshape(2 * F, slots_dev).astype(jnp.float32),
        precision=lax.Precision.HIGHEST,
    )
    block_x = field_now.shape[1]
    block_y = field_now.shape[2]
    depth = field_now.shape[3]
    columns = slot_target // depth
    layer_z = slot_target % depth
    weighted = traces * occupied[None, :]
    column_hot = (
        jnp.arange(3 * block_x * block_y, dtype=jnp.int32)[:, None] == columns[None, :]
    ).astype(jnp.float32)
    depth_hot = (layer_z[:, None] == jnp.arange(depth, dtype=jnp.int32)[None, :]).astype(
        jnp.float32
    )
    previous, current = (field_old, field_now)
    for instant in range(STEPS):
        spread = weighted[instant][:, None] * depth_hot
        source = jnp.dot(column_hot, spread, precision=lax.Precision.HIGHEST)
        source = source.reshape(3, block_x, block_y, depth)
        if instant == 0:
            xlo, xhi = first_x
            ylo, yhi = first_y
        else:
            xlo, xhi, ylo, yhi = halos(current, 2)
        advanced = elastic_step(current, xlo, xhi, ylo, yhi, previous, moduli, source)
        previous, current = (current, advanced)
    return (current, previous)


def solution(mesh):
    in_specs = (
        P(),
        P(),
        P(),
        P(),
        P(),
        P(),
        P(("gx", "gy")),
        P(("gx", "gy")),
        P(None, "gx", "gy", None),
        P(None, "gx", "gy", None),
        P(None, "gx", "gy", None),
    )
    out_specs = (P(None, "gx", "gy", None), P(None, "gx", "gy", None))
    return jax.shard_map(shards, mesh=mesh, in_specs=in_specs, out_specs=out_specs, check_vma=False)
```
